32 devices in a mesh: segment: 4 (over y, core), seq: 8 (over z, x).
Axes of the slice: x: 2, y: 2, z: 4, core: 2. Of those that a mesh axis runs over, the one named last changes fastest.
Arguments:
- patches: float32 [2, 1024, 128], P(None, 'seq'), may hold values from -6 to 6
- tile_list: int32 [8, 4], replicated, may hold values from 0 to 7, as said below
- input_weight: bfloat16 [4, 128, 1024], P('segment'), may hold values from -0.5 to 0.5
- attention_weight: bfloat16 [4, 1024, 3072], P('segment'), may hold values from -1 to 1
- mixing_weight: bfloat16 [4, 1024, 1024], P('segment'), may hold values from -0.1875 to 0.1875
- output_weight: bfloat16 [4, 1024, 256], P('segment'), may hold values from -0.09375 to 0.09375
- norm_gain: float32 [4, 1024], P('segment'), may hold values from 0.25 to 1.75
- final_gain: float32 [4, 1024], P('segment'), may hold values from 0.25 to 1.75
Outputs:
- flow_out: float32 [4, 2, 1024, 128], P('segment', None, 'seq')
The draws below stay inside these ranges and needn't reach their ends.
Inputs may be any that keep to these rules, and one draw needn't show every extreme that they name: `tile_list`: row t lists 4 key tiles; its first entry is t, every entry lies between max(t - 2, 0) and t, entries may repeat, and the last row has an entry exactly 2 tiles back.
All inputs are finite; a program needn't handle non-finite values.
Results may differ from the reference program's by a relative error of at most 0.0085.
Values may be sent and summed in bfloat16 or wider, within the bound.
No kernel may reach another device: no remote copies, remote signals or barrier semaphores. Data moves between devices by JAX's collectives and lax.ppermute only.
A program may use at most 64 MiB of HBM per device.

```python
import jax
import jax.numpy as jnp
from jax import lax

D = 1024
HEAD_DIM = 128
PATCH = 128
TILE = 128
LISTED = 4
ROWS_DEV = 128
MICRO = 2
HD = 1024
SEGMENTS = 4
LENGTH = 1024
TILES = 8
TILES_DEV = 1
N_SEGMENT = 4


def draw_tile_list(key, part):
    tiles = jnp.arange(TILES, dtype=jnp.int32)[:, None]
    offsets = jax.random.randint(key, (TILES, LISTED - 1), 0, 2 * TILES_DEV + 1, dtype=jnp.int32)
    offsets = offsets.at[TILES - 1, LISTED - 2].set(2 * TILES_DEV)
    entries = jnp.maximum(tiles - offsets, 0)
    return jnp.concatenate([tiles, entries], axis=1).astype(jnp.int32)


def draw_attention_weight(key, part):
    first = jax.random.fold_in(key, 0)
    bound = 6.0 * D ** (-0.5)
    base = jnp.clip(jax.random.normal(first, (SEGMENTS, D, 3 * HD), jnp.float32) * D ** (-0.5), -bound, bound)
    return jnp.clip(base, -1.0, 1.0).astype(jnp.bfloat16)


def level_of(key, extent, cuts, smallest, largest):
    level = 1.0
    for position, shards_of in cuts:
        draws = jax.random.uniform(jax.random.fold_in(jax.random.fold_in(key, 6), position), (shards_of,), jnp.float32, smallest / len(cuts), largest / len(cuts))
        level = level * jnp.repeat(jnp.exp(draws), extent[position] // shards_of).reshape((-1,) + (1,) * (len(extent) - 1 - position))
    return level


def noise(stream_key, shape, spread, reach, pieces=(), kind=jnp.bfloat16):
    result = jax.random.normal(stream_key, shape, jnp.float32) * spread
    if len(pieces) > 0:
        result = level_of(stream_key, shape, pieces, -0.22, 0.18) * result
    return jnp.clip(result, min=-reach, max=reach).astype(kind)


def setup_inputs(seed: int = 0) -> dict:
    seeds = jax.random.split(jax.random.key(seed), 9)
    return {
        "patches": noise(seeds[0], (MICRO, LENGTH, PATCH), 1.0, 6.0, ((1, 8),), jnp.float32),
        "tile_list": draw_tile_list(jax.random.fold_in(seeds[8], 71), 0),
        "input_weight": noise(seeds[2], (SEGMENTS, PATCH, D), PATCH ** -0.5, 0.5, ((0, 4),)),
        "attention_weight": draw_attention_weight(jax.random.fold_in(seeds[8], 71), 0),
        "mixing_weight": noise(seeds[4], (SEGMENTS, HD, D), HD ** -0.5, 0.1875, ((0, 4),)),
        "output_weight": noise(seeds[5], (SEGMENTS, D, 2 * PATCH), (4 * D) ** -0.5, 0.09375, ((0, 4),)),
        "norm_gain": jnp.clip(1.0 + 0.15 * jax.random.normal(seeds[6], (SEGMENTS, D), jnp.float32), 0.25, 1.75),
        "final_gain": jnp.clip(1.0 + 0.15 * jax.random.normal(seeds[7], (SEGMENTS, D), jnp.float32), 0.25, 1.75),
    }


def rms_scaled(values, gain):
    return values * lax.rsqrt(lax.optimization_barrier(jnp.mean(values * values, axis=-1, keepdims=True)) + 1e-06) * gain

def flow_block(flow_in, named, input_weight, attention_weight, mixing_weight, output_weight, norm_gain, final_gain):
    length = flow_in.shape[0]
    width_in = flow_in.shape[1]
    heads_all = mixing_weight.shape[0]
    head_count = heads_all // HEAD_DIM
    span = 3 * ROWS_DEV
    shifted = jnp.concatenate([jnp.zeros((1, width_in), flow_in.dtype), flow_in[:-1]], 0).astype(jnp.bfloat16)
    hidden = jnp.dot(shifted, input_weight, preferred_element_type=jnp.float32)
    normed = rms_scaled(hidden, norm_gain).astype(jnp.bfloat16)
    projected = jnp.dot(normed, attention_weight, preferred_element_type=jnp.float32).astype(jnp.bfloat16)
    queries = projected[:, :heads_all]
    keys = projected[:, heads_all:2 * heads_all]
    values = projected[:, 2 * heads_all:]

    def one_tile(tile):
        query_start = (tile * TILE).astype(jnp.int32)
        key_start = jnp.clip((tile - 2 * TILES_DEV) * TILE, 0, length - span).astype(jnp.int32)
        query_rows = lax.dynamic_slice_in_dim(queries, query_start, TILE, 0).astype(jnp.float32)
        key_rows = lax.dynamic_slice_in_dim(keys, key_start, span, 0).astype(jnp.float32)
        value_rows = lax.dynamic_slice_in_dim(values, key_start, span, 0).astype(jnp.float32)
        query_pos = query_start + jnp.arange(TILE, dtype=jnp.int32)
        key_pos = key_start + jnp.arange(span, dtype=jnp.int32)
        listed = named[tile][key_pos // TILE]
        allowed = listed[None, :] & (key_pos[None, :] <= query_pos[:, None])
        scores = jnp.einsum('qhd,khd->hqk', query_rows.reshape(TILE, head_count, HEAD_DIM), key_rows.reshape(span, head_count, HEAD_DIM)) * HEAD_DIM ** (-0.5)
        scores = jnp.where(allowed[None], scores, -jnp.inf)
        top = lax.optimization_barrier(jnp.max(scores, axis=-1, keepdims=True))
        expo = jnp.exp(scores - top)
        total = lax.optimization_barrier(jnp.sum(expo, axis=-1, keepdims=True))
        weights = expo.astype(jnp.bfloat16).astype(jnp.float32)
        mixed = jnp.einsum('hqk,khd->hqd', weights, value_rows.reshape(span, head_count, HEAD_DIM)) / total
        return jnp.transpose(mixed, (1, 0, 2)).reshape(TILE, heads_all).astype(jnp.bfloat16)
    mixed = lax.map(one_tile, jnp.arange(length // TILE, dtype=jnp.int32)).reshape(length, heads_all)
    residual = hidden + jnp.dot(mixed, mixing_weight, preferred_element_type=jnp.float32)
    final_normed = rms_scaled(residual, final_gain).astype(jnp.bfloat16)
    raw = jnp.dot(final_normed, output_weight, preferred_element_type=jnp.float32)
    shift_mean = raw[:, :width_in]
    log_scale = 0.5 * jnp.tanh(raw[:, width_in:])
    return (flow_in - shift_mean) * jnp.exp(-log_scale)

def reference(patches, tile_list, input_weight, attention_weight, mixing_weight, output_weight, norm_gain, final_gain):
    tiles_all = tile_list.shape[0]
    named = jnp.any(tile_list[:, :, None] == jnp.arange(tiles_all, dtype=jnp.int32)[None, None, :], axis=1)
    outputs = []
    for sequence in range(MICRO):
        flow_in = patches[sequence]
        per_block = []
        for block in range(N_SEGMENT):
            flow_out = flow_block(flow_in, named, input_weight[block], attention_weight[block], mixing_weight[block], output_weight[block], norm_gain[block], final_gain[block])
            per_block.append(flow_out)
            flow_in = flow_out[::-1]
        outputs.append(jnp.stack(per_block))
    return jnp.stack(outputs, 1)
```

```python
import jax
import jax.numpy as jnp
from jax import lax
from jax.sharding import PartitionSpec as P

HEAD_DIM = 128
TILE = 128
BACK = 2


def rms_scaled(values, gain):
    return values * lax.rsqrt(jnp.mean(values * values, axis=-1, keepdims=True) + 1e-06) * gain


def body(
    patches,
    tile_list,
    input_weight,
    attention_weight,
    mixing_weight,
    output_weight,
    norm_gain,
    final_gain,
):
    micro, rows, width_in = patches.shape
    assert rows == TILE
    heads_all = mixing_weight.shape[1]
    head_count = heads_all // HEAD_DIM
    segment = lax.axis_index("segment")
    place = lax.axis_index("seq")
    n_seq = lax.axis_size("seq")
    n_seg = lax.axis_size("segment")
    tiles_all = tile_list.shape[0]
    span = (BACK + 1) * rows

    window_tiles = place - BACK + jnp.arange(BACK + 1, dtype=jnp.int32)
    my_list = lax.dynamic_index_in_dim(tile_list, place, 0, keepdims=False)
    listed = jnp.any(my_list[:, None] == window_tiles[None, :], axis=0) & (window_tiles >= 0)
    listed = jnp.repeat(listed, rows)
    query_pos = jnp.arange(rows, dtype=jnp.int32) + BACK * rows
    key_pos = jnp.arange(span, dtype=jnp.int32)
    allowed = listed[None, :] & (key_pos[None, :] <= query_pos[:, None])

    embed = input_weight[0]
    w_query = attention_weight[0][:, :heads_all]
    w_keyval = attention_weight[0][:, heads_all:]
    mixing = mixing_weight[0]
    readout = output_weight[0]
    gain_first = norm_gain[0]
    gain_second = final_gain[0]

    def run_block(own, back1, back2, row3):
        window = jnp.concatenate([row3, back2, back1, own], axis=1)
        shifted = window[:, :-1].astype(jnp.bfloat16)
        hidden = jnp.einsum("mrc,cd->mrd", shifted, embed, preferred_element_type=jnp.float32)
        normed = rms_scaled(hidden, gain_first).astype(jnp.bfloat16)
        queries = jnp.einsum(
            "mrc,cd->mrd", normed[:, BACK * rows :], w_query, preferred_element_type=jnp.float32
        ).astype(jnp.bfloat16)
        keyval = jnp.einsum(
            "mrc,cd->mrd", normed, w_keyval, preferred_element_type=jnp.float32
        ).astype(jnp.bfloat16)
        queries = queries.reshape(micro, rows, head_count, HEAD_DIM)
        keys = keyval[:, :, :heads_all].reshape(micro, span, head_count, HEAD_DIM)
        values = keyval[:, :, heads_all:].reshape(micro, span, head_count, HEAD_DIM)
        scores = jnp.einsum(
            "mqhd,mkhd->mhqk", queries, keys, preferred_element_type=jnp.float32
        ) * HEAD_DIM ** (-0.5)
        scores = jnp.where(allowed[None, None], scores, -jnp.inf)
        top = jnp.max(scores, axis=-1, keepdims=True)
        expo = jnp.exp(scores - top)
        total = jnp.sum(expo, axis=-1, keepdims=True)
        mixed = (
            jnp.einsum(
                "mhqk,mkhd->mhqd",
                expo.astype(jnp.bfloat16),
                values,
                preferred_element_type=jnp.float32,
            )
            / total
        )
        mixed = jnp.transpose(mixed, (0, 2, 1, 3)).reshape(micro, rows, heads_all)
        mixed = mixed.astype(jnp.bfloat16)
        residual = hidden[:, BACK * rows :] + jnp.einsum(
            "mrc,cd->mrd", mixed, mixing, preferred_element_type=jnp.float32
        )
        final_normed = rms_scaled(residual, gain_second).astype(jnp.bfloat16)
        raw = jnp.einsum("mrc,cd->mrd", final_normed, readout, preferred_element_type=jnp.float32)
        shift_mean = raw[..., :width_in]
        log_scale = 0.5 * jnp.tanh(raw[..., width_in:])
        return (own - shift_mean) * jnp.exp(-log_scale)

    axes = ("segment", "seq")

    def first_inputs():
        def behind(block, distance):
            pairs = [(q, q + distance) for q in range(n_seq) if q + distance < n_seq]
            pairs = [(s, t) for s, t in pairs]
            return lax.ppermute(
                block, axes, [(0 * n_seq + s, 0 * n_seq + t) for s, t in pairs]
            )

        back1 = behind(patches, 1)
        back2 = behind(patches, 2)
        row3 = behind(patches[:, rows - 1 :], BACK + 1)
        return patches, back1, back2, row3

    def next_inputs(result, turn):
        mirrored = result[:, ::-1]
        src = turn * n_seq
        dst = (turn + 1) * n_seq

        def send(block, offset):
            pairs = []
            for q in range(n_seq):
                target = n_seq - 1 - q + offset
                if 0 <= target < n_seq:
                    pairs.append((src + q, dst + target))
            return lax.ppermute(block, axes, pairs)

        own = send(mirrored, 0)
        back1 = send(mirrored, 1)
        back2 = send(mirrored, 2)
        row3 = send(mirrored[:, rows - 1 :], BACK + 1)
        return own, back1, back2, row3

    inputs = first_inputs()
    out = jnp.zeros((micro, rows, width_in), jnp.float32)
    for turn in range(n_seg):
        result = run_block(*inputs)
        out = jnp.where(segment == turn, result, out)
        if turn + 1 < n_seg:
            inputs = next_inputs(result, turn)
    return out[None]


def solution(mesh):
    in_specs = (
        P(None, "seq", None),
        P(),
        P("segment", None, None),
        P("segment", None, None),
        P("segment", None, None),
        P("segment", None, None),
        P("segment", None),
        P("segment", None),
    )
    out_specs = P("segment", None, "seq", None)
    return jax.shard_map(body, mesh=mesh, in_specs=in_specs, out_specs=out_specs, check_vma=False)
```

```python
import jax
import jax.numpy as jnp
from jax import lax
from jax.experimental import pallas as pl
from jax.experimental.pallas import tpu as pltpu
from jax.sharding import PartitionSpec as P

HEAD_DIM = 128
TILE = 128
BACK = 2

CHUNK = 256


def make_block_call(micro, rows, width_in, heads_all):
    span = (BACK + 1) * rows
    own_at = BACK * rows
    n_rows = micro * span
    scale = HEAD_DIM ** (-0.5)
    heads = heads_all // HEAD_DIM

    def kernel(shifted_ref, own_ref, mask_ref, ga_ref, gb_ref,
               embed_hbm, attn_hbm, mix_hbm, read_hbm,
               out_ref,
               embed_v, attn_v, mix_v, read_v, sems,
               hidden_s, normed_s, q_s, kv_s, mixed_s, res_s):
        copies = [
            pltpu.make_async_copy(embed_hbm, embed_v, sems.at[0]),
            pltpu.make_async_copy(attn_hbm, attn_v, sems.at[1]),
            pltpu.make_async_copy(mix_hbm, mix_v, sems.at[2]),
            pltpu.make_async_copy(read_hbm, read_v, sems.at[3]),
        ]
        for copy in copies:
            copy.start()
        copies[0].wait()
        hidden = jnp.dot(shifted_ref[...], embed_v[...], preferred_element_type=jnp.float32)
        hidden_s[...] = hidden
        square = jnp.mean(hidden * hidden, axis=-1, keepdims=True)
        normed_s[...] = (hidden * lax.rsqrt(square + 1e-06) * ga_ref[...]).astype(jnp.bfloat16)
        copies[1].wait()

        def kv_step(j, carry):
            cols = pl.ds(pl.multiple_of(j * CHUNK, CHUNK), CHUNK)
            wcols = pl.ds(pl.multiple_of(heads_all + j * CHUNK, CHUNK), CHUNK)
            kv_s[:, cols] = jnp.dot(
                normed_s[...], attn_v[:, wcols], preferred_element_type=jnp.float32
            ).astype(jnp.bfloat16)
            return carry

        lax.fori_loop(0, 2 * heads_all // CHUNK, kv_step, 0)

        def q_step(j, carry):
            cols = pl.ds(pl.multiple_of(j * CHUNK, CHUNK), CHUNK)
            for m in range(micro):
                q_s[m * rows:(m + 1) * rows, cols] = jnp.dot(
                    normed_s[m * span + own_at:(m + 1) * span, :], attn_v[:, cols],
                    preferred_element_type=jnp.float32,
                ).astype(jnp.bfloat16)
            return carry

        lax.fori_loop(0, heads_all // CHUNK, q_step, 0)

        for m in range(micro):
            def head_step(h, carry):
                qcols = pl.ds(pl.multiple_of(h * HEAD_DIM, HEAD_DIM), HEAD_DIM)
                vcols = pl.ds(pl.multiple_of(heads_all + h * HEAD_DIM, HEAD_DIM), HEAD_DIM)
                qh = q_s[m * rows:(m + 1) * rows, qcols]
                kh = kv_s[m * span:(m + 1) * span, qcols]
                vh = kv_s[m * span:(m + 1) * span, vcols]
                scores = lax.dot_general(
                    qh, kh, (((1,), (1,)), ((), ())), preferred_element_type=jnp.float32
                ) * scale
                scores = jnp.where(mask_ref[...] > 0.5, scores, -jnp.inf)
                top = jnp.max(scores, axis=-1, keepdims=True)
                expo = jnp.exp(scores - top)
                total = jnp.sum(expo, axis=-1, keepdims=True)
                mixed = jnp.dot(
                    expo.astype(jnp.bfloat16), vh, preferred_element_type=jnp.float32
                ) / total
                mixed_s[m * rows:(m + 1) * rows, qcols] = mixed.astype(jnp.bfloat16)
                return carry

            lax.fori_loop(0, heads, head_step, 0)

        copies[2].wait()
        for m in range(micro):
            res_s[m * rows:(m + 1) * rows, :] = hidden_s[m * span + own_at:(m + 1) * span, :] + jnp.dot(
                mixed_s[m * rows:(m + 1) * rows, :], mix_v[...], preferred_element_type=jnp.float32
            )
        residual = res_s[...]
        square = jnp.mean(residual * residual, axis=-1, keepdims=True)
        final_normed = (residual * lax.rsqrt(square + 1e-06) * gb_ref[...]).astype(jnp.bfloat16)
        copies[3].wait()
        raw = jnp.dot(final_normed, read_v[...], preferred_element_type=jnp.float32)
        shift_mean = raw[:, :width_in]
        log_scale = 0.5 * jnp.tanh(raw[:, width_in:])
        out_ref[...] = (own_ref[...] - shift_mean) * jnp.exp(-log_scale)

    width = heads_all
    flops = 2 * n_rows * (width_in * width + width * 2 * heads_all)
    flops += 2 * micro * rows * (width * heads_all + 2 * heads * span * HEAD_DIM + heads_all * width + width * 2 * width_in)
    weight_bytes = 2 * (width_in * width + width * 3 * heads_all + heads_all * width + width * 2 * width_in)
    vmem = pltpu.VMEM
    call = pl.pallas_call(
        kernel,
        out_shape=jax.ShapeDtypeStruct((micro * rows, width_in), jnp.float32),
        in_specs=[pl.BlockSpec(memory_space=vmem)] * 5 + [pl.BlockSpec(memory_space=pl.ANY)] * 4,
        out_specs=pl.BlockSpec(memory_space=vmem),
        scratch_shapes=[
            vmem((width_in, width), jnp.bfloat16),
            vmem((width, 3 * heads_all), jnp.bfloat16),
            vmem((heads_all, width), jnp.bfloat16),
            vmem((width, 2 * width_in), jnp.bfloat16),
            pltpu.SemaphoreType.DMA((4,)),
            vmem((n_rows, width), jnp.float32),
            vmem((n_rows, width), jnp.bfloat16),
            vmem((micro * rows, heads_all), jnp.bfloat16),
            vmem((n_rows, 2 * heads_all), jnp.bfloat16),
            vmem((micro * rows, heads_all), jnp.bfloat16),
            vmem((micro * rows, width), jnp.float32),
        ],
        compiler_params=pltpu.CompilerParams(vmem_limit_bytes=56 * 1024 * 1024),
        cost_estimate=pl.CostEstimate(
            flops=flops,
            bytes_accessed=weight_bytes + n_rows * width_in * 2 + 2 * micro * rows * width_in * 4,
            transcendentals=micro * heads * rows * span + micro * rows * 2 * width_in,
        ),
    )
    return call


def rms_scaled(values, gain):
    return values * lax.rsqrt(jnp.mean(values * values, axis=-1, keepdims=True) + 1e-06) * gain


def body(
    patches,
    tile_list,
    input_weight,
    attention_weight,
    mixing_weight,
    output_weight,
    norm_gain,
    final_gain,
):
    micro, rows, width_in = patches.shape
    assert rows == TILE
    heads_all = mixing_weight.shape[1]
    head_count = heads_all // HEAD_DIM
    segment = lax.axis_index("segment")
    place = lax.axis_index("seq")
    n_seq = lax.axis_size("seq")
    n_seg = lax.axis_size("segment")
    tiles_all = tile_list.shape[0]
    span = (BACK + 1) * rows

    window_tiles = place - BACK + jnp.arange(BACK + 1, dtype=jnp.int32)
    my_list = lax.dynamic_index_in_dim(tile_list, place, 0, keepdims=False)
    listed = jnp.any(my_list[:, None] == window_tiles[None, :], axis=0) & (window_tiles >= 0)
    listed = jnp.repeat(listed, rows)
    query_pos = jnp.arange(rows, dtype=jnp.int32) + BACK * rows
    key_pos = jnp.arange(span, dtype=jnp.int32)
    allowed = listed[None, :] & (key_pos[None, :] <= query_pos[:, None])

    block_call = make_block_call(micro, rows, width_in, heads_all)
    mask = allowed.astype(jnp.float32)
    embed_w = input_weight[0]
    attn_w = attention_weight[0]
    mix_w = mixing_weight[0]
    read_w = output_weight[0]
    gain_a = norm_gain[0].reshape(1, -1)
    gain_b = final_gain[0].reshape(1, -1)

    def run_block(own, back1, back2, row3):
        window = jnp.concatenate([row3, back2, back1, own], axis=1)
        shifted = window[:, :-1].astype(jnp.bfloat16).reshape(micro * span, width_in)
        result = block_call(
            shifted, own.reshape(micro * rows, width_in), mask, gain_a, gain_b,
            embed_w, attn_w, mix_w, read_w,
        )
        return result.reshape(micro, rows, width_in)

    axes = ("segment", "seq")

    def first_inputs():
        def behind(block, distance):
            pairs = [(q, q + distance) for q in range(n_seq) if q + distance < n_seq]
            pairs = [(s, t) for s, t in pairs]
            return lax.ppermute(
                block, axes, [(0 * n_seq + s, 0 * n_seq + t) for s, t in pairs]
            )

        back1 = behind(patches, 1)
        back2 = behind(patches, 2)
        row3 = behind(patches[:, rows - 1 :], BACK + 1)
        return patches, back1, back2, row3

    def next_inputs(result, turn):
        mirrored = result[:, ::-1]
        src = turn * n_seq
        dst = (turn + 1) * n_seq

        def send(block, offset):
            pairs = []
            for q in range(n_seq):
                target = n_seq - 1 - q + offset
                if 0 <= target < n_seq:
                    pairs.append((src + q, dst + target))
            return lax.ppermute(block, axes, pairs)

        own = send(mirrored, 0)
        back1 = send(mirrored, 1)
        back2 = send(mirrored, 2)
        row3 = send(mirrored[:, rows - 1 :], BACK + 1)
        return own, back1, back2, row3

    inputs = first_inputs()
    out = jnp.zeros((micro, rows, width_in), jnp.float32)
    for turn in range(n_seg):
        result = run_block(*inputs)
        out = jnp.where(segment == turn, result, out)
        if turn + 1 < n_seg:
            inputs = next_inputs(result, turn)
    return out[None]


def solution(mesh):
    in_specs = (
        P(None, "seq", None),
        P(),
        P("segment", None, None),
        P("segment", None, None),
        P("segment", None, None),
        P("segment", None, None),
        P("segment", None),
        P("segment", None),
    )
    out_specs = P("segment", None, "seq", None)
    return jax.shard_map(body, mesh=mesh, in_specs=in_specs, out_specs=out_specs, check_vma=False)
```

```python
import jax
import jax.numpy as jnp
from jax import lax
from jax.experimental import pallas as pl
from jax.experimental.pallas import tpu as pltpu
from jax.sharding import PartitionSpec as P

HEAD_DIM = 128
TILE = 128
BACK = 2

CHUNK = 512


def make_block_call(micro, rows, width_in, heads_all):
    span = (BACK + 1) * rows
    own_at = BACK * rows
    n_rows = micro * span
    scale = HEAD_DIM ** (-0.5)
    heads = heads_all // HEAD_DIM

    def kernel(shifted_ref, own_ref, mask_ref, ga_ref, gb_ref,
               embed_hbm, attn_hbm, mix_hbm, read_hbm,
               out_ref,
               embed_v, attn_v, mix_v, read_v, sems,
               hidden_s, normed_s, q_s, kv_s, mixed_s, res_s):
        n_kv = 2 * heads_all // CHUNK
        kv_copies = [
            pltpu.make_async_copy(
                attn_hbm.at[:, heads_all + j * CHUNK:heads_all + (j + 1) * CHUNK],
                attn_v.at[:, heads_all + j * CHUNK:heads_all + (j + 1) * CHUNK],
                sems.at[4 + j],
            )
            for j in range(n_kv)
        ]
        copies = [
            pltpu.make_async_copy(embed_hbm, embed_v, sems.at[0]),
            pltpu.make_async_copy(attn_hbm.at[:, :heads_all], attn_v.at[:, :heads_all], sems.at[1]),
            pltpu.make_async_copy(mix_hbm, mix_v, sems.at[2]),
            pltpu.make_async_copy(read_hbm, read_v, sems.at[3]),
        ]
        copies[0].start()
        for copy in kv_copies:
            copy.start()
        for copy in copies[1:]:
            copy.start()
        copies[0].wait()
        hidden = jnp.dot(shifted_ref[...], embed_v[...], preferred_element_type=jnp.float32)
        hidden_s[...] = hidden
        square = jnp.mean(hidden * hidden, axis=-1, keepdims=True)
        normed_s[...] = (hidden * lax.rsqrt(square + 1e-06) * ga_ref[...]).astype(jnp.bfloat16)
        for j in range(n_kv):
            kv_copies[j].wait()
            kv_s[:, j * CHUNK:(j + 1) * CHUNK] = jnp.dot(
                normed_s[...], attn_v[:, heads_all + j * CHUNK:heads_all + (j + 1) * CHUNK],
                preferred_element_type=jnp.float32,
            ).astype(jnp.bfloat16)
        copies[1].wait()

        def q_step(j, carry):
            cols = pl.ds(pl.multiple_of(j * CHUNK, CHUNK), CHUNK)
            for m in range(micro):
                q_s[m * rows:(m + 1) * rows, cols] = jnp.dot(
                    normed_s[m * span + own_at:(m + 1) * span, :], attn_v[:, cols],
                    preferred_element_type=jnp.float32,
                ).astype(jnp.bfloat16)
            return carry

        lax.fori_loop(0, heads_all // CHUNK, q_step, 0)

        for m in range(micro):
            q3 = jnp.stack([q_s[m * rows:(m + 1) * rows, h * HEAD_DIM:(h + 1) * HEAD_DIM] for h in range(heads)])
            k3 = jnp.stack([kv_s[m * span:(m + 1) * span, h * HEAD_DIM:(h + 1) * HEAD_DIM] for h in range(heads)])
            v3 = jnp.stack([
                kv_s[m * span:(m + 1) * span, heads_all + h * HEAD_DIM:heads_all + (h + 1) * HEAD_DIM]
                for h in range(heads)
            ])
            scores = jnp.einsum("hqd,hkd->hqk", q3, k3, preferred_element_type=jnp.float32) * scale
            scores = jnp.where(mask_ref[...][None] > 0.5, scores, -jnp.inf)
            top = jnp.max(scores, axis=-1, keepdims=True)
            expo = jnp.exp(scores - top)
            total = jnp.sum(expo, axis=-1, keepdims=True)
            mixed = jnp.einsum(
                "hqk,hkd->hqd", expo.astype(jnp.bfloat16), v3, preferred_element_type=jnp.float32
            ) / total
            for h in range(heads):
                mixed_s[m * rows:(m + 1) * rows, h * HEAD_DIM:(h + 1) * HEAD_DIM] = mixed[h].astype(jnp.bfloat16)

        copies[2].wait()
        for m in range(micro):
            res_s[m * rows:(m + 1) * rows, :] = hidden_s[m * span + own_at:(m + 1) * span, :] + jnp.dot(
                mixed_s[m * rows:(m + 1) * rows, :], mix_v[...], preferred_element_type=jnp.float32
            )
        residual = res_s[...]
        square = jnp.mean(residual * residual, axis=-1, keepdims=True)
        final_normed = (residual * lax.rsqrt(square + 1e-06) * gb_ref[...]).astype(jnp.bfloat16)
        copies[3].wait()
        raw = jnp.dot(final_normed, read_v[...], preferred_element_type=jnp.float32)
        shift_mean = raw[:, :width_in]
        log_scale = 0.5 * jnp.tanh(raw[:, width_in:])
        out_ref[...] = (own_ref[...] - shift_mean) * jnp.exp(-log_scale)

    width = heads_all
    flops = 2 * n_rows * (width_in * width + width * 2 * heads_all)
    flops += 2 * micro * rows * (width * heads_all + 2 * heads * span * HEAD_DIM + heads_all * width + width * 2 * width_in)
    weight_bytes = 2 * (width_in * width + width * 3 * heads_all + heads_all * width + width * 2 * width_in)
    vmem = pltpu.VMEM
    call = pl.pallas_call(
        kernel,
        out_shape=jax.ShapeDtypeStruct((micro * rows, width_in), jnp.float32),
        in_specs=[pl.BlockSpec(memory_space=vmem)] * 5 + [pl.BlockSpec(memory_space=pl.ANY)] * 4,
        out_specs=pl.BlockSpec(memory_space=vmem),
        scratch_shapes=[
            vmem((width_in, width), jnp.bfloat16),
            vmem((width, 3 * heads_all), jnp.bfloat16),
            vmem((heads_all, width), jnp.bfloat16),
            vmem((width, 2 * width_in), jnp.bfloat16),
            pltpu.SemaphoreType.DMA((4 + 2 * heads_all // CHUNK,)),
            vmem((n_rows, width), jnp.float32),
            vmem((n_rows, width), jnp.bfloat16),
            vmem((micro * rows, heads_all), jnp.bfloat16),
            vmem((n_rows, 2 * heads_all), jnp.bfloat16),
            vmem((micro * rows, heads_all), jnp.bfloat16),
            vmem((micro * rows, width), jnp.float32),
        ],
        compiler_params=pltpu.CompilerParams(vmem_limit_bytes=56 * 1024 * 1024),
        cost_estimate=pl.CostEstimate(
            flops=flops,
            bytes_accessed=weight_bytes + n_rows * width_in * 2 + 2 * micro * rows * width_in * 4,
            transcendentals=micro * heads * rows * span + micro * rows * 2 * width_in,
        ),
    )
    return call


def rms_scaled(values, gain):
    return values * lax.rsqrt(jnp.mean(values * values, axis=-1, keepdims=True) + 1e-06) * gain


def body(
    patches,
    tile_list,
    input_weight,
    attention_weight,
    mixing_weight,
    output_weight,
    norm_gain,
    final_gain,
):
    micro, rows, width_in = patches.shape
    assert rows == TILE
    heads_all = mixing_weight.shape[1]
    head_count = heads_all // HEAD_DIM
    segment = lax.axis_index("segment")
    place = lax.axis_index("seq")
    n_seq = lax.axis_size("seq")
    n_seg = lax.axis_size("segment")
    tiles_all = tile_list.shape[0]
    span = (BACK + 1) * rows

    window_tiles = place - BACK + jnp.arange(BACK + 1, dtype=jnp.int32)
    my_list = lax.dynamic_index_in_dim(tile_list, place, 0, keepdims=False)
    listed = jnp.any(my_list[:, None] == window_tiles[None, :], axis=0) & (window_tiles >= 0)
    listed = jnp.repeat(listed, rows)
    query_pos = jnp.arange(rows, dtype=jnp.int32) + BACK * rows
    key_pos = jnp.arange(span, dtype=jnp.int32)
    allowed = listed[None, :] & (key_pos[None, :] <= query_pos[:, None])

    block_call = make_block_call(micro, rows, width_in, heads_all)
    mask = allowed.astype(jnp.float32)
    embed_w = input_weight[0]
    attn_w = attention_weight[0]
    mix_w = mixing_weight[0]
    read_w = output_weight[0]
    gain_a = norm_gain[0].reshape(1, -1)
    gain_b = final_gain[0].reshape(1, -1)

    def run_block(own, back1, back2, row3):
        window = jnp.concatenate([row3, back2, back1, own], axis=1)
        shifted = window[:, :-1].astype(jnp.bfloat16).reshape(micro * span, width_in)
        result = block_call(
            shifted, own.reshape(micro * rows, width_in), mask, gain_a, gain_b,
            embed_w, attn_w, mix_w, read_w,
        )
        return result.reshape(micro, rows, width_in)

    axes = ("segment", "seq")

    def first_inputs():
        def behind(block, distance):
            pairs = [(q, q + distance) for q in range(n_seq) if q + distance < n_seq]
            pairs = [(s, t) for s, t in pairs]
            return lax.ppermute(
                block, axes, [(0 * n_seq + s, 0 * n_seq + t) for s, t in pairs]
            )

        back1 = behind(patches, 1)
        back2 = behind(patches, 2)
        row3 = behind(patches[:, rows - 1 :], BACK + 1)
        return patches, back1, back2, row3

    def next_inputs(result, turn):
        mirrored = result[:, ::-1]
        src = turn * n_seq
        dst = (turn + 1) * n_seq

        def send(block, offset):
            pairs = []
            for q in range(n_seq):
                target = n_seq - 1 - q + offset
                if 0 <= target < n_seq:
                    pairs.append((src + q, dst + target))
            return lax.ppermute(block, axes, pairs)

        own = send(mirrored, 0)
        back1 = send(mirrored, 1)
        back2 = send(mirrored, 2)
        row3 = send(mirrored[:, rows - 1 :], BACK + 1)
        return own, back1, back2, row3

    inputs = first_inputs()
    out = jnp.zeros((micro, rows, width_in), jnp.float32)
    for turn in range(n_seg):
        result = run_block(*inputs)
        out = jnp.where(segment == turn, result, out)
        if turn + 1 < n_seg:
            inputs = next_inputs(result, turn)
    return out[None]


def solution(mesh):
    in_specs = (
        P(None, "seq", None),
        P(),
        P("segment", None, None),
        P("segment", None, None),
        P("segment", None, None),
        P("segment", None, None),
        P("segment", None),
        P("segment", None),
    )
    out_specs = P("segment", None, "seq", None)
    return jax.shard_map(body, mesh=mesh, in_specs=in_specs, out_specs=out_specs, check_vma=False)
```

```python
import jax
import jax.numpy as jnp
from jax import lax
from jax.experimental import pallas as pl
from jax.experimental.pallas import tpu as pltpu
from jax.sharding import PartitionSpec as P

HEAD_DIM = 128
TILE = 128
BACK = 2

CHUNK = 512


def make_block_call(micro, rows, width_in, heads_all, mirrored, piece_dtype):
    span = (BACK + 1) * rows
    own_at = BACK * rows
    n_rows = micro * span
    n_in = (BACK + 2) * rows
    scale = HEAD_DIM ** (-0.5)
    heads = heads_all // HEAD_DIM

    def kernel(own_ref, back1_ref, back2_ref, edge_ref, mask_ref, ga_ref, gb_ref,
               embed_hbm, attn_hbm, mix_hbm, read_hbm,
               out_ref, outb_ref,
               embed_v, attn_v, mix_v, read_v, sems,
               pieces_s, shifted_s, hidden_s, normed_s, q_s, kv_s, mixed_s, res_s):
        n_kv = 2 * heads_all // CHUNK
        kv_copies = [
            pltpu.make_async_copy(
                attn_hbm.at[:, heads_all + j * CHUNK:heads_all + (j + 1) * CHUNK],
                attn_v.at[:, heads_all + j * CHUNK:heads_all + (j + 1) * CHUNK],
                sems.at[4 + j],
            )
            for j in range(n_kv)
        ]
        copies = [
            pltpu.make_async_copy(embed_hbm, embed_v, sems.at[0]),
            pltpu.make_async_copy(attn_hbm.at[:, :heads_all], attn_v.at[:, :heads_all], sems.at[1]),
            pltpu.make_async_copy(mix_hbm, mix_v, sems.at[2]),
            pltpu.make_async_copy(read_hbm, read_v, sems.at[3]),
        ]
        copies[0].start()
        for copy in kv_copies:
            copy.start()
        for copy in copies[1:]:
            copy.start()
        before = lax.broadcasted_iota(jnp.int32, (span, n_in), 0) + (rows - 1)
        column = lax.broadcasted_iota(jnp.int32, (span, n_in), 1)
        if mirrored:
            source = ((before >> 7) << 7) + (rows - 1) - (before & (rows - 1))
        else:
            source = before
        select = (column == source).astype(jnp.bfloat16)
        for m in range(micro):
            pieces_s[0:rows, :] = edge_ref[m].astype(jnp.bfloat16)
            pieces_s[rows:2 * rows, :] = back2_ref[m].astype(jnp.bfloat16)
            pieces_s[2 * rows:3 * rows, :] = back1_ref[m].astype(jnp.bfloat16)
            pieces_s[3 * rows:4 * rows, :] = own_ref[m].astype(jnp.bfloat16)
            shifted_s[m * span:(m + 1) * span, :] = jnp.dot(
                select, pieces_s[...], preferred_element_type=jnp.float32
            ).astype(jnp.bfloat16)
        copies[0].wait()
        hidden = jnp.dot(shifted_s[...], embed_v[...], preferred_element_type=jnp.float32)
        hidden_s[...] = hidden
        square = jnp.mean(hidden * hidden, axis=-1, keepdims=True)
        normed_s[...] = (hidden * lax.rsqrt(square + 1e-06) * ga_ref[...]).astype(jnp.bfloat16)
        for j in range(n_kv):
            kv_copies[j].wait()
            kv_s[:, j * CHUNK:(j + 1) * CHUNK] = jnp.dot(
                normed_s[...], attn_v[:, heads_all + j * CHUNK:heads_all + (j + 1) * CHUNK],
                preferred_element_type=jnp.float32,
            ).astype(jnp.bfloat16)
        copies[1].wait()

        def q_step(j, carry):
            cols = pl.ds(pl.multiple_of(j * CHUNK, CHUNK), CHUNK)
            for m in range(micro):
                q_s[m * rows:(m + 1) * rows, cols] = jnp.dot(
                    normed_s[m * span + own_at:(m + 1) * span, :], attn_v[:, cols],
                    preferred_element_type=jnp.float32,
                ).astype(jnp.bfloat16)
            return carry

        lax.fori_loop(0, heads_all // CHUNK, q_step, 0)

        for m in range(micro):
            q3 = jnp.stack([q_s[m * rows:(m + 1) * rows, h * HEAD_DIM:(h + 1) * HEAD_DIM] for h in range(heads)])
            k3 = jnp.stack([kv_s[m * span:(m + 1) * span, h * HEAD_DIM:(h + 1) * HEAD_DIM] for h in range(heads)])
            v3 = jnp.stack([
                kv_s[m * span:(m + 1) * span, heads_all + h * HEAD_DIM:heads_all + (h + 1) * HEAD_DIM]
                for h in range(heads)
            ])
            scores = jnp.einsum("hqd,hkd->hqk", q3, k3, preferred_element_type=jnp.float32) * scale
            scores = jnp.where(mask_ref[...][None] > 0.5, scores, -jnp.inf)
            top = jnp.max(scores, axis=-1, keepdims=True)
            expo = jnp.exp(scores - top)
            total = jnp.sum(expo, axis=-1, keepdims=True)
            mixed = jnp.einsum(
                "hqk,hkd->hqd", expo.astype(jnp.bfloat16), v3, preferred_element_type=jnp.float32
            ) / total
            for h in range(heads):
                mixed_s[m * rows:(m + 1) * rows, h * HEAD_DIM:(h + 1) * HEAD_DIM] = mixed[h].astype(jnp.bfloat16)

        copies[2].wait()
        for m in range(micro):
            res_s[m * rows:(m + 1) * rows, :] = hidden_s[m * span + own_at:(m + 1) * span, :] + jnp.dot(
                mixed_s[m * rows:(m + 1) * rows, :], mix_v[...], preferred_element_type=jnp.float32
            )
        residual = res_s[...]
        square = jnp.mean(residual * residual, axis=-1, keepdims=True)
        final_normed = (residual * lax.rsqrt(square + 1e-06) * gb_ref[...]).astype(jnp.bfloat16)
        copies[3].wait()
        raw = jnp.dot(final_normed, read_v[...], preferred_element_type=jnp.float32)
        shift_mean = raw[:, :width_in]
        log_scale = 0.5 * jnp.tanh(raw[:, width_in:])
        if mirrored:
            i = lax.broadcasted_iota(jnp.int32, (rows, rows), 0)
            c = lax.broadcasted_iota(jnp.int32, (rows, rows), 1)
            flip = (c == (rows - 1) - i).astype(jnp.bfloat16)
        for m in range(micro):
            own = own_ref[m]
            if mirrored:
                high = own.astype(jnp.bfloat16)
                rest = own - high.astype(jnp.float32)
                middle = rest.astype(jnp.bfloat16)
                low = (rest - middle.astype(jnp.float32)).astype(jnp.bfloat16)
                parts = [jnp.dot(flip, part, preferred_element_type=jnp.float32) for part in (high, middle, low)]
                own = (parts[0] + parts[1]) + parts[2]
            rows_m = slice(m * rows, (m + 1) * rows)
            result = (own - shift_mean[rows_m]) * jnp.exp(-log_scale[rows_m])
            out_ref[m] = result
            outb_ref[m] = result.astype(jnp.bfloat16)

    width = heads_all
    flops = 2 * n_rows * (width_in * width + width * 2 * heads_all)
    flops += 2 * micro * rows * (width * heads_all + 2 * heads * span * HEAD_DIM + heads_all * width + width * 2 * width_in)
    weight_bytes = 2 * (width_in * width + width * 3 * heads_all + heads_all * width + width * 2 * width_in)
    vmem = pltpu.VMEM
    call = pl.pallas_call(
        kernel,
        out_shape=(
            jax.ShapeDtypeStruct((micro, rows, width_in), jnp.float32),
            jax.ShapeDtypeStruct((micro, rows, width_in), jnp.bfloat16),
        ),
        in_specs=[pl.BlockSpec(memory_space=vmem)] * 7 + [pl.BlockSpec(memory_space=pl.ANY)] * 4,
        out_specs=(pl.BlockSpec(memory_space=vmem), pl.BlockSpec(memory_space=vmem)),
        scratch_shapes=[
            vmem((width_in, width), jnp.bfloat16),
            vmem((width, 3 * heads_all), jnp.bfloat16),
            vmem((heads_all, width), jnp.bfloat16),
            vmem((width, 2 * width_in), jnp.bfloat16),
            pltpu.SemaphoreType.DMA((4 + 2 * heads_all // CHUNK,)),
            vmem((n_in, width_in), jnp.bfloat16),
            vmem((n_rows, width_in), jnp.bfloat16),
            vmem((n_rows, width), jnp.float32),
            vmem((n_rows, width), jnp.bfloat16),
            vmem((micro * rows, heads_all), jnp.bfloat16),
            vmem((n_rows, 2 * heads_all), jnp.bfloat16),
            vmem((micro * rows, heads_all), jnp.bfloat16),
            vmem((micro * rows, width), jnp.float32),
        ],
        compiler_params=pltpu.CompilerParams(vmem_limit_bytes=56 * 1024 * 1024),
        cost_estimate=pl.CostEstimate(
            flops=flops,
            bytes_accessed=weight_bytes + n_rows * width_in * 2 + 2 * micro * rows * width_in * 4,
            transcendentals=micro * heads * rows * span + micro * rows * 2 * width_in,
        ),
    )
    return call


def rms_scaled(values, gain):
    return values * lax.rsqrt(jnp.mean(values * values, axis=-1, keepdims=True) + 1e-06) * gain


def body(
    patches,
    tile_list,
    input_weight,
    attention_weight,
    mixing_weight,
    output_weight,
    norm_gain,
    final_gain,
):
    micro, rows, width_in = patches.shape
    assert rows == TILE
    heads_all = mixing_weight.shape[1]
    head_count = heads_all // HEAD_DIM
    segment = lax.axis_index("segment")
    place = lax.axis_index("seq")
    n_seq = lax.axis_size("seq")
    n_seg = lax.axis_size("segment")
    tiles_all = tile_list.shape[0]
    span = (BACK + 1) * rows

    window_tiles = place - BACK + jnp.arange(BACK + 1, dtype=jnp.int32)
    my_list = lax.dynamic_index_in_dim(tile_list, place, 0, keepdims=False)
    listed = jnp.any(my_list[:, None] == window_tiles[None, :], axis=0) & (window_tiles >= 0)
    listed = jnp.repeat(listed, rows)
    query_pos = jnp.arange(rows, dtype=jnp.int32) + BACK * rows
    key_pos = jnp.arange(span, dtype=jnp.int32)
    allowed = listed[None, :] & (key_pos[None, :] <= query_pos[:, None])

    first_call = make_block_call(micro, rows, width_in, heads_all, False, jnp.float32)
    later_call = make_block_call(micro, rows, width_in, heads_all, True, jnp.bfloat16)
    mask = allowed.astype(jnp.float32)
    weights = (
        norm_gain[0].reshape(1, -1),
        final_gain[0].reshape(1, -1),
        input_weight[0],
        attention_weight[0],
        mixing_weight[0],
        output_weight[0],
    )

    axes = ("segment", "seq")

    def first_inputs():
        def behind(distance):
            pairs = [(q, q + distance) for q in range(n_seq) if q + distance < n_seq]
            return lax.ppermute(patches, axes, pairs)

        return patches, behind(1), behind(2), behind(BACK + 1)

    def next_inputs(result, result_low, turn):
        src = turn * n_seq
        dst = (turn + 1) * n_seq

        def send(block, offset):
            pairs = []
            for q in range(n_seq):
                target = n_seq - 1 - q + offset
                if 0 <= target < n_seq:
                    pairs.append((src + q, dst + target))
            return lax.ppermute(block, axes, pairs)

        return (
            send(result, 0),
            send(result_low, 1),
            send(result_low, 2),
            send(result_low, BACK + 1),
        )

    inputs = first_inputs()
    out = jnp.zeros((micro, rows, width_in), jnp.float32)
    for turn in range(n_seg):
        call = first_call if turn == 0 else later_call
        result, result_low = call(*inputs, mask, *weights)
        out = jnp.where(segment == turn, result, out)
        if turn + 1 < n_seg:
            inputs = next_inputs(result, result_low, turn)
    return out[None]


def solution(mesh):
    in_specs = (
        P(None, "seq", None),
        P(),
        P("segment", None, None),
        P("segment", None, None),
        P("segment", None, None),
        P("segment", None, None),
        P("segment", None),
        P("segment", None),
    )
    out_specs = P("segment", None, "seq", None)
    return jax.shard_map(body, mesh=mesh, in_specs=in_specs, out_specs=out_specs, check_vma=False)
```

```python
import jax
import jax.numpy as jnp
from jax import lax
from jax.experimental import pallas as pl
from jax.experimental.pallas import tpu as pltpu
from jax.sharding import PartitionSpec as P

HEAD_DIM = 128
TILE = 128
BACK = 2

CHUNK = 512


def make_block_call(micro, rows, width_in, heads_all, mirrored, piece_dtype):
    span = (BACK + 1) * rows
    own_at = BACK * rows
    n_rows = micro * span
    n_in = (BACK + 2) * rows
    scale = HEAD_DIM ** (-0.5)
    heads = heads_all // HEAD_DIM

    def kernel(keep_ref, mask_ref, ga_ref, gb_ref,
               own_hbm, back1_hbm, back2_hbm, edge_hbm, prev_hbm,
               embed_hbm, attn_hbm, mix_hbm, read_hbm,
               stored_hbm, low_hbm,
               embed_v, attn_v, mix_v, read_v, sems, io_sems,
               own_ref, back1_ref, back2_ref, edge_ref, prev_v, stored_v, low_v,
               pieces_s, shifted_s, hidden_s, normed_s, q_s, kv_s, mixed_s, res_s):
        inputs = [
            pltpu.make_async_copy(src, dst, io_sems.at[k])
            for k, (src, dst) in enumerate(
                [(own_hbm, own_ref), (back1_hbm, back1_ref), (back2_hbm, back2_ref), (edge_hbm, edge_ref)]
            )
        ]
        for copy in inputs:
            copy.start()
        prev_copy = pltpu.make_async_copy(prev_hbm, prev_v, io_sems.at[4])
        n_kv = 2 * heads_all // CHUNK
        kv_copies = [
            pltpu.make_async_copy(
                attn_hbm.at[:, heads_all + j * CHUNK:heads_all + (j + 1) * CHUNK],
                attn_v.at[:, heads_all + j * CHUNK:heads_all + (j + 1) * CHUNK],
                sems.at[4 + j],
            )
            for j in range(n_kv)
        ]
        copies = [
            pltpu.make_async_copy(embed_hbm, embed_v, sems.at[0]),
            pltpu.make_async_copy(attn_hbm.at[:, :heads_all], attn_v.at[:, :heads_all], sems.at[1]),
            pltpu.make_async_copy(mix_hbm, mix_v, sems.at[2]),
            pltpu.make_async_copy(read_hbm, read_v, sems.at[3]),
        ]
        copies[0].start()
        for copy in kv_copies:
            copy.start()
        for copy in copies[1:]:
            copy.start()
        prev_copy.start()
        for copy in inputs:
            copy.wait()
        before = lax.broadcasted_iota(jnp.int32, (span, n_in), 0) + (rows - 1)
        column = lax.broadcasted_iota(jnp.int32, (span, n_in), 1)
        if mirrored:
            source = ((before >> 7) << 7) + (rows - 1) - (before & (rows - 1))
        else:
            source = before
        select = (column == source).astype(jnp.bfloat16)
        for m in range(micro):
            pieces_s[0:rows, :] = edge_ref[m].astype(jnp.bfloat16)
            pieces_s[rows:2 * rows, :] = back2_ref[m].astype(jnp.bfloat16)
            pieces_s[2 * rows:3 * rows, :] = back1_ref[m].astype(jnp.bfloat16)
            pieces_s[3 * rows:4 * rows, :] = own_ref[m].astype(jnp.bfloat16)
            shifted_s[m * span:(m + 1) * span, :] = jnp.dot(
                select, pieces_s[...], preferred_element_type=jnp.float32
            ).astype(jnp.bfloat16)
        copies[0].wait()
        hidden = jnp.dot(shifted_s[...], embed_v[...], preferred_element_type=jnp.float32)
        hidden_s[...] = hidden
        square = jnp.mean(hidden * hidden, axis=-1, keepdims=True)
        normed_s[...] = (hidden * lax.rsqrt(square + 1e-06) * ga_ref[...]).astype(jnp.bfloat16)
        for j in range(n_kv):
            kv_copies[j].wait()
            kv_s[:, j * CHUNK:(j + 1) * CHUNK] = jnp.dot(
                normed_s[...], attn_v[:, heads_all + j * CHUNK:heads_all + (j + 1) * CHUNK],
                preferred_element_type=jnp.float32,
            ).astype(jnp.bfloat16)
        copies[1].wait()

        def q_step(j, carry):
            cols = pl.ds(pl.multiple_of(j * CHUNK, CHUNK), CHUNK)
            for m in range(micro):
                q_s[m * rows:(m + 1) * rows, cols] = jnp.dot(
                    normed_s[m * span + own_at:(m + 1) * span, :], attn_v[:, cols],
                    preferred_element_type=jnp.float32,
                ).astype(jnp.bfloat16)
            return carry

        lax.fori_loop(0, heads_all // CHUNK, q_step, 0)

        for m in range(micro):
            q3 = jnp.stack([q_s[m * rows:(m + 1) * rows, h * HEAD_DIM:(h + 1) * HEAD_DIM] for h in range(heads)])
            k3 = jnp.stack([kv_s[m * span:(m + 1) * span, h * HEAD_DIM:(h + 1) * HEAD_DIM] for h in range(heads)])
            v3 = jnp.stack([
                kv_s[m * span:(m + 1) * span, heads_all + h * HEAD_DIM:heads_all + (h + 1) * HEAD_DIM]
                for h in range(heads)
            ])
            scores = jnp.einsum("hqd,hkd->hqk", q3, k3, preferred_element_type=jnp.float32) * scale
            scores = jnp.where(mask_ref[...][None] > 0.5, scores, -jnp.inf)
            top = jnp.max(scores, axis=-1, keepdims=True)
            expo = jnp.exp(scores - top)
            total = jnp.sum(expo, axis=-1, keepdims=True)
            mixed = jnp.einsum(
                "hqk,hkd->hqd", expo.astype(jnp.bfloat16), v3, preferred_element_type=jnp.float32
            ) / total
            for h in range(heads):
                mixed_s[m * rows:(m + 1) * rows, h * HEAD_DIM:(h + 1) * HEAD_DIM] = mixed[h].astype(jnp.bfloat16)

        copies[2].wait()
        for m in range(micro):
            res_s[m * rows:(m + 1) * rows, :] = hidden_s[m * span + own_at:(m + 1) * span, :] + jnp.dot(
                mixed_s[m * rows:(m + 1) * rows, :], mix_v[...], preferred_element_type=jnp.float32
            )
        residual = res_s[...]
        square = jnp.mean(residual * residual, axis=-1, keepdims=True)
        final_normed = (residual * lax.rsqrt(square + 1e-06) * gb_ref[...]).astype(jnp.bfloat16)
        copies[3].wait()
        raw = jnp.dot(final_normed, read_v[...], preferred_element_type=jnp.float32)
        shift_mean = raw[:, :width_in]
        log_scale = 0.5 * jnp.tanh(raw[:, width_in:])
        if mirrored:
            i = lax.broadcasted_iota(jnp.int32, (rows, rows), 0)
            c = lax.broadcasted_iota(jnp.int32, (rows, rows), 1)
            flip = (c == (rows - 1) - i).astype(jnp.bfloat16)
        for m in range(micro):
            own = own_ref[m]
            if mirrored:
                high = own.astype(jnp.bfloat16)
                rest = own - high.astype(jnp.float32)
                middle = rest.astype(jnp.bfloat16)
                low = (rest - middle.astype(jnp.float32)).astype(jnp.bfloat16)
                parts = [jnp.dot(flip, part, preferred_element_type=jnp.float32) for part in (high, middle, low)]
                own = (parts[0] + parts[1]) + parts[2]
            rows_m = slice(m * rows, (m + 1) * rows)
            result = (own - shift_mean[rows_m]) * jnp.exp(-log_scale[rows_m])
            low_v[m] = result.astype(jnp.bfloat16)
            if m == 0:
                prev_copy.wait()
            stored_v[m] = jnp.where(keep_ref[0] > 0, result, prev_v[m])
        outputs = [
            pltpu.make_async_copy(stored_v, stored_hbm, io_sems.at[5]),
            pltpu.make_async_copy(low_v, low_hbm, io_sems.at[6]),
        ]
        for copy in outputs:
            copy.start()
        for copy in outputs:
            copy.wait()

    width = heads_all
    flops = 2 * n_rows * (width_in * width + width * 2 * heads_all)
    flops += 2 * micro * rows * (width * heads_all + 2 * heads * span * HEAD_DIM + heads_all * width + width * 2 * width_in)
    weight_bytes = 2 * (width_in * width + width * 3 * heads_all + heads_all * width + width * 2 * width_in)
    vmem = pltpu.VMEM
    call = pl.pallas_call(
        kernel,
        out_shape=(
            jax.ShapeDtypeStruct((micro, rows, width_in), jnp.float32),
            jax.ShapeDtypeStruct((micro, rows, width_in), jnp.bfloat16),
        ),
        in_specs=[pl.BlockSpec(memory_space=pltpu.SMEM)] + [pl.BlockSpec(memory_space=vmem)] * 3
        + [pl.BlockSpec(memory_space=pltpu.HBM)] * 9,
        out_specs=(pl.BlockSpec(memory_space=pltpu.HBM), pl.BlockSpec(memory_space=pltpu.HBM)),
        scratch_shapes=[
            vmem((width_in, width), jnp.bfloat16),
            vmem((width, 3 * heads_all), jnp.bfloat16),
            vmem((heads_all, width), jnp.bfloat16),
            vmem((width, 2 * width_in), jnp.bfloat16),
            pltpu.SemaphoreType.DMA((4 + 2 * heads_all // CHUNK,)),
            pltpu.SemaphoreType.DMA((7,)),
            vmem((micro, rows, width_in), jnp.float32),
            vmem((micro, rows, width_in), piece_dtype),
            vmem((micro, rows, width_in), piece_dtype),
            vmem((micro, rows, width_in), piece_dtype),
            vmem((micro, rows, width_in), jnp.float32),
            vmem((micro, rows, width_in), jnp.float32),
            vmem((micro, rows, width_in), jnp.bfloat16),
            vmem((n_in, width_in), jnp.bfloat16),
            vmem((n_rows, width_in), jnp.bfloat16),
            vmem((n_rows, width), jnp.float32),
            vmem((n_rows, width), jnp.bfloat16),
            vmem((micro * rows, heads_all), jnp.bfloat16),
            vmem((n_rows, 2 * heads_all), jnp.bfloat16),
            vmem((micro * rows, heads_all), jnp.bfloat16),
            vmem((micro * rows, width), jnp.float32),
        ],
        compiler_params=pltpu.CompilerParams(vmem_limit_bytes=56 * 1024 * 1024),
        cost_estimate=pl.CostEstimate(
            flops=flops,
            bytes_accessed=weight_bytes + n_rows * width_in * 2 + 2 * micro * rows * width_in * 4,
            transcendentals=micro * heads * rows * span + micro * rows * 2 * width_in,
        ),
    )
    return call


def rms_scaled(values, gain):
    return values * lax.rsqrt(jnp.mean(values * values, axis=-1, keepdims=True) + 1e-06) * gain


def body(
    patches,
    tile_list,
    input_weight,
    attention_weight,
    mixing_weight,
    output_weight,
    norm_gain,
    final_gain,
):
    micro, rows, width_in = patches.shape
    assert rows == TILE
    heads_all = mixing_weight.shape[1]
    head_count = heads_all // HEAD_DIM
    segment = lax.axis_index("segment")
    place = lax.axis_index("seq")
    n_seq = lax.axis_size("seq")
    n_seg = lax.axis_size("segment")
    tiles_all = tile_list.shape[0]
    span = (BACK + 1) * rows

    window_tiles = place - BACK + jnp.arange(BACK + 1, dtype=jnp.int32)
    my_list = lax.dynamic_index_in_dim(tile_list, place, 0, keepdims=False)
    listed = jnp.any(my_list[:, None] == window_tiles[None, :], axis=0) & (window_tiles >= 0)
    listed = jnp.repeat(listed, rows)
    query_pos = jnp.arange(rows, dtype=jnp.int32) + BACK * rows
    key_pos = jnp.arange(span, dtype=jnp.int32)
    allowed = listed[None, :] & (key_pos[None, :] <= query_pos[:, None])

    first_call = make_block_call(micro, rows, width_in, heads_all, False, jnp.float32)
    later_call = make_block_call(micro, rows, width_in, heads_all, True, jnp.bfloat16)
    mask = allowed.astype(jnp.float32)
    weights = (
        norm_gain[0].reshape(1, -1),
        final_gain[0].reshape(1, -1),
        input_weight[0],
        attention_weight[0],
        mixing_weight[0],
        output_weight[0],
    )

    axes = ("segment", "seq")

    def first_inputs():
        def behind(distance):
            pairs = [(q, q + distance) for q in range(n_seq) if q + distance < n_seq]
            return lax.ppermute(patches, axes, pairs)

        return patches, behind(1), behind(2), behind(BACK + 1)

    def next_inputs(result, result_low, turn):
        src = turn * n_seq
        dst = (turn + 1) * n_seq

        def send(block, offset):
            pairs = []
            for q in range(n_seq):
                target = n_seq - 1 - q + offset
                if 0 <= target < n_seq:
                    pairs.append((src + q, dst + target))
            return lax.ppermute(block, axes, pairs)

        return (
            send(result, 0),
            send(result_low, 1),
            send(result_low, 2),
            send(result_low, BACK + 1),
        )

    inputs = first_inputs()
    out = jnp.zeros((micro, rows, width_in), jnp.float32)
    gains, matrices = weights[:2], weights[2:]
    for turn in range(n_seg):
        call = first_call if turn == 0 else later_call
        keep = (segment == turn).astype(jnp.int32).reshape(1)
        out, result_low = call(keep, mask, *gains, *inputs, out, *matrices)
        if turn + 1 < n_seg:
            inputs = next_inputs(out, result_low, turn)
    return out[None]


def solution(mesh):
    in_specs = (
        P(None, "seq", None),
        P(),
        P("segment", None, None),
        P("segment", None, None),
        P("segment", None, None),
        P("segment", None, None),
        P("segment", None),
        P("segment", None),
    )
    out_specs = P("segment", None, "seq", None)
    return jax.shard_map(body, mesh=mesh, in_specs=in_specs, out_specs=out_specs, check_vma=False)
```

```python
import jax
import jax.numpy as jnp
from jax import lax
from jax.experimental import pallas as pl
from jax.experimental.pallas import tpu as pltpu
from jax.sharding import PartitionSpec as P

HEAD_DIM = 128
TILE = 128
BACK = 2

CHUNK = 512


def make_block_call(micro, rows, width_in, heads_all, mirrored, piece_dtype):
    span = (BACK + 1) * rows
    own_at = BACK * rows
    n_rows = micro * span
    n_in = (BACK + 2) * rows
    scale = HEAD_DIM ** (-0.5)
    heads = heads_all // HEAD_DIM

    def kernel(keep_ref, prev_ref, own_ref, back1_ref, back2_ref, edge_ref, mask_ref, ga_ref, gb_ref,
               embed_hbm, attn_hbm, mix_hbm, read_hbm,
               out_ref, outb_ref,
               embed_v, attn_v, mix_v, read_v, sems,
               pieces_s, shifted_s, hidden_s, normed_s, q_s, kv_s, mixed_s, res_s):
        n_kv = 2 * heads_all // CHUNK
        kv_copies = [
            pltpu.make_async_copy(
                attn_hbm.at[:, heads_all + j * CHUNK:heads_all + (j + 1) * CHUNK],
                attn_v.at[:, heads_all + j * CHUNK:heads_all + (j + 1) * CHUNK],
                sems.at[4 + j],
            )
            for j in range(n_kv)
        ]
        copies = [
            pltpu.make_async_copy(embed_hbm, embed_v, sems.at[0]),
            pltpu.make_async_copy(attn_hbm.at[:, :heads_all], attn_v.at[:, :heads_all], sems.at[1]),
            pltpu.make_async_copy(mix_hbm, mix_v, sems.at[2]),
            pltpu.make_async_copy(read_hbm, read_v, sems.at[3]),
        ]
        copies[0].start()
        for copy in kv_copies:
            copy.start()
        for copy in copies[1:]:
            copy.start()
        before = lax.broadcasted_iota(jnp.int32, (span, n_in), 0) + (rows - 1)
        column = lax.broadcasted_iota(jnp.int32, (span, n_in), 1)
        if mirrored:
            source = ((before >> 7) << 7) + (rows - 1) - (before & (rows - 1))
        else:
            source = before
        select = (column == source).astype(jnp.bfloat16)
        for m in range(micro):
            pieces_s[0:rows, :] = edge_ref[m].astype(jnp.bfloat16)
            pieces_s[rows:2 * rows, :] = back2_ref[m].astype(jnp.bfloat16)
            pieces_s[2 * rows:3 * rows, :] = back1_ref[m].astype(jnp.bfloat16)
            pieces_s[3 * rows:4 * rows, :] = own_ref[m].astype(jnp.bfloat16)
            shifted_s[m * span:(m + 1) * span, :] = jnp.dot(
                select, pieces_s[...], preferred_element_type=jnp.float32
            ).astype(jnp.bfloat16)
        copies[0].wait()
        hidden = jnp.dot(shifted_s[...], embed_v[...], preferred_element_type=jnp.float32)
        hidden_s[...] = hidden
        square = jnp.mean(hidden * hidden, axis=-1, keepdims=True)
        normed_s[...] = (hidden * lax.rsqrt(square + 1e-06) * ga_ref[...]).astype(jnp.bfloat16)
        for j in range(n_kv):
            kv_copies[j].wait()
            kv_s[:, j * CHUNK:(j + 1) * CHUNK] = jnp.dot(
                normed_s[...], attn_v[:, heads_all + j * CHUNK:heads_all + (j + 1) * CHUNK],
                preferred_element_type=jnp.float32,
            ).astype(jnp.bfloat16)
        copies[1].wait()

        def q_step(j, carry):
            cols = pl.ds(pl.multiple_of(j * CHUNK, CHUNK), CHUNK)
            for m in range(micro):
                q_s[m * rows:(m + 1) * rows, cols] = jnp.dot(
                    normed_s[m * span + own_at:(m + 1) * span, :], attn_v[:, cols],
                    preferred_element_type=jnp.float32,
                ).astype(jnp.bfloat16)
            return carry

        lax.fori_loop(0, heads_all // CHUNK, q_step, 0)

        for m in range(micro):
            q3 = jnp.stack([q_s[m * rows:(m + 1) * rows, h * HEAD_DIM:(h + 1) * HEAD_DIM] for h in range(heads)])
            k3 = jnp.stack([kv_s[m * span:(m + 1) * span, h * HEAD_DIM:(h + 1) * HEAD_DIM] for h in range(heads)])
            v3 = jnp.stack([
                kv_s[m * span:(m + 1) * span, heads_all + h * HEAD_DIM:heads_all + (h + 1) * HEAD_DIM]
                for h in range(heads)
            ])
            scores = jnp.einsum("hqd,hkd->hqk", q3, k3, preferred_element_type=jnp.float32) * scale
            scores = jnp.where(mask_ref[...][None] > 0.5, scores, -jnp.inf)
            top = jnp.max(scores, axis=-1, keepdims=True)
            expo = jnp.exp(scores - top)
            total = jnp.sum(expo, axis=-1, keepdims=True)
            mixed = jnp.einsum(
                "hqk,hkd->hqd", expo.astype(jnp.bfloat16), v3, preferred_element_type=jnp.float32
            ) / total
            for h in range(heads):
                mixed_s[m * rows:(m + 1) * rows, h * HEAD_DIM:(h + 1) * HEAD_DIM] = mixed[h].astype(jnp.bfloat16)

        copies[2].wait()
        for m in range(micro):
            res_s[m * rows:(m + 1) * rows, :] = hidden_s[m * span + own_at:(m + 1) * span, :] + jnp.dot(
                mixed_s[m * rows:(m + 1) * rows, :], mix_v[...], preferred_element_type=jnp.float32
            )
        residual = res_s[...]
        square = jnp.mean(residual * residual, axis=-1, keepdims=True)
        final_normed = (residual * lax.rsqrt(square + 1e-06) * gb_ref[...]).astype(jnp.bfloat16)
        copies[3].wait()
        raw = jnp.dot(final_normed, read_v[...], preferred_element_type=jnp.float32)
        shift_mean = raw[:, :width_in]
        log_scale = 0.5 * jnp.tanh(raw[:, width_in:])
        if mirrored:
            i = lax.broadcasted_iota(jnp.int32, (rows, rows), 0)
            c = lax.broadcasted_iota(jnp.int32, (rows, rows), 1)
            flip = (c == (rows - 1) - i).astype(jnp.bfloat16)
        for m in range(micro):
            own = own_ref[m]
            if mirrored:
                high = own.astype(jnp.bfloat16)
                rest = own - high.astype(jnp.float32)
                middle = rest.astype(jnp.bfloat16)
                low = (rest - middle.astype(jnp.float32)).astype(jnp.bfloat16)
                parts = [jnp.dot(flip, part, preferred_element_type=jnp.float32) for part in (high, middle, low)]
                own = (parts[0] + parts[1]) + parts[2]
            rows_m = slice(m * rows, (m + 1) * rows)
            result = (own - shift_mean[rows_m]) * jnp.exp(-log_scale[rows_m])
            out_ref[m] = jnp.where(keep_ref[0] > 0, result, prev_ref[m])
            outb_ref[m] = result.astype(jnp.bfloat16)

    width = heads_all
    flops = 2 * n_rows * (width_in * width + width * 2 * heads_all)
    flops += 2 * micro * rows * (width * heads_all + 2 * heads * span * HEAD_DIM + heads_all * width + width * 2 * width_in)
    weight_bytes = 2 * (width_in * width + width * 3 * heads_all + heads_all * width + width * 2 * width_in)
    vmem = pltpu.VMEM
    call = pl.pallas_call(
        kernel,
        out_shape=(
            jax.ShapeDtypeStruct((micro, rows, width_in), jnp.float32),
            jax.ShapeDtypeStruct((micro, rows, width_in), jnp.bfloat16),
        ),
        in_specs=[pl.BlockSpec(memory_space=pltpu.SMEM)] + [pl.BlockSpec(memory_space=vmem)] * 8
        + [pl.BlockSpec(memory_space=pl.ANY)] * 4,
        out_specs=(pl.BlockSpec(memory_space=vmem), pl.BlockSpec(memory_space=vmem)),
        scratch_shapes=[
            vmem((width_in, width), jnp.bfloat16),
            vmem((width, 3 * heads_all), jnp.bfloat16),
            vmem((heads_all, width), jnp.bfloat16),
            vmem((width, 2 * width_in), jnp.bfloat16),
            pltpu.SemaphoreType.DMA((4 + 2 * heads_all // CHUNK,)),
            vmem((n_in, width_in), jnp.bfloat16),
            vmem((n_rows, width_in), jnp.bfloat16),
            vmem((n_rows, width), jnp.float32),
            vmem((n_rows, width), jnp.bfloat16),
            vmem((micro * rows, heads_all), jnp.bfloat16),
            vmem((n_rows, 2 * heads_all), jnp.bfloat16),
            vmem((micro * rows, heads_all), jnp.bfloat16),
            vmem((micro * rows, width), jnp.float32),
        ],
        compiler_params=pltpu.CompilerParams(vmem_limit_bytes=56 * 1024 * 1024),
        cost_estimate=pl.CostEstimate(
            flops=flops,
            bytes_accessed=weight_bytes + n_rows * width_in * 2 + 2 * micro * rows * width_in * 4,
            transcendentals=micro * heads * rows * span + micro * rows * 2 * width_in,
        ),
    )
    return call


def rms_scaled(values, gain):
    return values * lax.rsqrt(jnp.mean(values * values, axis=-1, keepdims=True) + 1e-06) * gain


def body(
    patches,
    tile_list,
    input_weight,
    attention_weight,
    mixing_weight,
    output_weight,
    norm_gain,
    final_gain,
):
    micro, rows, width_in = patches.shape
    assert rows == TILE
    heads_all = mixing_weight.shape[1]
    head_count = heads_all // HEAD_DIM
    segment = lax.axis_index("segment")
    place = lax.axis_index("seq")
    n_seq = lax.axis_size("seq")
    n_seg = lax.axis_size("segment")
    tiles_all = tile_list.shape[0]
    span = (BACK + 1) * rows

    window_tiles = place - BACK + jnp.arange(BACK + 1, dtype=jnp.int32)
    my_list = lax.dynamic_index_in_dim(tile_list, place, 0, keepdims=False)
    listed = jnp.any(my_list[:, None] == window_tiles[None, :], axis=0) & (window_tiles >= 0)
    listed = jnp.repeat(listed, rows)
    query_pos = jnp.arange(rows, dtype=jnp.int32) + BACK * rows
    key_pos = jnp.arange(span, dtype=jnp.int32)
    allowed = listed[None, :] & (key_pos[None, :] <= query_pos[:, None])

    first_call = make_block_call(micro, rows, width_in, heads_all, False, jnp.float32)
    later_call = make_block_call(micro, rows, width_in, heads_all, True, jnp.bfloat16)
    mask = allowed.astype(jnp.float32)
    weights = (
        norm_gain[0].reshape(1, -1),
        final_gain[0].reshape(1, -1),
        input_weight[0],
        attention_weight[0],
        mixing_weight[0],
        output_weight[0],
    )

    axes = ("segment", "seq")

    def first_inputs():
        def behind(distance):
            pairs = [(q, q + distance) for q in range(n_seq) if q + distance < n_seq]
            return lax.ppermute(patches, axes, pairs)

        return patches, behind(1), behind(2), behind(BACK + 1)

    def next_inputs(result, result_low, turn):
        src = turn * n_seq
        dst = (turn + 1) * n_seq

        def send(block, offset):
            pairs = []
            for q in range(n_seq):
                target = n_seq - 1 - q + offset
                if 0 <= target < n_seq:
                    pairs.append((src + q, dst + target))
            return lax.ppermute(block, axes, pairs)

        return (
            send(result, 0),
            send(result_low, 1),
            send(result_low, 2),
            send(result_low, BACK + 1),
        )

    inputs = first_inputs()
    out = jnp.zeros((micro, rows, width_in), jnp.float32)
    for turn in range(n_seg):
        call = first_call if turn == 0 else later_call
        keep = (segment == turn).astype(jnp.int32).reshape(1)
        out, result_low = call(keep, out, *inputs, mask, *weights)
        if turn + 1 < n_seg:
            inputs = next_inputs(out, result_low, turn)
    return out[None]


def solution(mesh):
    in_specs = (
        P(None, "seq", None),
        P(),
        P("segment", None, None),
        P("segment", None, None),
        P("segment", None, None),
        P("segment", None, None),
        P("segment", None),
        P("segment", None),
    )
    out_specs = P("segment", None, "seq", None)
    return jax.shard_map(body, mesh=mesh, in_specs=in_specs, out_specs=out_specs, check_vma=False)
```

```python
import jax
import jax.numpy as jnp
from jax import lax
from jax.experimental import pallas as pl
from jax.experimental.pallas import tpu as pltpu
from jax.sharding import PartitionSpec as P

HEAD_DIM = 128
TILE = 128
BACK = 2

CHUNK = 1024
VMEM_LIMIT = 24 * 1024 * 1024


def make_block_call(micro, rows, width_in, heads_all, mirrored, piece_dtype):
    span = (BACK + 1) * rows
    own_at = BACK * rows
    n_rows = micro * span
    n_in = (BACK + 2) * rows
    scale = HEAD_DIM ** (-0.5)
    heads = heads_all // HEAD_DIM

    def kernel(keep_ref, prev_ref, own_ref, back1_ref, back2_ref, edge_ref, mask_ref, ga_ref, gb_ref,
               embed_v, attn_v, mix_v, read_v,
               out_ref, outb_ref,
               pieces_s, shifted_s, hidden_s, normed_s, q_s, kv_s, mixed_s, res_s):
        before = lax.broadcasted_iota(jnp.int32, (span, n_in), 0) + (rows - 1)
        column = lax.broadcasted_iota(jnp.int32, (span, n_in), 1)
        if mirrored:
            source = ((before >> 7) << 7) + (rows - 1) - (before & (rows - 1))
        else:
            source = before
        select = (column == source).astype(jnp.bfloat16)
        for m in range(micro):
            pieces_s[0:rows, :] = edge_ref[m].astype(jnp.bfloat16)
            pieces_s[rows:2 * rows, :] = back2_ref[m].astype(jnp.bfloat16)
            pieces_s[2 * rows:3 * rows, :] = back1_ref[m].astype(jnp.bfloat16)
            pieces_s[3 * rows:4 * rows, :] = own_ref[m].astype(jnp.bfloat16)
            shifted_s[m * span:(m + 1) * span, :] = jnp.dot(
                select, pieces_s[...], preferred_element_type=jnp.float32
            ).astype(jnp.bfloat16)
        hidden = jnp.dot(shifted_s[...], embed_v[...], preferred_element_type=jnp.float32)
        hidden_s[...] = hidden
        square = jnp.mean(hidden * hidden, axis=-1, keepdims=True)
        normed_s[...] = (hidden * lax.rsqrt(square + 1e-06) * ga_ref[...]).astype(jnp.bfloat16)
        n_kv = 2 * heads_all // CHUNK
        for j in range(n_kv):
            kv_s[:, j * CHUNK:(j + 1) * CHUNK] = jnp.dot(
                normed_s[...], attn_v[:, heads_all + j * CHUNK:heads_all + (j + 1) * CHUNK],
                preferred_element_type=jnp.float32,
            ).astype(jnp.bfloat16)

        def q_step(j, carry):
            cols = pl.ds(pl.multiple_of(j * CHUNK, CHUNK), CHUNK)
            for m in range(micro):
                q_s[m * rows:(m + 1) * rows, cols] = jnp.dot(
                    normed_s[m * span + own_at:(m + 1) * span, :], attn_v[:, cols],
                    preferred_element_type=jnp.float32,
                ).astype(jnp.bfloat16)
            return carry

        lax.fori_loop(0, heads_all // CHUNK, q_step, 0)

        for m in range(micro):
            q3 = jnp.stack([q_s[m * rows:(m + 1) * rows, h * HEAD_DIM:(h + 1) * HEAD_DIM] for h in range(heads)])
            k3 = jnp.stack([kv_s[m * span:(m + 1) * span, h * HEAD_DIM:(h + 1) * HEAD_DIM] for h in range(heads)])
            v3 = jnp.stack([
                kv_s[m * span:(m + 1) * span, heads_all + h * HEAD_DIM:heads_all + (h + 1) * HEAD_DIM]
                for h in range(heads)
            ])
            scores = jnp.einsum("hqd,hkd->hqk", q3, k3, preferred_element_type=jnp.float32) * scale
            scores = jnp.where(mask_ref[...][None] > 0.5, scores, -jnp.inf)
            top = jnp.max(scores, axis=-1, keepdims=True)
            expo = jnp.exp(scores - top)
            total = jnp.sum(expo, axis=-1, keepdims=True)
            mixed = jnp.einsum(
                "hqk,hkd->hqd", expo.astype(jnp.bfloat16), v3, preferred_element_type=jnp.float32
            ) / total
            for h in range(heads):
                mixed_s[m * rows:(m + 1) * rows, h * HEAD_DIM:(h + 1) * HEAD_DIM] = mixed[h].astype(jnp.bfloat16)

        for m in range(micro):
            res_s[m * rows:(m + 1) * rows, :] = hidden_s[m * span + own_at:(m + 1) * span, :] + jnp.dot(
                mixed_s[m * rows:(m + 1) * rows, :], mix_v[...], preferred_element_type=jnp.float32
            )
        residual = res_s[...]
        square = jnp.mean(residual * residual, axis=-1, keepdims=True)
        final_normed = (residual * lax.rsqrt(square + 1e-06) * gb_ref[...]).astype(jnp.bfloat16)
        raw = jnp.dot(final_normed, read_v[...], preferred_element_type=jnp.float32)
        shift_mean = raw[:, :width_in]
        log_scale = 0.5 * jnp.tanh(raw[:, width_in:])
        if mirrored:
            i = lax.broadcasted_iota(jnp.int32, (rows, rows), 0)
            c = lax.broadcasted_iota(jnp.int32, (rows, rows), 1)
            flip = (c == (rows - 1) - i).astype(jnp.bfloat16)
        for m in range(micro):
            own = own_ref[m]
            if mirrored:
                high = own.astype(jnp.bfloat16)
                rest = own - high.astype(jnp.float32)
                middle = rest.astype(jnp.bfloat16)
                low = (rest - middle.astype(jnp.float32)).astype(jnp.bfloat16)
                parts = [jnp.dot(flip, part, preferred_element_type=jnp.float32) for part in (high, middle, low)]
                own = (parts[0] + parts[1]) + parts[2]
            rows_m = slice(m * rows, (m + 1) * rows)
            result = (own - shift_mean[rows_m]) * jnp.exp(-log_scale[rows_m])
            out_ref[m] = jnp.where(keep_ref[0] > 0, result, prev_ref[m])
            outb_ref[m] = result.astype(jnp.bfloat16)

    width = heads_all
    flops = 2 * n_rows * (width_in * width + width * 2 * heads_all)
    flops += 2 * micro * rows * (width * heads_all + 2 * heads * span * HEAD_DIM + heads_all * width + width * 2 * width_in)
    weight_bytes = 2 * (width_in * width + width * 3 * heads_all + heads_all * width + width * 2 * width_in)
    vmem = pltpu.VMEM
    call = pl.pallas_call(
        kernel,
        out_shape=(
            jax.ShapeDtypeStruct((micro, rows, width_in), jnp.float32),
            jax.ShapeDtypeStruct((micro, rows, width_in), jnp.bfloat16),
        ),
        in_specs=[pl.BlockSpec(memory_space=pltpu.SMEM)] + [pl.BlockSpec(memory_space=vmem)] * 12,
        out_specs=(pl.BlockSpec(memory_space=vmem), pl.BlockSpec(memory_space=vmem)),
        scratch_shapes=[
            vmem((n_in, width_in), jnp.bfloat16),
            vmem((n_rows, width_in), jnp.bfloat16),
            vmem((n_rows, width), jnp.float32),
            vmem((n_rows, width), jnp.bfloat16),
            vmem((micro * rows, heads_all), jnp.bfloat16),
            vmem((n_rows, 2 * heads_all), jnp.bfloat16),
            vmem((micro * rows, heads_all), jnp.bfloat16),
            vmem((micro * rows, width), jnp.float32),
        ],
        compiler_params=pltpu.CompilerParams(vmem_limit_bytes=VMEM_LIMIT),
        cost_estimate=pl.CostEstimate(
            flops=flops,
            bytes_accessed=weight_bytes + n_rows * width_in * 2 + 2 * micro * rows * width_in * 4,
            transcendentals=micro * heads * rows * span + micro * rows * 2 * width_in,
        ),
    )
    return call


def rms_scaled(values, gain):
    return values * lax.rsqrt(jnp.mean(values * values, axis=-1, keepdims=True) + 1e-06) * gain


def body(
    patches,
    tile_list,
    input_weight,
    attention_weight,
    mixing_weight,
    output_weight,
    norm_gain,
    final_gain,
):
    micro, rows, width_in = patches.shape
    assert rows == TILE
    heads_all = mixing_weight.shape[1]
    head_count = heads_all // HEAD_DIM
    segment = lax.axis_index("segment")
    place = lax.axis_index("seq")
    n_seq = lax.axis_size("seq")
    n_seg = lax.axis_size("segment")
    tiles_all = tile_list.shape[0]
    span = (BACK + 1) * rows

    window_tiles = place - BACK + jnp.arange(BACK + 1, dtype=jnp.int32)
    my_list = lax.dynamic_index_in_dim(tile_list, place, 0, keepdims=False)
    listed = jnp.any(my_list[:, None] == window_tiles[None, :], axis=0) & (window_tiles >= 0)
    listed = jnp.repeat(listed, rows)
    query_pos = jnp.arange(rows, dtype=jnp.int32) + BACK * rows
    key_pos = jnp.arange(span, dtype=jnp.int32)
    allowed = listed[None, :] & (key_pos[None, :] <= query_pos[:, None])

    first_call = make_block_call(micro, rows, width_in, heads_all, False, jnp.float32)
    later_call = make_block_call(micro, rows, width_in, heads_all, True, jnp.bfloat16)
    mask = allowed.astype(jnp.float32)
    weights = (
        norm_gain[0].reshape(1, -1),
        final_gain[0].reshape(1, -1),
        input_weight[0],
        attention_weight[0],
        mixing_weight[0],
        output_weight[0],
    )

    axes = ("segment", "seq")

    def first_inputs():
        def behind(distance):
            pairs = [(q, q + distance) for q in range(n_seq) if q + distance < n_seq]
            return lax.ppermute(patches, axes, pairs)

        return patches, behind(1), behind(2), behind(BACK + 1)

    def next_inputs(result, result_low, turn):
        src = turn * n_seq
        dst = (turn + 1) * n_seq

        def send(block, offset):
            pairs = []
            for q in range(n_seq):
                target = n_seq - 1 - q + offset
                if 0 <= target < n_seq:
                    pairs.append((src + q, dst + target))
            return lax.ppermute(block, axes, pairs)

        return (
            send(result, 0),
            send(result_low, 1),
            send(result_low, 2),
            send(result_low, BACK + 1),
        )

    inputs = first_inputs()
    out = jnp.zeros((micro, rows, width_in), jnp.float32)
    for turn in range(n_seg):
        call = first_call if turn == 0 else later_call
        keep = (segment == turn).astype(jnp.int32).reshape(1)
        out, result_low = call(keep, out, *inputs, mask, *weights)
        if turn + 1 < n_seg:
            inputs = next_inputs(out, result_low, turn)
    return out[None]


def solution(mesh):
    in_specs = (
        P(None, "seq", None),
        P(),
        P("segment", None, None),
        P("segment", None, None),
        P("segment", None, None),
        P("segment", None, None),
        P("segment", None),
        P("segment", None),
    )
    out_specs = P("segment", None, "seq", None)
    return jax.shard_map(body, mesh=mesh, in_specs=in_specs, out_specs=out_specs, check_vma=False)
```

```python
import jax
import jax.numpy as jnp
from jax import lax
from jax.experimental import pallas as pl
from jax.experimental.pallas import tpu as pltpu
from jax.sharding import PartitionSpec as P

HEAD_DIM = 128
TILE = 128
BACK = 2

CHUNK = 1024


def make_block_call(micro, rows, width_in, heads_all, mirrored, piece_dtype):
    span = (BACK + 1) * rows
    own_at = BACK * rows
    n_rows = micro * span
    n_in = (BACK + 2) * rows
    scale = HEAD_DIM ** (-0.5)
    heads = heads_all // HEAD_DIM

    def kernel(keep_ref, prev_ref, own_ref, back1_ref, back2_ref, edge_ref, mask_ref, ga_ref, gb_ref,
               embed_hbm, attn_hbm, mix_hbm, read_hbm,
               out_ref, outb_ref,
               embed_v, attn_v, mix_v, read_v, sems,
               pieces_s, shifted_s, hidden_s, normed_s, q_s, kv_s, mixed_s, res_s):
        n_kv = 2 * heads_all // CHUNK
        kv_copies = [
            pltpu.make_async_copy(
                attn_hbm.at[:, heads_all + j * CHUNK:heads_all + (j + 1) * CHUNK],
                attn_v.at[:, heads_all + j * CHUNK:heads_all + (j + 1) * CHUNK],
                sems.at[4 + j],
            )
            for j in range(n_kv)
        ]
        copies = [
            pltpu.make_async_copy(embed_hbm, embed_v, sems.at[0]),
            pltpu.make_async_copy(attn_hbm.at[:, :heads_all], attn_v.at[:, :heads_all], sems.at[1]),
            pltpu.make_async_copy(mix_hbm, mix_v, sems.at[2]),
            pltpu.make_async_copy(read_hbm, read_v, sems.at[3]),
        ]
        copies[0].start()
        for copy in kv_copies:
            copy.start()
        for copy in copies[1:]:
            copy.start()
        before = lax.broadcasted_iota(jnp.int32, (span, n_in), 0) + (rows - 1)
        column = lax.broadcasted_iota(jnp.int32, (span, n_in), 1)
        if mirrored:
            source = ((before >> 7) << 7) + (rows - 1) - (before & (rows - 1))
        else:
            source = before
        select = (column == source).astype(jnp.bfloat16)
        for m in range(micro):
            pieces_s[0:rows, :] = edge_ref[m].astype(jnp.bfloat16)
            pieces_s[rows:2 * rows, :] = back2_ref[m].astype(jnp.bfloat16)
            pieces_s[2 * rows:3 * rows, :] = back1_ref[m].astype(jnp.bfloat16)
            pieces_s[3 * rows:4 * rows, :] = own_ref[m].astype(jnp.bfloat16)
            shifted_s[m * span:(m + 1) * span, :] = jnp.dot(
                select, pieces_s[...], preferred_element_type=jnp.float32
            ).astype(jnp.bfloat16)
        copies[0].wait()
        hidden = jnp.dot(shifted_s[...], embed_v[...], preferred_element_type=jnp.float32)
        hidden_s[...] = hidden
        square = jnp.mean(hidden * hidden, axis=-1, keepdims=True)
        normed_s[...] = (hidden * lax.rsqrt(square + 1e-06) * ga_ref[...]).astype(jnp.bfloat16)
        for j in range(n_kv):
            kv_copies[j].wait()
            kv_s[:, j * CHUNK:(j + 1) * CHUNK] = jnp.dot(
                normed_s[...], attn_v[:, heads_all + j * CHUNK:heads_all + (j + 1) * CHUNK],
                preferred_element_type=jnp.float32,
            ).astype(jnp.bfloat16)
        copies[1].wait()

        def q_step(j, carry):
            cols = pl.ds(pl.multiple_of(j * CHUNK, CHUNK), CHUNK)
            for m in range(micro):
                q_s[m * rows:(m + 1) * rows, cols] = jnp.dot(
                    normed_s[m * span + own_at:(m + 1) * span, :], attn_v[:, cols],
                    preferred_element_type=jnp.float32,
                ).astype(jnp.bfloat16)
            return carry

        lax.fori_loop(0, heads_all // CHUNK, q_step, 0)

        for m in range(micro):
            q3 = jnp.stack([q_s[m * rows:(m + 1) * rows, h * HEAD_DIM:(h + 1) * HEAD_DIM] for h in range(heads)])
            k3 = jnp.stack([kv_s[m * span:(m + 1) * span, h * HEAD_DIM:(h + 1) * HEAD_DIM] for h in range(heads)])
            v3 = jnp.stack([
                kv_s[m * span:(m + 1) * span, heads_all + h * HEAD_DIM:heads_all + (h + 1) * HEAD_DIM]
                for h in range(heads)
            ])
            scores = jnp.einsum("hqd,hkd->hqk", q3, k3, preferred_element_type=jnp.float32) * scale
            scores = jnp.where(mask_ref[...][None] > 0.5, scores, -jnp.inf)
            top = jnp.max(scores, axis=-1, keepdims=True)
            expo = jnp.exp(scores - top)
            total = jnp.sum(expo, axis=-1, keepdims=True)
            mixed = jnp.einsum(
                "hqk,hkd->hqd", expo.astype(jnp.bfloat16), v3, preferred_element_type=jnp.float32
            ) / total
            for h in range(heads):
                mixed_s[m * rows:(m + 1) * rows, h * HEAD_DIM:(h + 1) * HEAD_DIM] = mixed[h].astype(jnp.bfloat16)

        copies[2].wait()
        for m in range(micro):
            res_s[m * rows:(m + 1) * rows, :] = hidden_s[m * span + own_at:(m + 1) * span, :] + jnp.dot(
                mixed_s[m * rows:(m + 1) * rows, :], mix_v[...], preferred_element_type=jnp.float32
            )
        residual = res_s[...]
        square = jnp.mean(residual * residual, axis=-1, keepdims=True)
        final_normed = (residual * lax.rsqrt(square + 1e-06) * gb_ref[...]).astype(jnp.bfloat16)
        copies[3].wait()
        raw = jnp.dot(final_normed, read_v[...], preferred_element_type=jnp.float32)
        shift_mean = raw[:, :width_in]
        log_scale = 0.5 * jnp.tanh(raw[:, width_in:])
        if mirrored:
            i = lax.broadcasted_iota(jnp.int32, (rows, rows), 0)
            c = lax.broadcasted_iota(jnp.int32, (rows, rows), 1)
            flip = (c == (rows - 1) - i).astype(jnp.bfloat16)
        for m in range(micro):
            own = own_ref[m]
            if mirrored:
                high = own.astype(jnp.bfloat16)
                rest = own - high.astype(jnp.float32)
                middle = rest.astype(jnp.bfloat16)
                low = (rest - middle.astype(jnp.float32)).astype(jnp.bfloat16)
                parts = [jnp.dot(flip, part, preferred_element_type=jnp.float32) for part in (high, middle, low)]
                own = (parts[0] + parts[1]) + parts[2]
            rows_m = slice(m * rows, (m + 1) * rows)
            result = (own - shift_mean[rows_m]) * jnp.exp(-log_scale[rows_m])
            out_ref[m] = jnp.where(keep_ref[0] > 0, result, prev_ref[m])
            outb_ref[m] = result.astype(jnp.bfloat16)

    width = heads_all
    flops = 2 * n_rows * (width_in * width + width * 2 * heads_all)
    flops += 2 * micro * rows * (width * heads_all + 2 * heads * span * HEAD_DIM + heads_all * width + width * 2 * width_in)
    weight_bytes = 2 * (width_in * width + width * 3 * heads_all + heads_all * width + width * 2 * width_in)
    vmem = pltpu.VMEM
    call = pl.pallas_call(
        kernel,
        out_shape=(
            jax.ShapeDtypeStruct((micro, rows, width_in), jnp.float32),
            jax.ShapeDtypeStruct((micro, rows, width_in), jnp.bfloat16),
        ),
        in_specs=[pl.BlockSpec(memory_space=pltpu.SMEM)] + [pl.BlockSpec(memory_space=vmem)] * 8
        + [pl.BlockSpec(memory_space=pl.ANY)] * 4,
        out_specs=(pl.BlockSpec(memory_space=vmem), pl.BlockSpec(memory_space=vmem)),
        scratch_shapes=[
            vmem((width_in, width), jnp.bfloat16),
            vmem((width, 3 * heads_all), jnp.bfloat16),
            vmem((heads_all, width), jnp.bfloat16),
            vmem((width, 2 * width_in), jnp.bfloat16),
            pltpu.SemaphoreType.DMA((4 + 2 * heads_all // CHUNK,)),
            vmem((n_in, width_in), jnp.bfloat16),
            vmem((n_rows, width_in), jnp.bfloat16),
            vmem((n_rows, width), jnp.float32),
            vmem((n_rows, width), jnp.bfloat16),
            vmem((micro * rows, heads_all), jnp.bfloat16),
            vmem((n_rows, 2 * heads_all), jnp.bfloat16),
            vmem((micro * rows, heads_all), jnp.bfloat16),
            vmem((micro * rows, width), jnp.float32),
        ],
        compiler_params=pltpu.CompilerParams(vmem_limit_bytes=56 * 1024 * 1024),
        cost_estimate=pl.CostEstimate(
            flops=flops,
            bytes_accessed=weight_bytes + n_rows * width_in * 2 + 2 * micro * rows * width_in * 4,
            transcendentals=micro * heads * rows * span + micro * rows * 2 * width_in,
        ),
    )
    return call


def rms_scaled(values, gain):
    return values * lax.rsqrt(jnp.mean(values * values, axis=-1, keepdims=True) + 1e-06) * gain


def body(
    patches,
    tile_list,
    input_weight,
    attention_weight,
    mixing_weight,
    output_weight,
    norm_gain,
    final_gain,
):
    micro, rows, width_in = patches.shape
    assert rows == TILE
    heads_all = mixing_weight.shape[1]
    head_count = heads_all // HEAD_DIM
    segment = lax.axis_index("segment")
    place = lax.axis_index("seq")
    n_seq = lax.axis_size("seq")
    n_seg = lax.axis_size("segment")
    tiles_all = tile_list.shape[0]
    span = (BACK + 1) * rows

    window_tiles = place - BACK + jnp.arange(BACK + 1, dtype=jnp.int32)
    my_list = lax.dynamic_index_in_dim(tile_list, place, 0, keepdims=False)
    listed = jnp.any(my_list[:, None] == window_tiles[None, :], axis=0) & (window_tiles >= 0)
    listed = jnp.repeat(listed, rows)
    query_pos = jnp.arange(rows, dtype=jnp.int32) + BACK * rows
    key_pos = jnp.arange(span, dtype=jnp.int32)
    allowed = listed[None, :] & (key_pos[None, :] <= query_pos[:, None])

    first_call = make_block_call(micro, rows, width_in, heads_all, False, jnp.float32)
    later_call = make_block_call(micro, rows, width_in, heads_all, True, jnp.bfloat16)
    mask = allowed.astype(jnp.float32)
    weights = (
        norm_gain[0].reshape(1, -1),
        final_gain[0].reshape(1, -1),
        input_weight[0],
        attention_weight[0],
        mixing_weight[0],
        output_weight[0],
    )

    axes = ("segment", "seq")

    def first_inputs():
        def behind(distance):
            pairs = [(q, q + distance) for q in range(n_seq) if q + distance < n_seq]
            return lax.ppermute(patches, axes, pairs)

        return patches, behind(1), behind(2), behind(BACK + 1)

    def next_inputs(result, result_low, turn):
        src = turn * n_seq
        dst = (turn + 1) * n_seq

        def send(block, offset):
            pairs = []
            for q in range(n_seq):
                target = n_seq - 1 - q + offset
                if 0 <= target < n_seq:
                    pairs.append((src + q, dst + target))
            return lax.ppermute(block, axes, pairs)

        return (
            send(result, 0),
            send(result_low, 1),
            send(result_low, 2),
            send(result_low, BACK + 1),
        )

    inputs = first_inputs()
    out = jnp.zeros((micro, rows, width_in), jnp.float32)
    for turn in range(n_seg):
        call = first_call if turn == 0 else later_call
        keep = (segment == turn).astype(jnp.int32).reshape(1)
        out, result_low = call(keep, out, *inputs, mask, *weights)
        if turn + 1 < n_seg:
            inputs = next_inputs(out, result_low, turn)
    return out[None]


def solution(mesh):
    in_specs = (
        P(None, "seq", None),
        P(),
        P("segment", None, None),
        P("segment", None, None),
        P("segment", None, None),
        P("segment", None, None),
        P("segment", None),
        P("segment", None),
    )
    out_specs = P("segment", None, "seq", None)
    return jax.shard_map(body, mesh=mesh, in_specs=in_specs, out_specs=out_specs, check_vma=False)
```

```python
import jax
import jax.numpy as jnp
from jax import lax
from jax.experimental import pallas as pl
from jax.experimental.pallas import tpu as pltpu
from jax.sharding import PartitionSpec as P

HEAD_DIM = 128
TILE = 128
BACK = 2

CHUNK = 1024


def make_block_call(micro, rows, width_in, heads_all, mirrored, piece_dtype):
    span = (BACK + 1) * rows
    own_at = BACK * rows
    n_rows = micro * span
    n_in = (BACK + 2) * rows
    scale = HEAD_DIM ** (-0.5)
    heads = heads_all // HEAD_DIM

    def kernel(keep_ref, prev_ref, own_ref, back1_ref, back2_ref, edge_ref, mask_ref, ga_ref, gb_ref,
               embed_v, read_v, attn_hbm, mix_hbm,
               out_ref, outb_ref,
               attn_v, mix_v, sems,
               pieces_s, shifted_s, hidden_s, normed_s, q_s, kv_s, mixed_s, res_s):
        n_kv = 2 * heads_all // CHUNK
        kv_copies = [
            pltpu.make_async_copy(
                attn_hbm.at[:, heads_all + j * CHUNK:heads_all + (j + 1) * CHUNK],
                attn_v.at[:, heads_all + j * CHUNK:heads_all + (j + 1) * CHUNK],
                sems.at[2 + j],
            )
            for j in range(n_kv)
        ]
        copies = [
            pltpu.make_async_copy(attn_hbm.at[:, :heads_all], attn_v.at[:, :heads_all], sems.at[0]),
            pltpu.make_async_copy(mix_hbm, mix_v, sems.at[1]),
        ]
        for copy in kv_copies:
            copy.start()
        for copy in copies:
            copy.start()
        before = lax.broadcasted_iota(jnp.int32, (span, n_in), 0) + (rows - 1)
        column = lax.broadcasted_iota(jnp.int32, (span, n_in), 1)
        if mirrored:
            source = ((before >> 7) << 7) + (rows - 1) - (before & (rows - 1))
        else:
            source = before
        select = (column == source).astype(jnp.bfloat16)
        for m in range(micro):
            pieces_s[0:rows, :] = edge_ref[m].astype(jnp.bfloat16)
            pieces_s[rows:2 * rows, :] = back2_ref[m].astype(jnp.bfloat16)
            pieces_s[2 * rows:3 * rows, :] = back1_ref[m].astype(jnp.bfloat16)
            pieces_s[3 * rows:4 * rows, :] = own_ref[m].astype(jnp.bfloat16)
            shifted_s[m * span:(m + 1) * span, :] = jnp.dot(
                select, pieces_s[...], preferred_element_type=jnp.float32
            ).astype(jnp.bfloat16)
        hidden = jnp.dot(shifted_s[...], embed_v[...], preferred_element_type=jnp.float32)
        hidden_s[...] = hidden
        square = jnp.mean(hidden * hidden, axis=-1, keepdims=True)
        normed_s[...] = (hidden * lax.rsqrt(square + 1e-06) * ga_ref[...]).astype(jnp.bfloat16)
        for j in range(n_kv):
            kv_copies[j].wait()
            kv_s[:, j * CHUNK:(j + 1) * CHUNK] = jnp.dot(
                normed_s[...], attn_v[:, heads_all + j * CHUNK:heads_all + (j + 1) * CHUNK],
                preferred_element_type=jnp.float32,
            ).astype(jnp.bfloat16)
        copies[0].wait()

        def q_step(j, carry):
            cols = pl.ds(pl.multiple_of(j * CHUNK, CHUNK), CHUNK)
            for m in range(micro):
                q_s[m * rows:(m + 1) * rows, cols] = jnp.dot(
                    normed_s[m * span + own_at:(m + 1) * span, :], attn_v[:, cols],
                    preferred_element_type=jnp.float32,
                ).astype(jnp.bfloat16)
            return carry

        lax.fori_loop(0, heads_all // CHUNK, q_step, 0)

        for m in range(micro):
            q3 = jnp.stack([q_s[m * rows:(m + 1) * rows, h * HEAD_DIM:(h + 1) * HEAD_DIM] for h in range(heads)])
            k3 = jnp.stack([kv_s[m * span:(m + 1) * span, h * HEAD_DIM:(h + 1) * HEAD_DIM] for h in range(heads)])
            v3 = jnp.stack([
                kv_s[m * span:(m + 1) * span, heads_all + h * HEAD_DIM:heads_all + (h + 1) * HEAD_DIM]
                for h in range(heads)
            ])
            scores = jnp.einsum("hqd,hkd->hqk", q3, k3, preferred_element_type=jnp.float32) * scale
            scores = jnp.where(mask_ref[...][None] > 0.5, scores, -jnp.inf)
            top = jnp.max(scores, axis=-1, keepdims=True)
            expo = jnp.exp(scores - top)
            total = jnp.sum(expo, axis=-1, keepdims=True)
            mixed = jnp.einsum(
                "hqk,hkd->hqd", expo.astype(jnp.bfloat16), v3, preferred_element_type=jnp.float32
            ) / total
            for h in range(heads):
                mixed_s[m * rows:(m + 1) * rows, h * HEAD_DIM:(h + 1) * HEAD_DIM] = mixed[h].astype(jnp.bfloat16)

        copies[1].wait()
        for m in range(micro):
            res_s[m * rows:(m + 1) * rows, :] = hidden_s[m * span + own_at:(m + 1) * span, :] + jnp.dot(
                mixed_s[m * rows:(m + 1) * rows, :], mix_v[...], preferred_element_type=jnp.float32
            )
        residual = res_s[...]
        square = jnp.mean(residual * residual, axis=-1, keepdims=True)
        final_normed = (residual * lax.rsqrt(square + 1e-06) * gb_ref[...]).astype(jnp.bfloat16)
        raw = jnp.dot(final_normed, read_v[...], preferred_element_type=jnp.float32)
        shift_mean = raw[:, :width_in]
        log_scale = 0.5 * jnp.tanh(raw[:, width_in:])
        if mirrored:
            i = lax.broadcasted_iota(jnp.int32, (rows, rows), 0)
            c = lax.broadcasted_iota(jnp.int32, (rows, rows), 1)
            flip = (c == (rows - 1) - i).astype(jnp.bfloat16)
        for m in range(micro):
            own = own_ref[m]
            if mirrored:
                high = own.astype(jnp.bfloat16)
                rest = own - high.astype(jnp.float32)
                middle = rest.astype(jnp.bfloat16)
                low = (rest - middle.astype(jnp.float32)).astype(jnp.bfloat16)
                parts = [jnp.dot(flip, part, preferred_element_type=jnp.float32) for part in (high, middle, low)]
                own = (parts[0] + parts[1]) + parts[2]
            rows_m = slice(m * rows, (m + 1) * rows)
            result = (own - shift_mean[rows_m]) * jnp.exp(-log_scale[rows_m])
            out_ref[m] = jnp.where(keep_ref[0] > 0, result, prev_ref[m])
            outb_ref[m] = result.astype(jnp.bfloat16)

    width = heads_all
    flops = 2 * n_rows * (width_in * width + width * 2 * heads_all)
    flops += 2 * micro * rows * (width * heads_all + 2 * heads * span * HEAD_DIM + heads_all * width + width * 2 * width_in)
    weight_bytes = 2 * (width_in * width + width * 3 * heads_all + heads_all * width + width * 2 * width_in)
    vmem = pltpu.VMEM
    call = pl.pallas_call(
        kernel,
        out_shape=(
            jax.ShapeDtypeStruct((micro, rows, width_in), jnp.float32),
            jax.ShapeDtypeStruct((micro, rows, width_in), jnp.bfloat16),
        ),
        in_specs=[pl.BlockSpec(memory_space=pltpu.SMEM)] + [pl.BlockSpec(memory_space=vmem)] * 10
        + [pl.BlockSpec(memory_space=pl.ANY)] * 2,
        out_specs=(pl.BlockSpec(memory_space=vmem), pl.BlockSpec(memory_space=vmem)),
        scratch_shapes=[
            vmem((width, 3 * heads_all), jnp.bfloat16),
            vmem((heads_all, width), jnp.bfloat16),
            pltpu.SemaphoreType.DMA((2 + 2 * heads_all // CHUNK,)),
            vmem((n_in, width_in), jnp.bfloat16),
            vmem((n_rows, width_in), jnp.bfloat16),
            vmem((n_rows, width), jnp.float32),
            vmem((n_rows, width), jnp.bfloat16),
            vmem((micro * rows, heads_all), jnp.bfloat16),
            vmem((n_rows, 2 * heads_all), jnp.bfloat16),
            vmem((micro * rows, heads_all), jnp.bfloat16),
            vmem((micro * rows, width), jnp.float32),
        ],
        compiler_params=pltpu.CompilerParams(vmem_limit_bytes=56 * 1024 * 1024),
        cost_estimate=pl.CostEstimate(
            flops=flops,
            bytes_accessed=weight_bytes + n_rows * width_in * 2 + 2 * micro * rows * width_in * 4,
            transcendentals=micro * heads * rows * span + micro * rows * 2 * width_in,
        ),
    )
    return call


def rms_scaled(values, gain):
    return values * lax.rsqrt(jnp.mean(values * values, axis=-1, keepdims=True) + 1e-06) * gain


def body(
    patches,
    tile_list,
    input_weight,
    attention_weight,
    mixing_weight,
    output_weight,
    norm_gain,
    final_gain,
):
    micro, rows, width_in = patches.shape
    assert rows == TILE
    heads_all = mixing_weight.shape[1]
    head_count = heads_all // HEAD_DIM
    segment = lax.axis_index("segment")
    place = lax.axis_index("seq")
    n_seq = lax.axis_size("seq")
    n_seg = lax.axis_size("segment")
    tiles_all = tile_list.shape[0]
    span = (BACK + 1) * rows

    window_tiles = place - BACK + jnp.arange(BACK + 1, dtype=jnp.int32)
    my_list = lax.dynamic_index_in_dim(tile_list, place, 0, keepdims=False)
    listed = jnp.any(my_list[:, None] == window_tiles[None, :], axis=0) & (window_tiles >= 0)
    listed = jnp.repeat(listed, rows)
    query_pos = jnp.arange(rows, dtype=jnp.int32) + BACK * rows
    key_pos = jnp.arange(span, dtype=jnp.int32)
    allowed = listed[None, :] & (key_pos[None, :] <= query_pos[:, None])

    first_call = make_block_call(micro, rows, width_in, heads_all, False, jnp.float32)
    later_call = make_block_call(micro, rows, width_in, heads_all, True, jnp.bfloat16)
    mask = allowed.astype(jnp.float32)
    weights = (
        norm_gain[0].reshape(1, -1),
        final_gain[0].reshape(1, -1),
        input_weight[0],
        output_weight[0],
        attention_weight[0],
        mixing_weight[0],
    )

    axes = ("segment", "seq")

    def first_inputs():
        def behind(distance):
            pairs = [(q, q + distance) for q in range(n_seq) if q + distance < n_seq]
            return lax.ppermute(patches, axes, pairs)

        return patches, behind(1), behind(2), behind(BACK + 1)

    def next_inputs(result, result_low, turn):
        src = turn * n_seq
        dst = (turn + 1) * n_seq

        def send(block, offset):
            pairs = []
            for q in range(n_seq):
                target = n_seq - 1 - q + offset
                if 0 <= target < n_seq:
                    pairs.append((src + q, dst + target))
            return lax.ppermute(block, axes, pairs)

        return (
            send(result, 0),
            send(result_low, 1),
            send(result_low, 2),
            send(result_low, BACK + 1),
        )

    inputs = first_inputs()
    out = jnp.zeros((micro, rows, width_in), jnp.float32)
    for turn in range(n_seg):
        call = first_call if turn == 0 else later_call
        keep = (segment == turn).astype(jnp.int32).reshape(1)
        out, result_low = call(keep, out, *inputs, mask, *weights)
        if turn + 1 < n_seg:
            inputs = next_inputs(out, result_low, turn)
    return out[None]


def solution(mesh):
    in_specs = (
        P(None, "seq", None),
        P(),
        P("segment", None, None),
        P("segment", None, None),
        P("segment", None, None),
        P("segment", None, None),
        P("segment", None),
        P("segment", None),
    )
    out_specs = P("segment", None, "seq", None)
    return jax.shard_map(body, mesh=mesh, in_specs=in_specs, out_specs=out_specs, check_vma=False)
```

```python
import jax
import jax.numpy as jnp
from jax import lax
from jax.experimental import pallas as pl
from jax.experimental.pallas import tpu as pltpu
from jax.sharding import PartitionSpec as P

HEAD_DIM = 128
TILE = 128
BACK = 2

CHUNK = 1024


def make_block_call(micro, rows, width_in, heads_all, mirrored, piece_dtype):
    span = (BACK + 1) * rows
    own_at = BACK * rows
    n_rows = micro * span
    n_in = (BACK + 2) * rows
    scale = HEAD_DIM ** (-0.5)
    heads = heads_all // HEAD_DIM

    def kernel(keep_ref, prev_ref, own_ref, back1_ref, back2_ref, edge_ref, mask_ref, ga_ref, gb_ref,
               embed_v, read_v, attn_hbm, mix_hbm,
               out_ref, outb_ref,
               attn_v, mix_v, sems,
               pieces_s, shifted_s, hidden_s, normed_s, q_s, kv_s, mixed_s, res_s):
        n_kv = 2 * heads_all // CHUNK
        kv_copies = [
            pltpu.make_async_copy(
                attn_hbm.at[:, heads_all + j * CHUNK:heads_all + (j + 1) * CHUNK],
                attn_v.at[:, heads_all + j * CHUNK:heads_all + (j + 1) * CHUNK],
                sems.at[2 + j],
            )
            for j in range(n_kv)
        ]
        copies = [
            pltpu.make_async_copy(attn_hbm.at[:, :heads_all], attn_v.at[:, :heads_all], sems.at[0]),
            pltpu.make_async_copy(mix_hbm, mix_v, sems.at[1]),
        ]
        for copy in kv_copies:
            copy.start()
        for copy in copies:
            copy.start()
        before = lax.broadcasted_iota(jnp.int32, (span, n_in), 0) + (rows - 1)
        column = lax.broadcasted_iota(jnp.int32, (span, n_in), 1)
        if mirrored:
            source = ((before >> 7) << 7) + (rows - 1) - (before & (rows - 1))
        else:
            source = before
        select = (column == source).astype(jnp.bfloat16)
        for m in range(micro):
            pieces_s[0:rows, :] = edge_ref[m].astype(jnp.bfloat16)
            pieces_s[rows:2 * rows, :] = back2_ref[m].astype(jnp.bfloat16)
            pieces_s[2 * rows:3 * rows, :] = back1_ref[m].astype(jnp.bfloat16)
            pieces_s[3 * rows:4 * rows, :] = own_ref[m].astype(jnp.bfloat16)
            shifted_s[m * span:(m + 1) * span, :] = jnp.dot(
                select, pieces_s[...], preferred_element_type=jnp.float32
            ).astype(jnp.bfloat16)
        hidden = jnp.dot(shifted_s[...], embed_v[...], preferred_element_type=jnp.float32)
        hidden_s[...] = hidden
        square = jnp.mean(hidden * hidden, axis=-1, keepdims=True)
        normed_s[...] = (hidden * lax.rsqrt(square + 1e-06) * ga_ref[...]).astype(jnp.bfloat16)
        for j in range(n_kv):
            kv_copies[j].wait()
            kv_s[:, j * CHUNK:(j + 1) * CHUNK] = jnp.dot(
                normed_s[...], attn_v[:, heads_all + j * CHUNK:heads_all + (j + 1) * CHUNK],
                preferred_element_type=jnp.float32,
            ).astype(jnp.bfloat16)
        copies[0].wait()

        def q_step(j, carry):
            cols = pl.ds(pl.multiple_of(j * CHUNK, CHUNK), CHUNK)
            for m in range(micro):
                q_s[m * rows:(m + 1) * rows, cols] = jnp.dot(
                    normed_s[m * span + own_at:(m + 1) * span, :], attn_v[:, cols],
                    preferred_element_type=jnp.float32,
                ).astype(jnp.bfloat16)
            return carry

        lax.fori_loop(0, heads_all // CHUNK, q_step, 0)

        for m in range(micro):
            q3 = jnp.stack([q_s[m * rows:(m + 1) * rows, h * HEAD_DIM:(h + 1) * HEAD_DIM] for h in range(heads)])
            k3 = jnp.stack([kv_s[m * span:(m + 1) * span, h * HEAD_DIM:(h + 1) * HEAD_DIM] for h in range(heads)])
            v3 = jnp.stack([
                kv_s[m * span:(m + 1) * span, heads_all + h * HEAD_DIM:heads_all + (h + 1) * HEAD_DIM]
                for h in range(heads)
            ])
            scores = jnp.einsum("hqd,hkd->hqk", q3, k3, preferred_element_type=jnp.float32) * scale
            scores = jnp.where(mask_ref[...][None] > 0.5, scores, -jnp.inf)
            top = jnp.max(scores, axis=-1, keepdims=True)
            expo = jnp.exp(scores - top)
            total = jnp.sum(expo, axis=-1, keepdims=True)
            mixed = jnp.einsum(
                "hqk,hkd->hqd", expo.astype(jnp.bfloat16), v3, preferred_element_type=jnp.float32
            ) / total
            for h in range(heads):
                mixed_s[m * rows:(m + 1) * rows, h * HEAD_DIM:(h + 1) * HEAD_DIM] = mixed[h].astype(jnp.bfloat16)

        copies[1].wait()
        for m in range(micro):
            res_s[m * rows:(m + 1) * rows, :] = hidden_s[m * span + own_at:(m + 1) * span, :] + jnp.dot(
                mixed_s[m * rows:(m + 1) * rows, :], mix_v[...], preferred_element_type=jnp.float32
            )
        residual = res_s[...]
        square = jnp.mean(residual * residual, axis=-1, keepdims=True)
        final_normed = (residual * lax.rsqrt(square + 1e-06) * gb_ref[...]).astype(jnp.bfloat16)
        raw = jnp.dot(final_normed, read_v[...], preferred_element_type=jnp.float32)
        shift_mean = raw[:, :width_in]
        log_scale = 0.5 * jnp.tanh(raw[:, width_in:])
        if mirrored:
            i = lax.broadcasted_iota(jnp.int32, (rows, rows), 0)
            c = lax.broadcasted_iota(jnp.int32, (rows, rows), 1)
            flip = (c == (rows - 1) - i).astype(jnp.bfloat16)
        for m in range(micro):
            own = own_ref[m]
            if mirrored:
                high = own.astype(jnp.bfloat16)
                rest = own - high.astype(jnp.float32)
                middle = rest.astype(jnp.bfloat16)
                low = (rest - middle.astype(jnp.float32)).astype(jnp.bfloat16)
                parts = [jnp.dot(flip, part, preferred_element_type=jnp.float32) for part in (high, middle, low)]
                own = (parts[0] + parts[1]) + parts[2]
            rows_m = slice(m * rows, (m + 1) * rows)
            result = (own - shift_mean[rows_m]) * jnp.exp(-log_scale[rows_m])
            out_ref[m] = jnp.where(keep_ref[0] > 0, result, prev_ref[m])
            outb_ref[m] = result.astype(jnp.bfloat16)

    width = heads_all
    flops = 2 * n_rows * (width_in * width + width * 2 * heads_all)
    flops += 2 * micro * rows * (width * heads_all + 2 * heads * span * HEAD_DIM + heads_all * width + width * 2 * width_in)
    weight_bytes = 2 * (width_in * width + width * 3 * heads_all + heads_all * width + width * 2 * width_in)
    vmem = pltpu.VMEM
    call = pl.pallas_call(
        kernel,
        out_shape=(
            jax.ShapeDtypeStruct((micro, rows, width_in), jnp.float32),
            jax.ShapeDtypeStruct((micro, rows, width_in), jnp.bfloat16),
        ),
        in_specs=[pl.BlockSpec(memory_space=pltpu.SMEM)] + [pl.BlockSpec(memory_space=vmem)] * 10
        + [pl.BlockSpec(memory_space=pl.ANY)] * 2,
        out_specs=(pl.BlockSpec(memory_space=vmem), pl.BlockSpec(memory_space=vmem)),
        scratch_shapes=[
            vmem((width, 3 * heads_all), jnp.bfloat16),
            vmem((heads_all, width), jnp.bfloat16),
            pltpu.SemaphoreType.DMA((2 + 2 * heads_all // CHUNK,)),
            vmem((n_in, width_in), jnp.bfloat16),
            vmem((n_rows, width_in), jnp.bfloat16),
            vmem((n_rows, width), jnp.float32),
            vmem((n_rows, width), jnp.bfloat16),
            vmem((micro * rows, heads_all), jnp.bfloat16),
            vmem((n_rows, 2 * heads_all), jnp.bfloat16),
            vmem((micro * rows, heads_all), jnp.bfloat16),
            vmem((micro * rows, width), jnp.float32),
        ],
        compiler_params=pltpu.CompilerParams(vmem_limit_bytes=56 * 1024 * 1024),
        cost_estimate=pl.CostEstimate(
            flops=flops,
            bytes_accessed=weight_bytes + n_rows * width_in * 2 + 2 * micro * rows * width_in * 4,
            transcendentals=micro * heads * rows * span + micro * rows * 2 * width_in,
        ),
    )
    return call


def rms_scaled(values, gain):
    return values * lax.rsqrt(jnp.mean(values * values, axis=-1, keepdims=True) + 1e-06) * gain


def body(
    patches,
    tile_list,
    input_weight,
    attention_weight,
    mixing_weight,
    output_weight,
    norm_gain,
    final_gain,
):
    micro, rows, width_in = patches.shape
    assert rows == TILE
    heads_all = mixing_weight.shape[1]
    head_count = heads_all // HEAD_DIM
    segment = lax.axis_index("segment")
    place = lax.axis_index("seq")
    n_seq = lax.axis_size("seq")
    n_seg = lax.axis_size("segment")
    tiles_all = tile_list.shape[0]
    span = (BACK + 1) * rows

    window_tiles = place - BACK + jnp.arange(BACK + 1, dtype=jnp.int32)
    my_list = lax.dynamic_index_in_dim(tile_list, place, 0, keepdims=False)
    listed = jnp.any(my_list[:, None] == window_tiles[None, :], axis=0) & (window_tiles >= 0)
    listed = jnp.repeat(listed, rows)
    query_pos = jnp.arange(rows, dtype=jnp.int32) + BACK * rows
    key_pos = jnp.arange(span, dtype=jnp.int32)
    allowed = listed[None, :] & (key_pos[None, :] <= query_pos[:, None])

    first_call = make_block_call(micro, rows, width_in, heads_all, False, jnp.float32)
    later_call = make_block_call(micro, rows, width_in, heads_all, True, jnp.bfloat16)
    mask = allowed.astype(jnp.float32)
    weights = (
        norm_gain[0].reshape(1, -1),
        final_gain[0].reshape(1, -1),
        input_weight[0],
        output_weight[0],
        attention_weight[0],
        mixing_weight[0],
    )

    axes = ("segment", "seq")

    def first_inputs():
        def behind(distance):
            pairs = [(n_seq + q, q + distance) for q in range(n_seq) if q + distance < n_seq]
            return lax.ppermute(patches, axes, pairs)

        return patches, behind(1), behind(2), behind(BACK + 1)

    def next_inputs(result, result_low, turn):
        src = turn * n_seq
        dst = (turn + 1) * n_seq

        def send(block, offset):
            pairs = []
            for q in range(n_seq):
                target = n_seq - 1 - q + offset
                if 0 <= target < n_seq:
                    pairs.append((src + q, dst + target))
            return lax.ppermute(block, axes, pairs)

        return (
            send(result, 0),
            send(result_low, 1),
            send(result_low, 2),
            send(result_low, BACK + 1),
        )

    inputs = first_inputs()
    out = jnp.zeros((micro, rows, width_in), jnp.float32)
    for turn in range(n_seg):
        call = first_call if turn == 0 else later_call
        keep = (segment == turn).astype(jnp.int32).reshape(1)
        out, result_low = call(keep, out, *inputs, mask, *weights)
        if turn + 1 < n_seg:
            inputs = next_inputs(out, result_low, turn)
    return out[None]


def solution(mesh):
    in_specs = (
        P(None, "seq", None),
        P(),
        P("segment", None, None),
        P("segment", None, None),
        P("segment", None, None),
        P("segment", None, None),
        P("segment", None),
        P("segment", None),
    )
    out_specs = P("segment", None, "seq", None)
    return jax.shard_map(body, mesh=mesh, in_specs=in_specs, out_specs=out_specs, check_vma=False)
```

```python
import jax
import jax.numpy as jnp
from jax import lax
from jax.experimental import pallas as pl
from jax.experimental.pallas import tpu as pltpu
from jax.sharding import PartitionSpec as P

HEAD_DIM = 128
TILE = 128
BACK = 2

CHUNK = 1024


def make_block_call(micro, rows, width_in, heads_all, mirrored, piece_dtype):
    span = (BACK + 1) * rows
    own_at = BACK * rows
    n_rows = micro * span
    n_in = (BACK + 2) * rows
    scale = HEAD_DIM ** (-0.5)
    heads = heads_all // HEAD_DIM

    def kernel(keep_ref, prev_ref, own_ref, back1_ref, back2_ref, edge_ref, mask_ref, ga_ref, gb_ref,
               embed_v, read_v, attn_hbm, mix_hbm,
               out_ref, outb_ref,
               attn_v, mix_v, sems,
               pieces_s, shifted_s, hidden_s, normed_s, q_s, kv_s, mixed_s, res_s):
        n_kv = 2 * heads_all // CHUNK
        kv_copies = [
            pltpu.make_async_copy(
                attn_hbm.at[:, heads_all + j * CHUNK:heads_all + (j + 1) * CHUNK],
                attn_v.at[:, heads_all + j * CHUNK:heads_all + (j + 1) * CHUNK],
                sems.at[2 + j],
            )
            for j in range(n_kv)
        ]
        copies = [
            pltpu.make_async_copy(attn_hbm.at[:, :heads_all], attn_v.at[:, :heads_all], sems.at[0]),
            pltpu.make_async_copy(mix_hbm, mix_v, sems.at[1]),
        ]
        for copy in kv_copies:
            copy.start()
        for copy in copies:
            copy.start()
        before = lax.broadcasted_iota(jnp.int32, (span, n_in), 0) + (rows - 1)
        column = lax.broadcasted_iota(jnp.int32, (span, n_in), 1)
        if mirrored:
            source = ((before >> 7) << 7) + (rows - 1) - (before & (rows - 1))
        else:
            source = before
        select = (column == source).astype(jnp.bfloat16)
        for m in range(micro):
            pieces_s[0:rows, :] = edge_ref[m].astype(jnp.bfloat16)
            pieces_s[rows:2 * rows, :] = back2_ref[m].astype(jnp.bfloat16)
            pieces_s[2 * rows:3 * rows, :] = back1_ref[m].astype(jnp.bfloat16)
            pieces_s[3 * rows:4 * rows, :] = own_ref[m].astype(jnp.bfloat16)
            shifted_s[m * span:(m + 1) * span, :] = jnp.dot(
                select, pieces_s[...], preferred_element_type=jnp.float32
            ).astype(jnp.bfloat16)
        hidden = jnp.dot(shifted_s[...], embed_v[...], preferred_element_type=jnp.float32)
        hidden_s[...] = hidden
        square = jnp.mean(hidden * hidden, axis=-1, keepdims=True)
        normed_s[...] = (hidden * lax.rsqrt(square + 1e-06) * ga_ref[...]).astype(jnp.bfloat16)
        for j in range(n_kv):
            kv_copies[j].wait()
            kv_s[:, j * CHUNK:(j + 1) * CHUNK] = jnp.dot(
                normed_s[...], attn_v[:, heads_all + j * CHUNK:heads_all + (j + 1) * CHUNK],
                preferred_element_type=jnp.float32,
            ).astype(jnp.bfloat16)
        copies[0].wait()

        def q_step(j, carry):
            cols = pl.ds(pl.multiple_of(j * CHUNK, CHUNK), CHUNK)
            for m in range(micro):
                q_s[m * rows:(m + 1) * rows, cols] = jnp.dot(
                    normed_s[m * span + own_at:(m + 1) * span, :], attn_v[:, cols],
                    preferred_element_type=jnp.float32,
                ).astype(jnp.bfloat16)
            return carry

        lax.fori_loop(0, heads_all // CHUNK, q_step, 0)

        for m in range(micro):
            q3 = jnp.stack([q_s[m * rows:(m + 1) * rows, h * HEAD_DIM:(h + 1) * HEAD_DIM] for h in range(heads)])
            k3 = jnp.stack([kv_s[m * span:(m + 1) * span, h * HEAD_DIM:(h + 1) * HEAD_DIM] for h in range(heads)])
            v3 = jnp.stack([
                kv_s[m * span:(m + 1) * span, heads_all + h * HEAD_DIM:heads_all + (h + 1) * HEAD_DIM]
                for h in range(heads)
            ])
            scores = jnp.einsum("hqd,hkd->hqk", q3, k3, preferred_element_type=jnp.float32) * scale
            scores = jnp.where(mask_ref[...][None] > 0.5, scores, -jnp.inf)
            top = jnp.max(scores, axis=-1, keepdims=True)
            expo = jnp.exp(scores - top)
            total = jnp.sum(expo, axis=-1, keepdims=True)
            mixed = jnp.einsum(
                "hqk,hkd->hqd", expo.astype(jnp.bfloat16), v3, preferred_element_type=jnp.float32
            ) / total
            for h in range(heads):
                mixed_s[m * rows:(m + 1) * rows, h * HEAD_DIM:(h + 1) * HEAD_DIM] = mixed[h].astype(jnp.bfloat16)

        copies[1].wait()
        for m in range(micro):
            res_s[m * rows:(m + 1) * rows, :] = hidden_s[m * span + own_at:(m + 1) * span, :] + jnp.dot(
                mixed_s[m * rows:(m + 1) * rows, :], mix_v[...], preferred_element_type=jnp.float32
            )
        residual = res_s[...]
        square = jnp.mean(residual * residual, axis=-1, keepdims=True)
        final_normed = (residual * lax.rsqrt(square + 1e-06) * gb_ref[...]).astype(jnp.bfloat16)
        raw = jnp.dot(final_normed, read_v[...], preferred_element_type=jnp.float32)
        shift_mean = raw[:, :width_in]
        log_scale = 0.5 * jnp.tanh(raw[:, width_in:])
        if mirrored:
            i = lax.broadcasted_iota(jnp.int32, (rows, rows), 0)
            c = lax.broadcasted_iota(jnp.int32, (rows, rows), 1)
            flip = (c == (rows - 1) - i).astype(jnp.bfloat16)
        for m in range(micro):
            own = own_ref[m]
            if mirrored:
                high = own.astype(jnp.bfloat16)
                rest = own - high.astype(jnp.float32)
                middle = rest.astype(jnp.bfloat16)
                low = (rest - middle.astype(jnp.float32)).astype(jnp.bfloat16)
                parts = [jnp.dot(flip, part, preferred_element_type=jnp.float32) for part in (high, middle, low)]
                own = (parts[0] + parts[1]) + parts[2]
            rows_m = slice(m * rows, (m + 1) * rows)
            result = (own - shift_mean[rows_m]) * jnp.exp(-log_scale[rows_m])
            out_ref[m] = jnp.where(keep_ref[0] > 0, result, prev_ref[m])
            outb_ref[m] = result.astype(jnp.bfloat16)

    width = heads_all
    flops = 2 * n_rows * (width_in * width + width * 2 * heads_all)
    flops += 2 * micro * rows * (width * heads_all + 2 * heads * span * HEAD_DIM + heads_all * width + width * 2 * width_in)
    weight_bytes = 2 * (width_in * width + width * 3 * heads_all + heads_all * width + width * 2 * width_in)
    vmem = pltpu.VMEM
    call = pl.pallas_call(
        kernel,
        out_shape=(
            jax.ShapeDtypeStruct((micro, rows, width_in), jnp.float32),
            jax.ShapeDtypeStruct((micro, rows, width_in), jnp.bfloat16),
        ),
        in_specs=[pl.BlockSpec(memory_space=pltpu.SMEM)] + [pl.BlockSpec(memory_space=vmem)] * 10
        + [pl.BlockSpec(memory_space=pl.ANY)] * 2,
        out_specs=(pl.BlockSpec(memory_space=vmem), pl.BlockSpec(memory_space=vmem)),
        scratch_shapes=[
            vmem((width, 3 * heads_all), jnp.bfloat16),
            vmem((heads_all, width), jnp.bfloat16),
            pltpu.SemaphoreType.DMA((2 + 2 * heads_all // CHUNK,)),
            vmem((n_in, width_in), jnp.bfloat16),
            vmem((n_rows, width_in), jnp.bfloat16),
            vmem((n_rows, width), jnp.float32),
            vmem((n_rows, width), jnp.bfloat16),
            vmem((micro * rows, heads_all), jnp.bfloat16),
            vmem((n_rows, 2 * heads_all), jnp.bfloat16),
            vmem((micro * rows, heads_all), jnp.bfloat16),
            vmem((micro * rows, width), jnp.float32),
        ],
        compiler_params=pltpu.CompilerParams(vmem_limit_bytes=56 * 1024 * 1024),
        cost_estimate=pl.CostEstimate(
            flops=flops,
            bytes_accessed=weight_bytes + n_rows * width_in * 2 + 2 * micro * rows * width_in * 4,
            transcendentals=micro * heads * rows * span + micro * rows * 2 * width_in,
        ),
    )
    return call


def rms_scaled(values, gain):
    return values * lax.rsqrt(jnp.mean(values * values, axis=-1, keepdims=True) + 1e-06) * gain


def body(
    patches,
    tile_list,
    input_weight,
    attention_weight,
    mixing_weight,
    output_weight,
    norm_gain,
    final_gain,
):
    micro, rows, width_in = patches.shape
    assert rows == TILE
    heads_all = mixing_weight.shape[1]
    head_count = heads_all // HEAD_DIM
    segment = lax.axis_index("segment")
    place = lax.axis_index("seq")
    n_seq = lax.axis_size("seq")
    n_seg = lax.axis_size("segment")
    tiles_all = tile_list.shape[0]
    span = (BACK + 1) * rows

    window_tiles = place - BACK + jnp.arange(BACK + 1, dtype=jnp.int32)
    my_list = lax.dynamic_index_in_dim(tile_list, place, 0, keepdims=False)
    listed = jnp.any(my_list[:, None] == window_tiles[None, :], axis=0) & (window_tiles >= 0)
    listed = jnp.repeat(listed, rows)
    query_pos = jnp.arange(rows, dtype=jnp.int32) + BACK * rows
    key_pos = jnp.arange(span, dtype=jnp.int32)
    allowed = listed[None, :] & (key_pos[None, :] <= query_pos[:, None])

    first_call = make_block_call(micro, rows, width_in, heads_all, False, jnp.float32)
    later_call = make_block_call(micro, rows, width_in, heads_all, True, jnp.bfloat16)
    mask = allowed.astype(jnp.float32)
    weights = (
        norm_gain[0].reshape(1, -1),
        final_gain[0].reshape(1, -1),
        input_weight[0],
        output_weight[0],
        attention_weight[0],
        mixing_weight[0],
    )

    axes = ("segment", "seq")

    def first_inputs():
        def behind(distance):
            source = (n_seg - 1) * n_seq
            pairs = [(source + q, q + distance) for q in range(n_seq) if q + distance < n_seq]
            return lax.ppermute(patches, axes, pairs)

        return patches, behind(1), behind(2), behind(BACK + 1)

    def next_inputs(result, result_low, turn):
        src = turn * n_seq
        dst = (turn + 1) * n_seq

        def send(block, offset):
            pairs = []
            for q in range(n_seq):
                target = n_seq - 1 - q + offset
                if 0 <= target < n_seq:
                    pairs.append((src + q, dst + target))
            return lax.ppermute(block, axes, pairs)

        return (
            send(result, 0),
            send(result_low, 1),
            send(result_low, 2),
            send(result_low, BACK + 1),
        )

    inputs = first_inputs()
    out = jnp.zeros((micro, rows, width_in), jnp.float32)
    for turn in range(n_seg):
        call = first_call if turn == 0 else later_call
        keep = (segment == turn).astype(jnp.int32).reshape(1)
        out, result_low = call(keep, out, *inputs, mask, *weights)
        if turn + 1 < n_seg:
            inputs = next_inputs(out, result_low, turn)
    return out[None]


def solution(mesh):
    in_specs = (
        P(None, "seq", None),
        P(),
        P("segment", None, None),
        P("segment", None, None),
        P("segment", None, None),
        P("segment", None, None),
        P("segment", None),
        P("segment", None),
    )
    out_specs = P("segment", None, "seq", None)
    return jax.shard_map(body, mesh=mesh, in_specs=in_specs, out_specs=out_specs, check_vma=False)
```

```python
import jax
import jax.numpy as jnp
from jax import lax
from jax.experimental import pallas as pl
from jax.experimental.pallas import tpu as pltpu
from jax.sharding import PartitionSpec as P

HEAD_DIM = 128
TILE = 128
BACK = 2

CHUNK = 1024


def make_block_call(micro, rows, width_in, heads_all, mirrored, piece_dtype):
    span = (BACK + 1) * rows
    own_at = BACK * rows
    n_rows = micro * span
    n_in = (BACK + 2) * rows
    scale = HEAD_DIM ** (-0.5)
    heads = heads_all // HEAD_DIM

    def kernel(keep_ref, prev_ref, own_ref, back1_ref, back2_ref, edge_ref, mask_ref, ga_ref, gb_ref,
               embed_v, read_v, attn_hbm, mix_hbm,
               out_ref, outb_ref,
               attn_v, mix_v, sems,
               pieces_s, shifted_s, hidden_s, normed_s, q_s, kv_s, mixed_s, res_s):
        n_kv = 2 * heads_all // CHUNK
        kv_copies = [
            pltpu.make_async_copy(
                attn_hbm.at[:, heads_all + j * CHUNK:heads_all + (j + 1) * CHUNK],
                attn_v.at[:, heads_all + j * CHUNK:heads_all + (j + 1) * CHUNK],
                sems.at[2 + j],
            )
            for j in range(n_kv)
        ]
        copies = [
            pltpu.make_async_copy(attn_hbm.at[:, :heads_all], attn_v.at[:, :heads_all], sems.at[0]),
            pltpu.make_async_copy(mix_hbm, mix_v, sems.at[1]),
        ]
        for copy in kv_copies:
            copy.start()
        for copy in copies:
            copy.start()
        before = lax.broadcasted_iota(jnp.int32, (span, n_in), 0) + (rows - 1)
        column = lax.broadcasted_iota(jnp.int32, (span, n_in), 1)
        if mirrored:
            source = ((before >> 7) << 7) + (rows - 1) - (before & (rows - 1))
        else:
            source = before
        select = (column == source).astype(jnp.bfloat16)
        for m in range(micro):
            pieces_s[0:rows, :] = edge_ref[m].astype(jnp.bfloat16)
            pieces_s[rows:2 * rows, :] = back2_ref[m].astype(jnp.bfloat16)
            pieces_s[2 * rows:3 * rows, :] = back1_ref[m].astype(jnp.bfloat16)
            pieces_s[3 * rows:4 * rows, :] = own_ref[m].astype(jnp.bfloat16)
            shifted_s[m * span:(m + 1) * span, :] = jnp.dot(
                select, pieces_s[...], preferred_element_type=jnp.float32
            ).astype(jnp.bfloat16)
        hidden = jnp.dot(shifted_s[...], embed_v[...], preferred_element_type=jnp.float32)
        hidden_s[...] = hidden
        square = jnp.mean(hidden * hidden, axis=-1, keepdims=True)
        normed_s[...] = (hidden * lax.rsqrt(square + 1e-06) * ga_ref[...]).astype(jnp.bfloat16)
        for j in range(n_kv):
            kv_copies[j].wait()
            kv_s[:, j * CHUNK:(j + 1) * CHUNK] = jnp.dot(
                normed_s[...], attn_v[:, heads_all + j * CHUNK:heads_all + (j + 1) * CHUNK],
                preferred_element_type=jnp.float32,
            ).astype(jnp.bfloat16)
        copies[0].wait()

        def q_step(j, carry):
            cols = pl.ds(pl.multiple_of(j * CHUNK, CHUNK), CHUNK)
            for m in range(micro):
                q_s[m * rows:(m + 1) * rows, cols] = jnp.dot(
                    normed_s[m * span + own_at:(m + 1) * span, :], attn_v[:, cols],
                    preferred_element_type=jnp.float32,
                ).astype(jnp.bfloat16)
            return carry

        lax.fori_loop(0, heads_all // CHUNK, q_step, 0)

        for m in range(micro):
            q3 = jnp.stack([q_s[m * rows:(m + 1) * rows, h * HEAD_DIM:(h + 1) * HEAD_DIM] for h in range(heads)])
            k3 = jnp.stack([kv_s[m * span:(m + 1) * span, h * HEAD_DIM:(h + 1) * HEAD_DIM] for h in range(heads)])
            v3 = jnp.stack([
                kv_s[m * span:(m + 1) * span, heads_all + h * HEAD_DIM:heads_all + (h + 1) * HEAD_DIM]
                for h in range(heads)
            ])
            scores = jnp.einsum("hqd,hkd->hqk", q3, k3, preferred_element_type=jnp.float32) * scale
            scores = jnp.where(mask_ref[...][None] > 0.5, scores, -jnp.inf)
            top = jnp.max(scores, axis=-1, keepdims=True)
            expo = jnp.exp(scores - top)
            total = jnp.sum(expo, axis=-1, keepdims=True)
            mixed = jnp.einsum(
                "hqk,hkd->hqd", expo.astype(jnp.bfloat16), v3, preferred_element_type=jnp.float32
            ) / total
            for h in range(heads):
                mixed_s[m * rows:(m + 1) * rows, h * HEAD_DIM:(h + 1) * HEAD_DIM] = mixed[h].astype(jnp.bfloat16)

        copies[1].wait()
        for m in range(micro):
            res_s[m * rows:(m + 1) * rows, :] = hidden_s[m * span + own_at:(m + 1) * span, :] + jnp.dot(
                mixed_s[m * rows:(m + 1) * rows, :], mix_v[...], preferred_element_type=jnp.float32
            )
        residual = res_s[...]
        square = jnp.mean(residual * residual, axis=-1, keepdims=True)
        final_normed = (residual * lax.rsqrt(square + 1e-06) * gb_ref[...]).astype(jnp.bfloat16)
        raw = jnp.dot(final_normed, read_v[...], preferred_element_type=jnp.float32)
        shift_mean = raw[:, :width_in]
        log_scale = 0.5 * jnp.tanh(raw[:, width_in:])
        if mirrored:
            i = lax.broadcasted_iota(jnp.int32, (rows, rows), 0)
            c = lax.broadcasted_iota(jnp.int32, (rows, rows), 1)
            flip = (c == (rows - 1) - i).astype(jnp.bfloat16)
        for m in range(micro):
            own = own_ref[m]
            if mirrored:
                high = own.astype(jnp.bfloat16)
                rest = own - high.astype(jnp.float32)
                middle = rest.astype(jnp.bfloat16)
                low = (rest - middle.astype(jnp.float32)).astype(jnp.bfloat16)
                parts = [jnp.dot(flip, part, preferred_element_type=jnp.float32) for part in (high, middle, low)]
                own = (parts[0] + parts[1]) + parts[2]
            rows_m = slice(m * rows, (m + 1) * rows)
            result = (own - shift_mean[rows_m]) * jnp.exp(-log_scale[rows_m])
            out_ref[m] = jnp.where(keep_ref[0] > 0, result, prev_ref[m])
            outb_ref[m] = result.astype(jnp.bfloat16)

    width = heads_all
    flops = 2 * n_rows * (width_in * width + width * 2 * heads_all)
    flops += 2 * micro * rows * (width * heads_all + 2 * heads * span * HEAD_DIM + heads_all * width + width * 2 * width_in)
    weight_bytes = 2 * (width_in * width + width * 3 * heads_all + heads_all * width + width * 2 * width_in)
    vmem = pltpu.VMEM
    call = pl.pallas_call(
        kernel,
        out_shape=(
            jax.ShapeDtypeStruct((micro, rows, width_in), jnp.float32),
            jax.ShapeDtypeStruct((micro, rows, width_in), jnp.bfloat16),
        ),
        in_specs=[pl.BlockSpec(memory_space=pltpu.SMEM)] + [pl.BlockSpec(memory_space=vmem)] * 10
        + [pl.BlockSpec(memory_space=pl.ANY)] * 2,
        out_specs=(pl.BlockSpec(memory_space=vmem), pl.BlockSpec(memory_space=vmem)),
        scratch_shapes=[
            vmem((width, 3 * heads_all), jnp.bfloat16),
            vmem((heads_all, width), jnp.bfloat16),
            pltpu.SemaphoreType.DMA((2 + 2 * heads_all // CHUNK,)),
            vmem((n_in, width_in), jnp.bfloat16),
            vmem((n_rows, width_in), jnp.bfloat16),
            vmem((n_rows, width), jnp.float32),
            vmem((n_rows, width), jnp.bfloat16),
            vmem((micro * rows, heads_all), jnp.bfloat16),
            vmem((n_rows, 2 * heads_all), jnp.bfloat16),
            vmem((micro * rows, heads_all), jnp.bfloat16),
            vmem((micro * rows, width), jnp.float32),
        ],
        compiler_params=pltpu.CompilerParams(vmem_limit_bytes=56 * 1024 * 1024),
        cost_estimate=pl.CostEstimate(
            flops=flops,
            bytes_accessed=weight_bytes + n_rows * width_in * 2 + 2 * micro * rows * width_in * 4,
            transcendentals=micro * heads * rows * span + micro * rows * 2 * width_in,
        ),
    )
    return call


def rms_scaled(values, gain):
    return values * lax.rsqrt(jnp.mean(values * values, axis=-1, keepdims=True) + 1e-06) * gain


def body(
    patches,
    tile_list,
    input_weight,
    attention_weight,
    mixing_weight,
    output_weight,
    norm_gain,
    final_gain,
):
    micro, rows, width_in = patches.shape
    assert rows == TILE
    heads_all = mixing_weight.shape[1]
    head_count = heads_all // HEAD_DIM
    segment = lax.axis_index("segment")
    place = lax.axis_index("seq")
    n_seq = lax.axis_size("seq")
    n_seg = lax.axis_size("segment")
    tiles_all = tile_list.shape[0]
    span = (BACK + 1) * rows

    window_tiles = place - BACK + jnp.arange(BACK + 1, dtype=jnp.int32)
    my_list = lax.dynamic_index_in_dim(tile_list, place, 0, keepdims=False)
    listed = jnp.any(my_list[:, None] == window_tiles[None, :], axis=0) & (window_tiles >= 0)
    listed = jnp.repeat(listed, rows)
    query_pos = jnp.arange(rows, dtype=jnp.int32) + BACK * rows
    key_pos = jnp.arange(span, dtype=jnp.int32)
    allowed = listed[None, :] & (key_pos[None, :] <= query_pos[:, None])

    first_call = make_block_call(micro, rows, width_in, heads_all, False, jnp.bfloat16)
    later_call = make_block_call(micro, rows, width_in, heads_all, True, jnp.bfloat16)
    mask = allowed.astype(jnp.float32)
    weights = (
        norm_gain[0].reshape(1, -1),
        final_gain[0].reshape(1, -1),
        input_weight[0],
        output_weight[0],
        attention_weight[0],
        mixing_weight[0],
    )

    axes = ("segment", "seq")

    def first_inputs():
        def behind(distance):
            source = (n_seg - 1) * n_seq
            pairs = [(source + q, q + distance) for q in range(n_seq) if q + distance < n_seq]
            return lax.ppermute(patches_low, axes, pairs)

        patches_low = patches.astype(jnp.bfloat16)
        return patches, behind(1), behind(2), behind(BACK + 1)

    def next_inputs(result, result_low, turn):
        src = turn * n_seq
        dst = (turn + 1) * n_seq

        def send(block, offset):
            pairs = []
            for q in range(n_seq):
                target = n_seq - 1 - q + offset
                if 0 <= target < n_seq:
                    pairs.append((src + q, dst + target))
            return lax.ppermute(block, axes, pairs)

        return (
            send(result, 0),
            send(result_low, 1),
            send(result_low, 2),
            send(result_low, BACK + 1),
        )

    inputs = first_inputs()
    out = jnp.zeros((micro, rows, width_in), jnp.float32)
    for turn in range(n_seg):
        call = first_call if turn == 0 else later_call
        keep = (segment == turn).astype(jnp.int32).reshape(1)
        out, result_low = call(keep, out, *inputs, mask, *weights)
        if turn + 1 < n_seg:
            inputs = next_inputs(out, result_low, turn)
    return out[None]


def solution(mesh):
    in_specs = (
        P(None, "seq", None),
        P(),
        P("segment", None, None),
        P("segment", None, None),
        P("segment", None, None),
        P("segment", None, None),
        P("segment", None),
        P("segment", None),
    )
    out_specs = P("segment", None, "seq", None)
    return jax.shard_map(body, mesh=mesh, in_specs=in_specs, out_specs=out_specs, check_vma=False)
```

```python
import jax
import jax.numpy as jnp
from jax import lax
from jax.experimental import pallas as pl
from jax.experimental.pallas import tpu as pltpu
from jax.sharding import PartitionSpec as P

HEAD_DIM = 128
TILE = 128
BACK = 2

CHUNK = 1024


def make_block_call(micro, rows, width_in, heads_all, mirrored, piece_dtype):
    span = (BACK + 1) * rows
    own_at = BACK * rows
    n_rows = micro * span
    n_in = (BACK + 2) * rows
    scale = HEAD_DIM ** (-0.5)
    heads = heads_all // HEAD_DIM

    def kernel(keep_ref, prev_ref, own_ref, back1_ref, back2_ref, edge_ref, mask_ref, ga_ref, gb_ref,
               embed_v, read_v, attn_hbm, mix_hbm,
               out_ref, outb_ref,
               attn_v, mix_v, sems,
               pieces_s, shifted_s, hidden_s, normed_s, q_s, kv_s, mixed_s, res_s):
        n_kv = 2 * heads_all // CHUNK
        kv_copies = [
            pltpu.make_async_copy(
                attn_hbm.at[:, heads_all + j * CHUNK:heads_all + (j + 1) * CHUNK],
                attn_v.at[:, heads_all + j * CHUNK:heads_all + (j + 1) * CHUNK],
                sems.at[2 + j],
            )
            for j in range(n_kv)
        ]
        copies = [
            pltpu.make_async_copy(attn_hbm.at[:, :heads_all], attn_v.at[:, :heads_all], sems.at[0]),
            pltpu.make_async_copy(mix_hbm, mix_v, sems.at[1]),
        ]
        for copy in kv_copies:
            copy.start()
        for copy in copies:
            copy.start()
        before = lax.broadcasted_iota(jnp.int32, (span, n_in), 0) + (rows - 1)
        column = lax.broadcasted_iota(jnp.int32, (span, n_in), 1)
        if mirrored:
            source = ((before >> 7) << 7) + (rows - 1) - (before & (rows - 1))
        else:
            source = before
        select = (column == source).astype(jnp.bfloat16)
        for m in range(micro):
            pieces_s[0:rows, :] = edge_ref[m].astype(jnp.bfloat16)
            pieces_s[rows:2 * rows, :] = back2_ref[m].astype(jnp.bfloat16)
            pieces_s[2 * rows:3 * rows, :] = back1_ref[m].astype(jnp.bfloat16)
            pieces_s[3 * rows:4 * rows, :] = own_ref[m].astype(jnp.bfloat16)
            shifted_s[m * span:(m + 1) * span, :] = jnp.dot(
                select, pieces_s[...], preferred_element_type=jnp.float32
            ).astype(jnp.bfloat16)
        hidden = jnp.dot(shifted_s[...], embed_v[...], preferred_element_type=jnp.float32)
        hidden_s[...] = hidden
        square = jnp.mean(hidden * hidden, axis=-1, keepdims=True)
        normed_s[...] = (hidden * lax.rsqrt(square + 1e-06) * ga_ref[...]).astype(jnp.bfloat16)
        for j in range(n_kv):
            kv_copies[j].wait()
            kv_s[:, j * CHUNK:(j + 1) * CHUNK] = jnp.dot(
                normed_s[...], attn_v[:, heads_all + j * CHUNK:heads_all + (j + 1) * CHUNK],
                preferred_element_type=jnp.float32,
            ).astype(jnp.bfloat16)
        copies[0].wait()

        def q_step(j, carry):
            cols = pl.ds(pl.multiple_of(j * CHUNK, CHUNK), CHUNK)
            for m in range(micro):
                q_s[m * rows:(m + 1) * rows, cols] = jnp.dot(
                    normed_s[m * span + own_at:(m + 1) * span, :], attn_v[:, cols],
                    preferred_element_type=jnp.float32,
                ).astype(jnp.bfloat16)
            return carry

        lax.fori_loop(0, heads_all // CHUNK, q_step, 0)

        for m in range(micro):
            q3 = jnp.stack([q_s[m * rows:(m + 1) * rows, h * HEAD_DIM:(h + 1) * HEAD_DIM] for h in range(heads)])
            k3 = jnp.stack([kv_s[m * span:(m + 1) * span, h * HEAD_DIM:(h + 1) * HEAD_DIM] for h in range(heads)])
            v3 = jnp.stack([
                kv_s[m * span:(m + 1) * span, heads_all + h * HEAD_DIM:heads_all + (h + 1) * HEAD_DIM]
                for h in range(heads)
            ])
            scores = jnp.einsum("hqd,hkd->hqk", q3, k3, preferred_element_type=jnp.float32) * scale
            scores = jnp.where(mask_ref[...][None] > 0.5, scores, -jnp.inf)
            top = jnp.max(scores, axis=-1, keepdims=True)
            expo = jnp.exp(scores - top)
            total = jnp.sum(expo, axis=-1, keepdims=True)
            mixed = jnp.einsum(
                "hqk,hkd->hqd", expo.astype(jnp.bfloat16), v3, preferred_element_type=jnp.float32
            ) / total
            for h in range(heads):
                mixed_s[m * rows:(m + 1) * rows, h * HEAD_DIM:(h + 1) * HEAD_DIM] = mixed[h].astype(jnp.bfloat16)

        copies[1].wait()
        for m in range(micro):
            res_s[m * rows:(m + 1) * rows, :] = hidden_s[m * span + own_at:(m + 1) * span, :] + jnp.dot(
                mixed_s[m * rows:(m + 1) * rows, :], mix_v[...], preferred_element_type=jnp.float32
            )
        residual = res_s[...]
        square = jnp.mean(residual * residual, axis=-1, keepdims=True)
        final_normed = (residual * lax.rsqrt(square + 1e-06) * gb_ref[...]).astype(jnp.bfloat16)
        raw = jnp.dot(final_normed, read_v[...], preferred_element_type=jnp.float32)
        shift_mean = raw[:, :width_in]
        log_scale = 0.5 * jnp.tanh(raw[:, width_in:])
        if mirrored:
            i = lax.broadcasted_iota(jnp.int32, (rows, rows), 0)
            c = lax.broadcasted_iota(jnp.int32, (rows, rows), 1)
            flip = (c == (rows - 1) - i).astype(jnp.bfloat16)
        for m in range(micro):
            own = own_ref[m]
            if mirrored:
                high = own.astype(jnp.bfloat16)
                rest = own - high.astype(jnp.float32)
                middle = rest.astype(jnp.bfloat16)
                low = (rest - middle.astype(jnp.float32)).astype(jnp.bfloat16)
                parts = [jnp.dot(flip, part, preferred_element_type=jnp.float32) for part in (high, middle, low)]
                own = (parts[0] + parts[1]) + parts[2]
            rows_m = slice(m * rows, (m + 1) * rows)
            result = (own - shift_mean[rows_m]) * jnp.exp(-log_scale[rows_m])
            out_ref[m] = jnp.where(keep_ref[0] > 0, result, prev_ref[m])
            outb_ref[m] = result.astype(jnp.bfloat16)

    width = heads_all
    flops = 2 * n_rows * (width_in * width + width * 2 * heads_all)
    flops += 2 * micro * rows * (width * heads_all + 2 * heads * span * HEAD_DIM + heads_all * width + width * 2 * width_in)
    weight_bytes = 2 * (width_in * width + width * 3 * heads_all + heads_all * width + width * 2 * width_in)
    vmem = pltpu.VMEM
    call = pl.pallas_call(
        kernel,
        out_shape=(
            jax.ShapeDtypeStruct((micro, rows, width_in), jnp.float32),
            jax.ShapeDtypeStruct((micro, rows, width_in), jnp.bfloat16),
        ),
        in_specs=[pl.BlockSpec(memory_space=pltpu.SMEM)] + [pl.BlockSpec(memory_space=vmem)] * 10
        + [pl.BlockSpec(memory_space=pl.ANY)] * 2,
        out_specs=(pl.BlockSpec(memory_space=vmem), pl.BlockSpec(memory_space=vmem)),
        scratch_shapes=[
            vmem((width, 3 * heads_all), jnp.bfloat16),
            vmem((heads_all, width), jnp.bfloat16),
            pltpu.SemaphoreType.DMA((2 + 2 * heads_all // CHUNK,)),
            vmem((n_in, width_in), jnp.bfloat16),
            vmem((n_rows, width_in), jnp.bfloat16),
            vmem((n_rows, width), jnp.float32),
            vmem((n_rows, width), jnp.bfloat16),
            vmem((micro * rows, heads_all), jnp.bfloat16),
            vmem((n_rows, 2 * heads_all), jnp.bfloat16),
            vmem((micro * rows, heads_all), jnp.bfloat16),
            vmem((micro * rows, width), jnp.float32),
        ],
        compiler_params=pltpu.CompilerParams(vmem_limit_bytes=56 * 1024 * 1024),
        cost_estimate=pl.CostEstimate(
            flops=flops,
            bytes_accessed=weight_bytes + n_rows * width_in * 2 + 2 * micro * rows * width_in * 4,
            transcendentals=micro * heads * rows * span + micro * rows * 2 * width_in,
        ),
    )
    return call


def rms_scaled(values, gain):
    return values * lax.rsqrt(jnp.mean(values * values, axis=-1, keepdims=True) + 1e-06) * gain


def body(
    patches,
    tile_list,
    input_weight,
    attention_weight,
    mixing_weight,
    output_weight,
    norm_gain,
    final_gain,
):
    micro, rows, width_in = patches.shape
    assert rows == TILE
    heads_all = mixing_weight.shape[1]
    head_count = heads_all // HEAD_DIM
    segment = lax.axis_index("segment")
    place = lax.axis_index("seq")
    n_seq = lax.axis_size("seq")
    n_seg = lax.axis_size("segment")
    tiles_all = tile_list.shape[0]
    span = (BACK + 1) * rows

    window_tiles = place - BACK + jnp.arange(BACK + 1, dtype=jnp.int32)
    my_list = lax.dynamic_index_in_dim(tile_list, place, 0, keepdims=False)
    listed = jnp.any(my_list[:, None] == window_tiles[None, :], axis=0) & (window_tiles >= 0)
    listed = jnp.repeat(listed, rows)
    query_pos = jnp.arange(rows, dtype=jnp.int32) + BACK * rows
    key_pos = jnp.arange(span, dtype=jnp.int32)
    allowed = listed[None, :] & (key_pos[None, :] <= query_pos[:, None])

    first_call = make_block_call(micro, rows, width_in, heads_all, False, jnp.bfloat16)
    later_call = make_block_call(micro, rows, width_in, heads_all, True, jnp.bfloat16)
    mask = allowed.astype(jnp.float32)
    weights = (
        norm_gain[0].reshape(1, -1),
        final_gain[0].reshape(1, -1),
        input_weight[0],
        output_weight[0],
        attention_weight[0],
        mixing_weight[0],
    )

    axes = ("segment", "seq")

    def first_inputs():
        def behind(distance):
            source = (n_seg - 1) * n_seq
            pairs = [(source + q, q + distance) for q in range(n_seq) if q + distance < n_seq]
            return lax.ppermute(patches_low, axes, pairs)

        patches_low = patches.astype(jnp.bfloat16)
        return patches, behind(1), behind(2), behind(BACK + 1)

    def next_inputs(result, result_low, turn):
        src = turn * n_seq
        dst = (turn + 1) * n_seq

        def send(block, offset):
            pairs = []
            for q in range(n_seq):
                target = n_seq - 1 - q + offset
                if 0 <= target < n_seq:
                    pairs.append((src + q, dst + target))
            return lax.ppermute(block, axes, pairs)

        return (
            send(result, 0),
            send(result_low, 1),
            send(result_low, 2),
            send(result_low, BACK + 1),
        )

    inputs = first_inputs()
    out = jnp.zeros((micro, rows, width_in), jnp.float32)
    for turn in range(n_seg):
        call = first_call if turn == 0 else later_call
        keep = (segment == turn).astype(jnp.int32).reshape(1)
        out, result_low = lax.cond(
            segment == turn,
            lambda args, call=call: call(*args),
            lambda args: (args[1], jnp.zeros(args[1].shape, jnp.bfloat16)),
            (keep, out, *inputs, mask, *weights),
        )
        if turn + 1 < n_seg:
            inputs = next_inputs(out, result_low, turn)
    return out[None]


def solution(mesh):
    in_specs = (
        P(None, "seq", None),
        P(),
        P("segment", None, None),
        P("segment", None, None),
        P("segment", None, None),
        P("segment", None, None),
        P("segment", None),
        P("segment", None),
    )
    out_specs = P("segment", None, "seq", None)
    return jax.shard_map(body, mesh=mesh, in_specs=in_specs, out_specs=out_specs, check_vma=False)
```

```python
import jax
import jax.numpy as jnp
from jax import lax
from jax.experimental import pallas as pl
from jax.experimental.pallas import tpu as pltpu
from jax.sharding import PartitionSpec as P

HEAD_DIM = 128
TILE = 128
BACK = 2

CHUNK = 1024


def make_block_call(micro, rows, width_in, heads_all, mirrored, piece_dtype):
    span = (BACK + 1) * rows
    own_at = BACK * rows
    n_rows = micro * span
    n_in = (BACK + 2) * rows
    scale = HEAD_DIM ** (-0.5)
    heads = heads_all // HEAD_DIM

    def kernel(listed_ref, own_ref, back1_ref, back2_ref, edge_ref, ga_ref, gb_ref,
               embed_v, read_v, attn_hbm, mix_hbm,
               out_ref, outb_ref,
               attn_v, mix_v, sems,
               pieces_s, shifted_s, hidden_s, normed_s, q_s, kv_s, mixed_s, res_s):
        n_kv = 2 * heads_all // CHUNK
        kv_copies = [
            pltpu.make_async_copy(
                attn_hbm.at[:, heads_all + j * CHUNK:heads_all + (j + 1) * CHUNK],
                attn_v.at[:, heads_all + j * CHUNK:heads_all + (j + 1) * CHUNK],
                sems.at[2 + j],
            )
            for j in range(n_kv)
        ]
        copies = [
            pltpu.make_async_copy(attn_hbm.at[:, :heads_all], attn_v.at[:, :heads_all], sems.at[0]),
            pltpu.make_async_copy(mix_hbm, mix_v, sems.at[1]),
        ]
        for copy in kv_copies:
            copy.start()
        for copy in copies:
            copy.start()
        before = lax.broadcasted_iota(jnp.int32, (span, n_in), 0) + (rows - 1)
        column = lax.broadcasted_iota(jnp.int32, (span, n_in), 1)
        if mirrored:
            source = ((before >> 7) << 7) + (rows - 1) - (before & (rows - 1))
        else:
            source = before
        select = (column == source).astype(jnp.bfloat16)
        for m in range(micro):
            pieces_s[0:rows, :] = edge_ref[m].astype(jnp.bfloat16)
            pieces_s[rows:2 * rows, :] = back2_ref[m].astype(jnp.bfloat16)
            pieces_s[2 * rows:3 * rows, :] = back1_ref[m].astype(jnp.bfloat16)
            pieces_s[3 * rows:4 * rows, :] = own_ref[m].astype(jnp.bfloat16)
            shifted_s[m * span:(m + 1) * span, :] = jnp.dot(
                select, pieces_s[...], preferred_element_type=jnp.float32
            ).astype(jnp.bfloat16)
        hidden = jnp.dot(shifted_s[...], embed_v[...], preferred_element_type=jnp.float32)
        hidden_s[...] = hidden
        square = jnp.mean(hidden * hidden, axis=-1, keepdims=True)
        normed_s[...] = (hidden * lax.rsqrt(square + 1e-06) * ga_ref[...]).astype(jnp.bfloat16)
        for j in range(n_kv):
            kv_copies[j].wait()
            kv_s[:, j * CHUNK:(j + 1) * CHUNK] = jnp.dot(
                normed_s[...], attn_v[:, heads_all + j * CHUNK:heads_all + (j + 1) * CHUNK],
                preferred_element_type=jnp.float32,
            ).astype(jnp.bfloat16)
        copies[0].wait()

        def q_step(j, carry):
            cols = pl.ds(pl.multiple_of(j * CHUNK, CHUNK), CHUNK)
            for m in range(micro):
                q_s[m * rows:(m + 1) * rows, cols] = jnp.dot(
                    normed_s[m * span + own_at:(m + 1) * span, :], attn_v[:, cols],
                    preferred_element_type=jnp.float32,
                ).astype(jnp.bfloat16)
            return carry

        lax.fori_loop(0, heads_all // CHUNK, q_step, 0)

        query = lax.broadcasted_iota(jnp.int32, (rows, span), 0)
        key = lax.broadcasted_iota(jnp.int32, (rows, span), 1)
        tile_ok = jnp.where(
            key < rows, listed_ref[0], jnp.where(key < 2 * rows, listed_ref[1], listed_ref[2])
        )
        allowed = (tile_ok > 0) & (key <= query + own_at)
        for m in range(micro):
            q3 = jnp.stack([q_s[m * rows:(m + 1) * rows, h * HEAD_DIM:(h + 1) * HEAD_DIM] for h in range(heads)])
            k3 = jnp.stack([kv_s[m * span:(m + 1) * span, h * HEAD_DIM:(h + 1) * HEAD_DIM] for h in range(heads)])
            v3 = jnp.stack([
                kv_s[m * span:(m + 1) * span, heads_all + h * HEAD_DIM:heads_all + (h + 1) * HEAD_DIM]
                for h in range(heads)
            ])
            scores = jnp.einsum("hqd,hkd->hqk", q3, k3, preferred_element_type=jnp.float32) * scale
            scores = jnp.where(allowed[None], scores, -jnp.inf)
            top = jnp.max(scores, axis=-1, keepdims=True)
            expo = jnp.exp(scores - top)
            total = jnp.sum(expo, axis=-1, keepdims=True)
            mixed = jnp.einsum(
                "hqk,hkd->hqd", expo.astype(jnp.bfloat16), v3, preferred_element_type=jnp.float32
            ) / total
            for h in range(heads):
                mixed_s[m * rows:(m + 1) * rows, h * HEAD_DIM:(h + 1) * HEAD_DIM] = mixed[h].astype(jnp.bfloat16)

        copies[1].wait()
        for m in range(micro):
            res_s[m * rows:(m + 1) * rows, :] = hidden_s[m * span + own_at:(m + 1) * span, :] + jnp.dot(
                mixed_s[m * rows:(m + 1) * rows, :], mix_v[...], preferred_element_type=jnp.float32
            )
        residual = res_s[...]
        square = jnp.mean(residual * residual, axis=-1, keepdims=True)
        final_normed = (residual * lax.rsqrt(square + 1e-06) * gb_ref[...]).astype(jnp.bfloat16)
        raw = jnp.dot(final_normed, read_v[...], preferred_element_type=jnp.float32)
        shift_mean = raw[:, :width_in]
        log_scale = 0.5 * jnp.tanh(raw[:, width_in:])
        if mirrored:
            i = lax.broadcasted_iota(jnp.int32, (rows, rows), 0)
            c = lax.broadcasted_iota(jnp.int32, (rows, rows), 1)
            flip = (c == (rows - 1) - i).astype(jnp.bfloat16)
        for m in range(micro):
            own = own_ref[m]
            if mirrored:
                high = own.astype(jnp.bfloat16)
                rest = own - high.astype(jnp.float32)
                middle = rest.astype(jnp.bfloat16)
                low = (rest - middle.astype(jnp.float32)).astype(jnp.bfloat16)
                parts = [jnp.dot(flip, part, preferred_element_type=jnp.float32) for part in (high, middle, low)]
                own = (parts[0] + parts[1]) + parts[2]
            rows_m = slice(m * rows, (m + 1) * rows)
            result = (own - shift_mean[rows_m]) * jnp.exp(-log_scale[rows_m])
            out_ref[m] = result
            outb_ref[m] = result.astype(jnp.bfloat16)

    width = heads_all
    flops = 2 * n_rows * (width_in * width + width * 2 * heads_all)
    flops += 2 * micro * rows * (width * heads_all + 2 * heads * span * HEAD_DIM + heads_all * width + width * 2 * width_in)
    weight_bytes = 2 * (width_in * width + width * 3 * heads_all + heads_all * width + width * 2 * width_in)
    vmem = pltpu.VMEM
    call = pl.pallas_call(
        kernel,
        out_shape=(
            jax.ShapeDtypeStruct((micro, rows, width_in), jnp.float32),
            jax.ShapeDtypeStruct((micro, rows, width_in), jnp.bfloat16),
        ),
        in_specs=[pl.BlockSpec(memory_space=pltpu.SMEM)] + [pl.BlockSpec(memory_space=vmem)] * 8
        + [pl.BlockSpec(memory_space=pl.ANY)] * 2,
        out_specs=(pl.BlockSpec(memory_space=vmem), pl.BlockSpec(memory_space=vmem)),
        scratch_shapes=[
            vmem((width, 3 * heads_all), jnp.bfloat16),
            vmem((heads_all, width), jnp.bfloat16),
            pltpu.SemaphoreType.DMA((2 + 2 * heads_all // CHUNK,)),
            vmem((n_in, width_in), jnp.bfloat16),
            vmem((n_rows, width_in), jnp.bfloat16),
            vmem((n_rows, width), jnp.float32),
            vmem((n_rows, width), jnp.bfloat16),
            vmem((micro * rows, heads_all), jnp.bfloat16),
            vmem((n_rows, 2 * heads_all), jnp.bfloat16),
            vmem((micro * rows, heads_all), jnp.bfloat16),
            vmem((micro * rows, width), jnp.float32),
        ],
        compiler_params=pltpu.CompilerParams(vmem_limit_bytes=56 * 1024 * 1024),
        cost_estimate=pl.CostEstimate(
            flops=flops,
            bytes_accessed=weight_bytes + n_rows * width_in * 2 + 2 * micro * rows * width_in * 4,
            transcendentals=micro * heads * rows * span + micro * rows * 2 * width_in,
        ),
    )
    return call


def rms_scaled(values, gain):
    return values * lax.rsqrt(jnp.mean(values * values, axis=-1, keepdims=True) + 1e-06) * gain


def body(
    patches,
    tile_list,
    input_weight,
    attention_weight,
    mixing_weight,
    output_weight,
    norm_gain,
    final_gain,
):
    micro, rows, width_in = patches.shape
    assert rows == TILE
    heads_all = mixing_weight.shape[1]
    head_count = heads_all // HEAD_DIM
    segment = lax.axis_index("segment")
    place = lax.axis_index("seq")
    n_seq = lax.axis_size("seq")
    n_seg = lax.axis_size("segment")
    tiles_all = tile_list.shape[0]
    span = (BACK + 1) * rows

    window_tiles = place - BACK + jnp.arange(BACK + 1, dtype=jnp.int32)
    my_list = lax.dynamic_index_in_dim(tile_list, place, 0, keepdims=False)
    listed = jnp.any(my_list[:, None] == window_tiles[None, :], axis=0) & (window_tiles >= 0)
    listed = listed.astype(jnp.int32)

    first_call = make_block_call(micro, rows, width_in, heads_all, False, jnp.bfloat16)
    later_call = make_block_call(micro, rows, width_in, heads_all, True, jnp.bfloat16)
    weights = (
        norm_gain[0].reshape(1, -1),
        final_gain[0].reshape(1, -1),
        input_weight[0],
        output_weight[0],
        attention_weight[0],
        mixing_weight[0],
    )

    axes = ("segment", "seq")

    def first_inputs():
        def behind(distance):
            source = (n_seg - 1) * n_seq
            pairs = [(source + q, q + distance) for q in range(n_seq) if q + distance < n_seq]
            return lax.ppermute(patches_low, axes, pairs)

        patches_low = patches.astype(jnp.bfloat16)
        return patches, behind(1), behind(2), behind(BACK + 1)

    def next_inputs(result, result_low, turn):
        src = turn * n_seq
        dst = (turn + 1) * n_seq

        def send(block, offset):
            pairs = []
            for q in range(n_seq):
                target = n_seq - 1 - q + offset
                if 0 <= target < n_seq:
                    pairs.append((src + q, dst + target))
            return lax.ppermute(block, axes, pairs)

        return (
            send(result, 0),
            send(result_low, 1),
            send(result_low, 2),
            send(result_low, BACK + 1),
        )

    inputs = first_inputs()
    out = jnp.zeros((micro, rows, width_in), jnp.float32)
    for turn in range(n_seg):
        call = first_call if turn == 0 else later_call
        out, result_low = lax.cond(
            segment == turn,
            lambda args, call=call: call(*args[1:]),
            lambda args: (args[0], jnp.zeros(args[0].shape, jnp.bfloat16)),
            (out, listed, *inputs, *weights),
        )
        if turn + 1 < n_seg:
            inputs = next_inputs(out, result_low, turn)
    return out[None]


def solution(mesh):
    in_specs = (
        P(None, "seq", None),
        P(),
        P("segment", None, None),
        P("segment", None, None),
        P("segment", None, None),
        P("segment", None, None),
        P("segment", None),
        P("segment", None),
    )
    out_specs = P("segment", None, "seq", None)
    return jax.shard_map(body, mesh=mesh, in_specs=in_specs, out_specs=out_specs, check_vma=False)
```

```python
import jax
import jax.numpy as jnp
from jax import lax
from jax.experimental import pallas as pl
from jax.experimental.pallas import tpu as pltpu
from jax.sharding import PartitionSpec as P

HEAD_DIM = 128
TILE = 128
BACK = 2

CHUNK = 1024


def make_block_call(micro, rows, width_in, heads_all, mirrored, piece_dtype):
    span = (BACK + 1) * rows
    own_at = BACK * rows
    n_rows = micro * span
    n_in = (BACK + 2) * rows
    scale = HEAD_DIM ** (-0.5)
    heads = heads_all // HEAD_DIM

    def kernel(listed_ref, own_ref, back1_ref, back2_ref, edge_ref, ga_ref, gb_ref,
               embed_v, read_v, attn_hbm, mix_hbm,
               out_ref, outb_ref,
               attn_v, mix_v, sems,
               pieces_s, shifted_s, hidden_s, normed_s, q_s, kv_s, mixed_s, res_s):
        n_kv = 2 * heads_all // CHUNK
        kv_copies = [
            pltpu.make_async_copy(
                attn_hbm.at[:, heads_all + j * CHUNK:heads_all + (j + 1) * CHUNK],
                attn_v.at[:, heads_all + j * CHUNK:heads_all + (j + 1) * CHUNK],
                sems.at[2 + j],
            )
            for j in range(n_kv)
        ]
        copies = [
            pltpu.make_async_copy(attn_hbm.at[:, :heads_all], attn_v.at[:, :heads_all], sems.at[0]),
            pltpu.make_async_copy(mix_hbm, mix_v, sems.at[1]),
        ]
        for copy in kv_copies:
            copy.start()
        for copy in copies:
            copy.start()
        before = lax.broadcasted_iota(jnp.int32, (span, n_in), 0) + (rows - 1)
        column = lax.broadcasted_iota(jnp.int32, (span, n_in), 1)
        if mirrored:
            source = ((before >> 7) << 7) + (rows - 1) - (before & (rows - 1))
        else:
            source = before
        select = (column == source).astype(jnp.bfloat16)
        for m in range(micro):
            pieces_s[0:rows, :] = edge_ref[m].astype(jnp.bfloat16)
            pieces_s[rows:2 * rows, :] = back2_ref[m].astype(jnp.bfloat16)
            pieces_s[2 * rows:3 * rows, :] = back1_ref[m].astype(jnp.bfloat16)
            pieces_s[3 * rows:4 * rows, :] = own_ref[m].astype(jnp.bfloat16)
            shifted_s[m * span:(m + 1) * span, :] = jnp.dot(
                select, pieces_s[...], preferred_element_type=jnp.float32
            ).astype(jnp.bfloat16)
        hidden = jnp.dot(shifted_s[...], embed_v[...], preferred_element_type=jnp.float32)
        hidden_s[...] = hidden
        square = jnp.mean(hidden * hidden, axis=-1, keepdims=True)
        normed_s[...] = (hidden * lax.rsqrt(square + 1e-06) * ga_ref[...]).astype(jnp.bfloat16)
        for j in range(n_kv):
            kv_copies[j].wait()
            kv_s[:, j * CHUNK:(j + 1) * CHUNK] = jnp.dot(
                normed_s[...], attn_v[:, heads_all + j * CHUNK:heads_all + (j + 1) * CHUNK],
                preferred_element_type=jnp.float32,
            ).astype(jnp.bfloat16)
        copies[0].wait()

        def q_step(j, carry):
            cols = pl.ds(pl.multiple_of(j * CHUNK, CHUNK), CHUNK)
            for m in range(micro):
                q_s[m * rows:(m + 1) * rows, cols] = jnp.dot(
                    normed_s[m * span + own_at:(m + 1) * span, :], attn_v[:, cols],
                    preferred_element_type=jnp.float32,
                ).astype(jnp.bfloat16)
            return carry

        lax.fori_loop(0, heads_all // CHUNK, q_step, 0)

        query = lax.broadcasted_iota(jnp.int32, (rows, span), 0)
        key = lax.broadcasted_iota(jnp.int32, (rows, span), 1)
        tile_ok = jnp.where(
            key < rows, listed_ref[0], jnp.where(key < 2 * rows, listed_ref[1], listed_ref[2])
        )
        allowed = (tile_ok > 0) & (key <= query + own_at)
        for m in range(micro):
            q3 = jnp.stack([q_s[m * rows:(m + 1) * rows, h * HEAD_DIM:(h + 1) * HEAD_DIM] for h in range(heads)])
            k3 = jnp.stack([kv_s[m * span:(m + 1) * span, h * HEAD_DIM:(h + 1) * HEAD_DIM] for h in range(heads)])
            v3 = jnp.stack([
                kv_s[m * span:(m + 1) * span, heads_all + h * HEAD_DIM:heads_all + (h + 1) * HEAD_DIM]
                for h in range(heads)
            ])
            scores = jnp.einsum("hqd,hkd->hqk", q3, k3, preferred_element_type=jnp.float32) * scale
            scores = jnp.where(allowed[None], scores, -jnp.inf)
            top = jnp.max(scores, axis=-1, keepdims=True)
            expo = jnp.exp(scores - top)
            total = jnp.sum(expo, axis=-1, keepdims=True)
            mixed = jnp.einsum(
                "hqk,hkd->hqd", expo.astype(jnp.bfloat16), v3, preferred_element_type=jnp.float32
            ) / total
            for h in range(heads):
                mixed_s[m * rows:(m + 1) * rows, h * HEAD_DIM:(h + 1) * HEAD_DIM] = mixed[h].astype(jnp.bfloat16)

        copies[1].wait()
        for m in range(micro):
            res_s[m * rows:(m + 1) * rows, :] = hidden_s[m * span + own_at:(m + 1) * span, :] + jnp.dot(
                mixed_s[m * rows:(m + 1) * rows, :], mix_v[...], preferred_element_type=jnp.float32
            )
        residual = res_s[...]
        square = jnp.mean(residual * residual, axis=-1, keepdims=True)
        final_normed = (residual * lax.rsqrt(square + 1e-06) * gb_ref[...]).astype(jnp.bfloat16)
        raw = jnp.dot(final_normed, read_v[...], preferred_element_type=jnp.float32)
        shift_mean = raw[:, :width_in]
        log_scale = 0.5 * jnp.tanh(raw[:, width_in:])
        if mirrored:
            i = lax.broadcasted_iota(jnp.int32, (rows, rows), 0)
            c = lax.broadcasted_iota(jnp.int32, (rows, rows), 1)
            flip = (c == (rows - 1) - i).astype(jnp.bfloat16)
        for m in range(micro):
            own = own_ref[m]
            if mirrored:
                high = own.astype(jnp.bfloat16)
                rest = own - high.astype(jnp.float32)
                middle = rest.astype(jnp.bfloat16)
                low = (rest - middle.astype(jnp.float32)).astype(jnp.bfloat16)
                parts = [jnp.dot(flip, part, preferred_element_type=jnp.float32) for part in (high, middle, low)]
                own = (parts[0] + parts[1]) + parts[2]
            rows_m = slice(m * rows, (m + 1) * rows)
            result = (own - shift_mean[rows_m]) * jnp.exp(-log_scale[rows_m])
            out_ref[m] = result
            outb_ref[m] = result.astype(jnp.bfloat16)

    width = heads_all
    flops = 2 * n_rows * (width_in * width + width * 2 * heads_all)
    flops += 2 * micro * rows * (width * heads_all + 2 * heads * span * HEAD_DIM + heads_all * width + width * 2 * width_in)
    weight_bytes = 2 * (width_in * width + width * 3 * heads_all + heads_all * width + width * 2 * width_in)
    vmem = pltpu.VMEM
    call = pl.pallas_call(
        kernel,
        out_shape=(
            jax.ShapeDtypeStruct((micro, rows, width_in), jnp.float32),
            jax.ShapeDtypeStruct((micro, rows, width_in), jnp.bfloat16),
        ),
        in_specs=[pl.BlockSpec(memory_space=pltpu.SMEM)] + [pl.BlockSpec(memory_space=vmem)] * 8
        + [pl.BlockSpec(memory_space=pl.ANY)] * 2,
        out_specs=(pl.BlockSpec(memory_space=vmem), pl.BlockSpec(memory_space=vmem)),
        scratch_shapes=[
            vmem((width, 3 * heads_all), jnp.bfloat16),
            vmem((heads_all, width), jnp.bfloat16),
            pltpu.SemaphoreType.DMA((2 + 2 * heads_all // CHUNK,)),
            vmem((n_in, width_in), jnp.bfloat16),
            vmem((n_rows, width_in), jnp.bfloat16),
            vmem((n_rows, width), jnp.float32),
            vmem((n_rows, width), jnp.bfloat16),
            vmem((micro * rows, heads_all), jnp.bfloat16),
            vmem((n_rows, 2 * heads_all), jnp.bfloat16),
            vmem((micro * rows, heads_all), jnp.bfloat16),
            vmem((micro * rows, width), jnp.float32),
        ],
        compiler_params=pltpu.CompilerParams(vmem_limit_bytes=56 * 1024 * 1024),
        cost_estimate=pl.CostEstimate(
            flops=flops,
            bytes_accessed=weight_bytes + n_rows * width_in * 2 + 2 * micro * rows * width_in * 4,
            transcendentals=micro * heads * rows * span + micro * rows * 2 * width_in,
        ),
    )
    return call


def rms_scaled(values, gain):
    return values * lax.rsqrt(jnp.mean(values * values, axis=-1, keepdims=True) + 1e-06) * gain


def body(
    patches,
    tile_list,
    input_weight,
    attention_weight,
    mixing_weight,
    output_weight,
    norm_gain,
    final_gain,
):
    micro, rows, width_in = patches.shape
    assert rows == TILE
    heads_all = mixing_weight.shape[1]
    head_count = heads_all // HEAD_DIM
    segment = lax.axis_index("segment")
    place = lax.axis_index("seq")
    n_seq = lax.axis_size("seq")
    n_seg = lax.axis_size("segment")
    tiles_all = tile_list.shape[0]
    span = (BACK + 1) * rows

    window_tiles = place - BACK + jnp.arange(BACK + 1, dtype=jnp.int32)
    my_list = lax.dynamic_index_in_dim(tile_list, place, 0, keepdims=False)
    listed = jnp.any(my_list[:, None] == window_tiles[None, :], axis=0) & (window_tiles >= 0)
    listed = listed.astype(jnp.int32)

    first_call = make_block_call(micro, rows, width_in, heads_all, False, jnp.float32)
    later_call = make_block_call(micro, rows, width_in, heads_all, True, jnp.bfloat16)
    weights = (
        norm_gain[0].reshape(1, -1),
        final_gain[0].reshape(1, -1),
        input_weight[0],
        output_weight[0],
        attention_weight[0],
        mixing_weight[0],
    )

    axes = ("segment", "seq")

    def first_inputs():
        def behind(distance):
            source = (n_seg - 1) * n_seq
            pairs = [(source + q, q + distance) for q in range(n_seq) if q + distance < n_seq]
            return lax.ppermute(patches, axes, pairs)

        return patches, behind(1), behind(2), behind(BACK + 1)

    def next_inputs(result, result_low, turn):
        src = turn * n_seq
        dst = (turn + 1) * n_seq

        def send(block, offset):
            pairs = []
            for q in range(n_seq):
                target = n_seq - 1 - q + offset
                if 0 <= target < n_seq:
                    pairs.append((src + q, dst + target))
            return lax.ppermute(block, axes, pairs)

        return (
            send(result, 0),
            send(result_low, 1),
            send(result_low, 2),
            send(result_low, BACK + 1),
        )

    inputs = first_inputs()
    out = jnp.zeros((micro, rows, width_in), jnp.float32)
    for turn in range(n_seg):
        call = first_call if turn == 0 else later_call
        out, result_low = lax.cond(
            segment == turn,
            lambda args, call=call: call(*args[1:]),
            lambda args: (args[0], jnp.zeros(args[0].shape, jnp.bfloat16)),
            (out, listed, *inputs, *weights),
        )
        if turn + 1 < n_seg:
            inputs = next_inputs(out, result_low, turn)
    return out[None]


def solution(mesh):
    in_specs = (
        P(None, "seq", None),
        P(),
        P("segment", None, None),
        P("segment", None, None),
        P("segment", None, None),
        P("segment", None, None),
        P("segment", None),
        P("segment", None),
    )
    out_specs = P("segment", None, "seq", None)
    return jax.shard_map(body, mesh=mesh, in_specs=in_specs, out_specs=out_specs, check_vma=False)
```

```python
import jax
import jax.numpy as jnp
from jax import lax
from jax.experimental import pallas as pl
from jax.experimental.pallas import tpu as pltpu
from jax.sharding import PartitionSpec as P

HEAD_DIM = 128
TILE = 128
BACK = 2

CHUNK = 1024


def make_block_call(micro, rows, width_in, heads_all, mirrored, piece_dtype):
    span = (BACK + 1) * rows
    own_at = BACK * rows
    n_rows = micro * span
    n_in = (BACK + 2) * rows
    scale = HEAD_DIM ** (-0.5)
    heads = heads_all // HEAD_DIM

    def kernel(listed_ref, own_ref, back1_ref, back2_ref, edge_ref, ga_ref, gb_ref,
               embed_v, read_v, attn_hbm, mix_hbm,
               out_ref, outb_ref,
               attn_v, mix_v, sems,
               pieces_s, shifted_s, hidden_s, normed_s, q_s, kv_s, mixed_s, res_s):
        n_kv = 2 * heads_all // CHUNK
        kv_copies = [
            pltpu.make_async_copy(
                attn_hbm.at[:, heads_all + j * CHUNK:heads_all + (j + 1) * CHUNK],
                attn_v.at[:, heads_all + j * CHUNK:heads_all + (j + 1) * CHUNK],
                sems.at[2 + j],
            )
            for j in range(n_kv)
        ]
        copies = [
            pltpu.make_async_copy(attn_hbm.at[:, :heads_all], attn_v.at[:, :heads_all], sems.at[0]),
            pltpu.make_async_copy(mix_hbm, mix_v, sems.at[1]),
        ]
        for copy in kv_copies:
            copy.start()
        for copy in copies:
            copy.start()
        before = lax.broadcasted_iota(jnp.int32, (span, n_in), 0) + (rows - 1)
        column = lax.broadcasted_iota(jnp.int32, (span, n_in), 1)
        if mirrored:
            source = ((before >> 7) << 7) + (rows - 1) - (before & (rows - 1))
        else:
            source = before
        select = (column == source).astype(jnp.bfloat16)
        for m in range(micro):
            pieces_s[0:rows, :] = edge_ref[m].astype(jnp.bfloat16)
            pieces_s[rows:2 * rows, :] = back2_ref[m].astype(jnp.bfloat16)
            pieces_s[2 * rows:3 * rows, :] = back1_ref[m].astype(jnp.bfloat16)
            pieces_s[3 * rows:4 * rows, :] = own_ref[m].astype(jnp.bfloat16)
            shifted_s[m * span:(m + 1) * span, :] = jnp.dot(
                select, pieces_s[...], preferred_element_type=jnp.float32
            ).astype(jnp.bfloat16)
        hidden = jnp.dot(shifted_s[...], embed_v[...], preferred_element_type=jnp.float32)
        hidden_s[...] = hidden
        square = jnp.mean(hidden * hidden, axis=-1, keepdims=True)
        normed_s[...] = (hidden * lax.rsqrt(square + 1e-06) * ga_ref[...]).astype(jnp.bfloat16)
        for j in range(n_kv):
            kv_copies[j].wait()
            kv_s[:, j * CHUNK:(j + 1) * CHUNK] = jnp.dot(
                normed_s[...], attn_v[:, heads_all + j * CHUNK:heads_all + (j + 1) * CHUNK],
                preferred_element_type=jnp.float32,
            ).astype(jnp.bfloat16)
        copies[0].wait()

        def q_step(j, carry):
            cols = pl.ds(pl.multiple_of(j * CHUNK, CHUNK), CHUNK)
            for m in range(micro):
                q_s[m * rows:(m + 1) * rows, cols] = jnp.dot(
                    normed_s[m * span + own_at:(m + 1) * span, :], attn_v[:, cols],
                    preferred_element_type=jnp.float32,
                ).astype(jnp.bfloat16)
            return carry

        lax.fori_loop(0, heads_all // CHUNK, q_step, 0)

        query = lax.broadcasted_iota(jnp.int32, (rows, span), 0)
        key = lax.broadcasted_iota(jnp.int32, (rows, span), 1)
        tile_ok = jnp.where(
            key < rows, listed_ref[0], jnp.where(key < 2 * rows, listed_ref[1], listed_ref[2])
        )
        allowed = (tile_ok > 0) & (key <= query + own_at)
        for m in range(micro):
            q3 = jnp.stack([q_s[m * rows:(m + 1) * rows, h * HEAD_DIM:(h + 1) * HEAD_DIM] for h in range(heads)])
            k3 = jnp.stack([kv_s[m * span:(m + 1) * span, h * HEAD_DIM:(h + 1) * HEAD_DIM] for h in range(heads)])
            v3 = jnp.stack([
                kv_s[m * span:(m + 1) * span, heads_all + h * HEAD_DIM:heads_all + (h + 1) * HEAD_DIM]
                for h in range(heads)
            ])
            scores = jnp.einsum("hqd,hkd->hqk", q3, k3, preferred_element_type=jnp.float32) * scale
            scores = jnp.where(allowed[None], scores, -jnp.inf)
            top = jnp.max(scores, axis=-1, keepdims=True)
            expo = jnp.exp(scores - top)
            total = jnp.sum(expo, axis=-1, keepdims=True)
            mixed = jnp.einsum(
                "hqk,hkd->hqd", expo.astype(jnp.bfloat16), v3, preferred_element_type=jnp.float32
            ) / total
            for h in range(heads):
                mixed_s[m * rows:(m + 1) * rows, h * HEAD_DIM:(h + 1) * HEAD_DIM] = mixed[h].astype(jnp.bfloat16)

        copies[1].wait()
        for m in range(micro):
            res_s[m * rows:(m + 1) * rows, :] = hidden_s[m * span + own_at:(m + 1) * span, :] + jnp.dot(
                mixed_s[m * rows:(m + 1) * rows, :], mix_v[...], preferred_element_type=jnp.float32
            )
        residual = res_s[...]
        square = jnp.mean(residual * residual, axis=-1, keepdims=True)
        final_normed = (residual * lax.rsqrt(square + 1e-06) * gb_ref[...]).astype(jnp.bfloat16)
        raw = jnp.dot(final_normed, read_v[...], preferred_element_type=jnp.float32)
        shift_mean = raw[:, :width_in]
        log_scale = 0.5 * jnp.tanh(raw[:, width_in:])
        if mirrored:
            i = lax.broadcasted_iota(jnp.int32, (rows, rows), 0)
            c = lax.broadcasted_iota(jnp.int32, (rows, rows), 1)
            flip = (c == (rows - 1) - i).astype(jnp.bfloat16)
        for m in range(micro):
            own = own_ref[m]
            if mirrored:
                high = own.astype(jnp.bfloat16)
                rest = own - high.astype(jnp.float32)
                middle = rest.astype(jnp.bfloat16)
                low = (rest - middle.astype(jnp.float32)).astype(jnp.bfloat16)
                parts = [jnp.dot(flip, part, preferred_element_type=jnp.float32) for part in (high, middle, low)]
                own = (parts[0] + parts[1]) + parts[2]
            rows_m = slice(m * rows, (m + 1) * rows)
            result = (own - shift_mean[rows_m]) * jnp.exp(-log_scale[rows_m])
            out_ref[m] = result
            outb_ref[m] = result.astype(jnp.bfloat16)

    width = heads_all
    flops = 2 * n_rows * (width_in * width + width * 2 * heads_all)
    flops += 2 * micro * rows * (width * heads_all + 2 * heads * span * HEAD_DIM + heads_all * width + width * 2 * width_in)
    weight_bytes = 2 * (width_in * width + width * 3 * heads_all + heads_all * width + width * 2 * width_in)
    vmem = pltpu.VMEM
    call = pl.pallas_call(
        kernel,
        out_shape=(
            jax.ShapeDtypeStruct((micro, rows, width_in), jnp.float32),
            jax.ShapeDtypeStruct((micro, rows, width_in), jnp.bfloat16),
        ),
        in_specs=[pl.BlockSpec(memory_space=pltpu.SMEM)] + [pl.BlockSpec(memory_space=vmem)] * 8
        + [pl.BlockSpec(memory_space=pl.ANY)] * 2,
        out_specs=(pl.BlockSpec(memory_space=vmem), pl.BlockSpec(memory_space=vmem)),
        scratch_shapes=[
            vmem((width, 3 * heads_all), jnp.bfloat16),
            vmem((heads_all, width), jnp.bfloat16),
            pltpu.SemaphoreType.DMA((2 + 2 * heads_all // CHUNK,)),
            vmem((n_in, width_in), jnp.bfloat16),
            vmem((n_rows, width_in), jnp.bfloat16),
            vmem((n_rows, width), jnp.float32),
            vmem((n_rows, width), jnp.bfloat16),
            vmem((micro * rows, heads_all), jnp.bfloat16),
            vmem((n_rows, 2 * heads_all), jnp.bfloat16),
            vmem((micro * rows, heads_all), jnp.bfloat16),
            vmem((micro * rows, width), jnp.float32),
        ],
        compiler_params=pltpu.CompilerParams(vmem_limit_bytes=56 * 1024 * 1024),
        cost_estimate=pl.CostEstimate(
            flops=flops,
            bytes_accessed=weight_bytes + n_rows * width_in * 2 + 2 * micro * rows * width_in * 4,
            transcendentals=micro * heads * rows * span + micro * rows * 2 * width_in,
        ),
    )
    return call


def rms_scaled(values, gain):
    return values * lax.rsqrt(jnp.mean(values * values, axis=-1, keepdims=True) + 1e-06) * gain


def body(
    patches,
    tile_list,
    input_weight,
    attention_weight,
    mixing_weight,
    output_weight,
    norm_gain,
    final_gain,
):
    micro, rows, width_in = patches.shape
    assert rows == TILE
    heads_all = mixing_weight.shape[1]
    head_count = heads_all // HEAD_DIM
    segment = lax.axis_index("segment")
    place = lax.axis_index("seq")
    n_seq = lax.axis_size("seq")
    n_seg = lax.axis_size("segment")
    tiles_all = tile_list.shape[0]
    span = (BACK + 1) * rows

    window_tiles = place - BACK + jnp.arange(BACK + 1, dtype=jnp.int32)
    my_list = lax.dynamic_index_in_dim(tile_list, place, 0, keepdims=False)
    listed = jnp.any(my_list[:, None] == window_tiles[None, :], axis=0) & (window_tiles >= 0)
    listed = listed.astype(jnp.int32)

    first_call = make_block_call(micro, rows, width_in, heads_all, False, jnp.bfloat16)
    later_call = make_block_call(micro, rows, width_in, heads_all, True, jnp.bfloat16)
    weights = (
        norm_gain[0].reshape(1, -1),
        final_gain[0].reshape(1, -1),
        input_weight[0],
        output_weight[0],
        attention_weight[0],
        mixing_weight[0],
    )

    axes = ("segment", "seq")

    def first_inputs():
        def behind(distance):
            source = n_seq
            pairs = [(source + q, q + distance) for q in range(n_seq) if q + distance < n_seq]
            return lax.ppermute(patches_low, axes, pairs)

        patches_low = patches.astype(jnp.bfloat16)
        return patches, behind(1), behind(2), behind(BACK + 1)

    def next_inputs(result, result_low, turn):
        src = turn * n_seq
        dst = (turn + 1) * n_seq

        def send(block, offset):
            pairs = []
            for q in range(n_seq):
                target = n_seq - 1 - q + offset
                if 0 <= target < n_seq:
                    pairs.append((src + q, dst + target))
            return lax.ppermute(block, axes, pairs)

        return (
            send(result, 0),
            send(result_low, 1),
            send(result_low, 2),
            send(result_low, BACK + 1),
        )

    inputs = first_inputs()
    out = jnp.zeros((micro, rows, width_in), jnp.float32)
    for turn in range(n_seg):
        call = first_call if turn == 0 else later_call
        out, result_low = lax.cond(
            segment == turn,
            lambda args, call=call: call(*args[1:]),
            lambda args: (args[0], jnp.zeros(args[0].shape, jnp.bfloat16)),
            (out, listed, *inputs, *weights),
        )
        if turn + 1 < n_seg:
            inputs = next_inputs(out, result_low, turn)
    return out[None]


def solution(mesh):
    in_specs = (
        P(None, "seq", None),
        P(),
        P("segment", None, None),
        P("segment", None, None),
        P("segment", None, None),
        P("segment", None, None),
        P("segment", None),
        P("segment", None),
    )
    out_specs = P("segment", None, "seq", None)
    return jax.shard_map(body, mesh=mesh, in_specs=in_specs, out_specs=out_specs, check_vma=False)
```

```python
import jax
import jax.numpy as jnp
from jax import lax
from jax.experimental import pallas as pl
from jax.experimental.pallas import tpu as pltpu
from jax.sharding import PartitionSpec as P

HEAD_DIM = 128
TILE = 128
BACK = 2

CHUNK = 1024


def make_block_call(micro, rows, width_in, heads_all, mirrored, piece_dtype):
    span = (BACK + 1) * rows
    own_at = BACK * rows
    n_rows = micro * span
    n_in = (BACK + 2) * rows
    scale = HEAD_DIM ** (-0.5)
    heads = heads_all // HEAD_DIM

    def kernel(listed_ref, own_ref, back1_ref, back2_ref, edge_ref, ga_ref, gb_ref,
               embed_v, read_v, attn_hbm, mix_hbm,
               out_ref, outb_ref,
               attn_v, mix_v, sems,
               pieces_s, shifted_s, hidden_s, normed_s, q_s, kv_s, mixed_s, res_s):
        n_kv = 2 * heads_all // CHUNK
        kv_copies = [
            pltpu.make_async_copy(
                attn_hbm.at[:, heads_all + j * CHUNK:heads_all + (j + 1) * CHUNK],
                attn_v.at[:, heads_all + j * CHUNK:heads_all + (j + 1) * CHUNK],
                sems.at[2 + j],
            )
            for j in range(n_kv)
        ]
        copies = [
            pltpu.make_async_copy(attn_hbm.at[:, :heads_all], attn_v.at[:, :heads_all], sems.at[0]),
            pltpu.make_async_copy(mix_hbm, mix_v, sems.at[1]),
        ]
        for copy in kv_copies:
            copy.start()
        for copy in copies:
            copy.start()
        before = lax.broadcasted_iota(jnp.int32, (span, n_in), 0) + (rows - 1)
        column = lax.broadcasted_iota(jnp.int32, (span, n_in), 1)
        if mirrored:
            source = ((before >> 7) << 7) + (rows - 1) - (before & (rows - 1))
        else:
            source = before
        select = (column == source).astype(jnp.bfloat16)
        for m in range(micro):
            pieces_s[0:rows, :] = edge_ref[m].astype(jnp.bfloat16)
            pieces_s[rows:2 * rows, :] = back2_ref[m].astype(jnp.bfloat16)
            pieces_s[2 * rows:3 * rows, :] = back1_ref[m].astype(jnp.bfloat16)
            pieces_s[3 * rows:4 * rows, :] = own_ref[m].astype(jnp.bfloat16)
            shifted_s[m * span:(m + 1) * span, :] = jnp.dot(
                select, pieces_s[...], preferred_element_type=jnp.float32
            ).astype(jnp.bfloat16)
        hidden = jnp.dot(shifted_s[...], embed_v[...], preferred_element_type=jnp.float32)
        hidden_s[...] = hidden
        square = jnp.mean(hidden * hidden, axis=-1, keepdims=True)
        normed_s[...] = (hidden * lax.rsqrt(square + 1e-06) * ga_ref[...]).astype(jnp.bfloat16)
        for j in range(n_kv):
            kv_copies[j].wait()
            kv_s[:, j * CHUNK:(j + 1) * CHUNK] = jnp.dot(
                normed_s[...], attn_v[:, heads_all + j * CHUNK:heads_all + (j + 1) * CHUNK],
                preferred_element_type=jnp.float32,
            ).astype(jnp.bfloat16)
        copies[0].wait()

        def q_step(j, carry):
            cols = pl.ds(pl.multiple_of(j * CHUNK, CHUNK), CHUNK)
            for m in range(micro):
                q_s[m * rows:(m + 1) * rows, cols] = jnp.dot(
                    normed_s[m * span + own_at:(m + 1) * span, :], attn_v[:, cols],
                    preferred_element_type=jnp.float32,
                ).astype(jnp.bfloat16)
            return carry

        lax.fori_loop(0, heads_all // CHUNK, q_step, 0)

        query = lax.broadcasted_iota(jnp.int32, (rows, span), 0)
        key = lax.broadcasted_iota(jnp.int32, (rows, span), 1)
        tile_ok = jnp.where(
            key < rows, listed_ref[0], jnp.where(key < 2 * rows, listed_ref[1], listed_ref[2])
        )
        allowed = (tile_ok > 0) & (key <= query + own_at)
        for m in range(micro):
            q3 = jnp.stack([q_s[m * rows:(m + 1) * rows, h * HEAD_DIM:(h + 1) * HEAD_DIM] for h in range(heads)])
            k3 = jnp.stack([kv_s[m * span:(m + 1) * span, h * HEAD_DIM:(h + 1) * HEAD_DIM] for h in range(heads)])
            v3 = jnp.stack([
                kv_s[m * span:(m + 1) * span, heads_all + h * HEAD_DIM:heads_all + (h + 1) * HEAD_DIM]
                for h in range(heads)
            ])
            scores = jnp.einsum("hqd,hkd->hqk", q3, k3, preferred_element_type=jnp.float32) * scale
            scores = jnp.where(allowed[None], scores, -jnp.inf)
            top = jnp.max(scores, axis=-1, keepdims=True)
            expo = jnp.exp(scores - top)
            total = jnp.sum(expo, axis=-1, keepdims=True)
            mixed = jnp.einsum(
                "hqk,hkd->hqd", expo.astype(jnp.bfloat16), v3, preferred_element_type=jnp.float32
            ) / total
            for h in range(heads):
                mixed_s[m * rows:(m + 1) * rows, h * HEAD_DIM:(h + 1) * HEAD_DIM] = mixed[h].astype(jnp.bfloat16)

        copies[1].wait()
        for m in range(micro):
            res_s[m * rows:(m + 1) * rows, :] = hidden_s[m * span + own_at:(m + 1) * span, :] + jnp.dot(
                mixed_s[m * rows:(m + 1) * rows, :], mix_v[...], preferred_element_type=jnp.float32
            )
        residual = res_s[...]
        square = jnp.mean(residual * residual, axis=-1, keepdims=True)
        final_normed = (residual * lax.rsqrt(square + 1e-06) * gb_ref[...]).astype(jnp.bfloat16)
        raw = jnp.dot(final_normed, read_v[...], preferred_element_type=jnp.float32)
        shift_mean = raw[:, :width_in]
        log_scale = 0.5 * jnp.tanh(raw[:, width_in:])
        if mirrored:
            i = lax.broadcasted_iota(jnp.int32, (rows, rows), 0)
            c = lax.broadcasted_iota(jnp.int32, (rows, rows), 1)
            flip = (c == (rows - 1) - i).astype(jnp.bfloat16)
        for m in range(micro):
            own = own_ref[m]
            if mirrored:
                high = own.astype(jnp.bfloat16)
                rest = own - high.astype(jnp.float32)
                middle = rest.astype(jnp.bfloat16)
                low = (rest - middle.astype(jnp.float32)).astype(jnp.bfloat16)
                parts = [jnp.dot(flip, part, preferred_element_type=jnp.float32) for part in (high, middle, low)]
                own = (parts[0] + parts[1]) + parts[2]
            rows_m = slice(m * rows, (m + 1) * rows)
            result = (own - shift_mean[rows_m]) * jnp.exp(-log_scale[rows_m])
            out_ref[m] = result
            outb_ref[m] = result.astype(jnp.bfloat16)

    width = heads_all
    flops = 2 * n_rows * (width_in * width + width * 2 * heads_all)
    flops += 2 * micro * rows * (width * heads_all + 2 * heads * span * HEAD_DIM + heads_all * width + width * 2 * width_in)
    weight_bytes = 2 * (width_in * width + width * 3 * heads_all + heads_all * width + width * 2 * width_in)
    vmem = pltpu.VMEM
    call = pl.pallas_call(
        kernel,
        out_shape=(
            jax.ShapeDtypeStruct((micro, rows, width_in), jnp.float32),
            jax.ShapeDtypeStruct((micro, rows, width_in), jnp.bfloat16),
        ),
        in_specs=[pl.BlockSpec(memory_space=pltpu.SMEM)] + [pl.BlockSpec(memory_space=vmem)] * 8
        + [pl.BlockSpec(memory_space=pl.ANY)] * 2,
        out_specs=(pl.BlockSpec(memory_space=vmem), pl.BlockSpec(memory_space=vmem)),
        scratch_shapes=[
            vmem((width, 3 * heads_all), jnp.bfloat16),
            vmem((heads_all, width), jnp.bfloat16),
            pltpu.SemaphoreType.DMA((2 + 2 * heads_all // CHUNK,)),
            vmem((n_in, width_in), jnp.bfloat16),
            vmem((n_rows, width_in), jnp.bfloat16),
            vmem((n_rows, width), jnp.float32),
            vmem((n_rows, width), jnp.bfloat16),
            vmem((micro * rows, heads_all), jnp.bfloat16),
            vmem((n_rows, 2 * heads_all), jnp.bfloat16),
            vmem((micro * rows, heads_all), jnp.bfloat16),
            vmem((micro * rows, width), jnp.float32),
        ],
        compiler_params=pltpu.CompilerParams(vmem_limit_bytes=56 * 1024 * 1024),
        cost_estimate=pl.CostEstimate(
            flops=flops,
            bytes_accessed=weight_bytes + n_rows * width_in * 2 + 2 * micro * rows * width_in * 4,
            transcendentals=micro * heads * rows * span + micro * rows * 2 * width_in,
        ),
    )
    return call


def rms_scaled(values, gain):
    return values * lax.rsqrt(jnp.mean(values * values, axis=-1, keepdims=True) + 1e-06) * gain


def body(
    patches,
    tile_list,
    input_weight,
    attention_weight,
    mixing_weight,
    output_weight,
    norm_gain,
    final_gain,
):
    micro, rows, width_in = patches.shape
    assert rows == TILE
    heads_all = mixing_weight.shape[1]
    head_count = heads_all // HEAD_DIM
    segment = lax.axis_index("segment")
    place = lax.axis_index("seq")
    n_seq = lax.axis_size("seq")
    n_seg = lax.axis_size("segment")
    tiles_all = tile_list.shape[0]
    span = (BACK + 1) * rows

    window_tiles = place - BACK + jnp.arange(BACK + 1, dtype=jnp.int32)
    my_list = lax.dynamic_index_in_dim(tile_list, place, 0, keepdims=False)
    listed = jnp.any(my_list[:, None] == window_tiles[None, :], axis=0) & (window_tiles >= 0)
    listed = listed.astype(jnp.int32)

    first_call = make_block_call(micro, rows, width_in, heads_all, False, jnp.float32)
    later_call = make_block_call(micro, rows, width_in, heads_all, True, jnp.bfloat16)
    weights = (
        norm_gain[0].reshape(1, -1),
        final_gain[0].reshape(1, -1),
        input_weight[0],
        output_weight[0],
        attention_weight[0],
        mixing_weight[0],
    )

    axes = ("segment", "seq")

    def first_inputs():
        def behind(distance):
            source = n_seq
            pairs = [(source + q, q + distance) for q in range(n_seq) if q + distance < n_seq]
            return lax.ppermute(patches, axes, pairs)

        return patches, behind(1), behind(2), behind(BACK + 1)

    def next_inputs(result, result_low, turn):
        src = turn * n_seq
        dst = (turn + 1) * n_seq

        def send(block, offset):
            pairs = []
            for q in range(n_seq):
                target = n_seq - 1 - q + offset
                if 0 <= target < n_seq:
                    pairs.append((src + q, dst + target))
            return lax.ppermute(block, axes, pairs)

        return (
            send(result, 0),
            send(result_low, 1),
            send(result_low, 2),
            send(result_low, BACK + 1),
        )

    inputs = first_inputs()
    out = jnp.zeros((micro, rows, width_in), jnp.float32)
    for turn in range(n_seg):
        call = first_call if turn == 0 else later_call
        out, result_low = lax.cond(
            segment == turn,
            lambda args, call=call: call(*args[1:]),
            lambda args: (args[0], jnp.zeros(args[0].shape, jnp.bfloat16)),
            (out, listed, *inputs, *weights),
        )
        if turn + 1 < n_seg:
            inputs = next_inputs(out, result_low, turn)
    return out[None]


def solution(mesh):
    in_specs = (
        P(None, "seq", None),
        P(),
        P("segment", None, None),
        P("segment", None, None),
        P("segment", None, None),
        P("segment", None, None),
        P("segment", None),
        P("segment", None),
    )
    out_specs = P("segment", None, "seq", None)
    return jax.shard_map(body, mesh=mesh, in_specs=in_specs, out_specs=out_specs, check_vma=False)
```
